32 devices in a mesh: gx: 8 (over y, x, core), gy: 4 (over z).
Axes of the slice: x: 2, y: 2, z: 4, core: 2. Of those that a mesh axis runs over, the one named last changes fastest.
Arguments:
- prior_gas_warmth: float32 [128, 128, 512], P(None, 'gx', 'gy'), may hold values from -8 to 8
- fire_power_output: float32 [128, 128, 512], P(None, 'gx', 'gy'), may hold values from -6 to 6
- measured_warmth: float32 [32768], P(('gx', 'gy')), may hold values from -8 to 8
- reading_noise_spread: float32 [32768], P(('gx', 'gy')), may hold values from 1.15 to 6
- reading_local_location: int32 [32768], P(('gx', 'gy')), may hold values from 0 to 2047
Outputs:
- temperature_analysis: float32 [128, 128, 512], P(None, 'gx', 'gy')
- heat_analysis: float32 [128, 128, 512], P(None, 'gx', 'gy')
The draws below stay inside these ranges and needn't reach their ends.
All inputs are finite; a program needn't handle non-finite values.
Results may differ from the reference program's by a relative error of at most 0.0003.
Values sent between devices are 32-bit elements; how exact they have to be, the bound alone decides.
No kernel may reach another device: no remote copies, remote signals or barrier semaphores. Data moves between devices by JAX's collectives and lax.ppermute only.
A program may use at most 64 MiB of HBM per device.

```python
import math
import jax
import jax.numpy as jnp
from jax import lax

M = 128
CX = 16
CY = 128
OBS_DEV = 1024
NX = 128
NY = 512
READINGS_TOTAL = 32768
N_GY = 4


mode_count = 16


def draw_reading_noise_spread(key, part):
    position = jnp.arange(READINGS_TOTAL, dtype=jnp.float32) / max(READINGS_TOTAL - 1, 1)
    falling = jnp.exp(-0.5 * math.log(3.0) * position)
    base = jnp.exp(jax.random.uniform(key, (READINGS_TOTAL,), jnp.float32, math.log(2.0), math.log(6.0)))
    return base * falling


def draw_prior_gas_warmth(key, part):
    key_noise = jax.random.fold_in(key, 11)
    key_coef = jax.random.fold_in(key, 12)
    key_mode = jax.random.fold_in(key, 13)
    field = jnp.clip(jax.random.normal(key_noise, (M, NX, NY), jnp.float32), -3.0, 3.0)
    coefficient = 0.6 * jnp.clip(jax.random.normal(key_coef, (M, mode_count), jnp.float32), -2.5, 2.5)
    for index in range(mode_count):
        mode_field = jnp.clip(jax.random.normal(jax.random.fold_in(key_mode, index), (NX, NY), jnp.float32), -3.0, 3.0)
        field = field + coefficient[:, index][:, None, None] * mode_field[None, :, :]
    return jnp.clip(field, -8.0, 8.0)


def set_ends(result, own_key, low, largest):
    longest = result.shape.index(max(result.shape))
    spots = []
    for shift in (0, 1):
        where = [jax.random.randint(jax.random.fold_in(own_key, axis), (), 0, length) for axis, length in enumerate(result.shape)]
        where[longest] = (where[longest] + shift) % result.shape[longest]
        spots.append(tuple(where))
    return result.at[spots[0]].set(low).at[spots[1]].set(largest)


def levels(rng, shape, cuts, least, high):
    gain, own = 1.0, jax.random.fold_in(rng, 6)
    for dim, parts in cuts:
        draws = jnp.exp(jax.random.uniform(jax.random.fold_in(own, dim), (parts,), jnp.float32, least / len(cuts), high / len(cuts)))
        gain = gain * jnp.repeat(draws, shape[dim] // parts).reshape([-1 if axis == dim else 1 for axis in range(len(shape))])
    return gain


def bell_draw(key, shape, scale, most, split=(), kind=jnp.bfloat16):
    drawn = scale * jax.random.normal(key, shape, jnp.float32)
    if split:
        drawn = drawn * levels(key, shape, split, -0.22, 0.18)
    return jnp.clip(drawn, -most, most).astype(kind)


def setup_inputs(seed: int = 0) -> dict:
    streams_of = jax.random.split(jax.random.key(seed), 6)
    prior_gas_warmth = draw_prior_gas_warmth(jax.random.fold_in(streams_of[5], 71), 0)
    fire_power_output = bell_draw(streams_of[1], (M, NX, NY), 1.0, 6.0, ((1, 8), (2, 4)), jnp.float32)
    measured_warmth = bell_draw(streams_of[2], (READINGS_TOTAL,), 2.0, 8.0, ((0, 32),), jnp.float32)
    reading_noise_spread = draw_reading_noise_spread(jax.random.fold_in(streams_of[5], 71), 0)
    reading_local_location = set_ends(jax.random.randint(streams_of[4], (READINGS_TOTAL,), 0, CX * CY), jax.random.fold_in(streams_of[4], 1), 0, (CX * CY) - 1).astype(jnp.int32)
    return {"prior_gas_warmth": prior_gas_warmth, "fire_power_output": fire_power_output, "measured_warmth": measured_warmth, "reading_noise_spread": reading_noise_spread, "reading_local_location": reading_local_location}


diffusion = 0.2
heating = 0.5

def propagate_model(padded_field, source_term):
    laplacian = padded_field[:, 2:, 1:-1] + padded_field[:, :-2, 1:-1] + padded_field[:, 1:-1, 2:] + padded_field[:, 1:-1, :-2] - 4.0 * padded_field[:, 1:-1, 1:-1]
    return padded_field[:, 1:-1, 1:-1] + diffusion * laplacian + heating * source_term

def reference(prior_gas_warmth, fire_power_output, measured_warmth, reading_noise_spread, reading_local_location):
    predicted_vector = prior_gas_warmth
    for section in range(2):
        predicted_vector = propagate_model(jnp.pad(predicted_vector, ((0, 0), (1, 1), (1, 1))), fire_power_output)
    average_gas_warmth = lax.optimization_barrier(jnp.mean(predicted_vector, axis=0))
    mean_heat = lax.optimization_barrier(jnp.mean(fire_power_output, axis=0))
    sample_deviation_matrix = predicted_vector - average_gas_warmth
    heat_anomaly = fire_power_output - mean_heat
    tile_of = jnp.arange(READINGS_TOTAL, dtype=jnp.int32) // OBS_DEV
    horizontal_line_position = tile_of // N_GY * CX + reading_local_location // CY
    vertical_line_position = tile_of % N_GY * CY + reading_local_location % CY
    picked = sample_deviation_matrix[:, horizontal_line_position, vertical_line_position]
    coefficient_line = 1.0 / (reading_noise_spread * math.sqrt(M - 1))
    s_matrix = picked * coefficient_line
    measurement_residual = (measured_warmth - average_gas_warmth[horizontal_line_position, vertical_line_position]) * coefficient_line
    identity = jnp.eye(M, dtype=jnp.float32)
    gram = jnp.dot(s_matrix, s_matrix.T, precision=lax.Precision.HIGHEST) + identity
    projected = jnp.dot(s_matrix, measurement_residual, precision=lax.Precision.HIGHEST)
    lower = jnp.linalg.cholesky(gram)
    mean_weights = jax.scipy.linalg.cho_solve((lower, True), projected)
    inverse_factor = jax.scipy.linalg.solve_triangular(lower, identity, lower=True, trans=1)
    combination_matrix = mean_weights[:, None] + inverse_factor
    updated_warmth = average_gas_warmth + jnp.tensordot(combination_matrix, sample_deviation_matrix, axes=((0,), (0,)), precision=lax.Precision.HIGHEST)
    heat_out = mean_heat + jnp.tensordot(combination_matrix, heat_anomaly, axes=((0,), (0,)), precision=lax.Precision.HIGHEST)
    return (updated_warmth, heat_out)
```

```python
import math

import jax
import jax.numpy as jnp
from jax import lax
from jax.sharding import PartitionSpec as P

diffusion = 0.2
heating = 0.5


def with_halo(block, sides, width):
    for axis, dim in sides:
        count = lax.axis_size(axis)
        forward = [(i, i + 1) for i in range(count - 1)]
        backward = [(target, source) for source, target in forward]
        low = lax.ppermute(
            lax.slice_in_dim(block, block.shape[dim] - width, None, axis=dim), axis, forward
        )
        high = lax.ppermute(lax.slice_in_dim(block, 0, width, axis=dim), axis, backward)
        block = jnp.concatenate([low, block, high], axis=dim)
    return block


def butterfly_sum(value, axes):
    for axis in axes:
        count = lax.axis_size(axis)
        if count & (count - 1):
            value = lax.psum(value, axis)
            continue
        stride = 1
        while stride < count:
            pairs = [(i, i ^ stride) for i in range(count)]
            value = value + lax.ppermute(value, axis, pairs)
            stride *= 2
    return value


def propagate_model(padded_field, source_term):
    laplacian = (
        padded_field[:, 2:, 1:-1]
        + padded_field[:, :-2, 1:-1]
        + padded_field[:, 1:-1, 2:]
        + padded_field[:, 1:-1, :-2]
        - 4.0 * padded_field[:, 1:-1, 1:-1]
    )
    return padded_field[:, 1:-1, 1:-1] + diffusion * laplacian + heating * source_term


def shards(
    prior_gas_warmth,
    fire_power_output,
    measured_warmth,
    reading_noise_spread,
    reading_local_location,
):
    sample_number, block_height_number, block_width_number = prior_gas_warmth.shape
    predicted_vector = prior_gas_warmth
    for section in range(2):
        bordered_vector = with_halo(predicted_vector, (("gx", 1), ("gy", 2)), 1)
        predicted_vector = propagate_model(bordered_vector, fire_power_output)
    grid_points_number = block_height_number * block_width_number
    warmth_vectorised = predicted_vector.reshape(sample_number, grid_points_number)
    heat_flat = fire_power_output.reshape(sample_number, grid_points_number)
    average_gas_warmth = jnp.mean(warmth_vectorised, axis=0)
    mean_heat = jnp.mean(heat_flat, axis=0)
    sample_deviation_matrix = warmth_vectorised - average_gas_warmth
    heat_anomaly = heat_flat - mean_heat
    picked = jnp.take(sample_deviation_matrix, reading_local_location, axis=1)
    coefficient_line = 1.0 / (reading_noise_spread * math.sqrt(sample_number - 1))
    s_matrix = picked * coefficient_line
    measurement_residual = (
        measured_warmth - jnp.take(average_gas_warmth, reading_local_location)
    ) * coefficient_line
    identity = jnp.eye(sample_number, dtype=jnp.float32)
    gram_local = jnp.dot(s_matrix, s_matrix.T, precision=lax.Precision.HIGHEST)
    projected = jnp.dot(s_matrix, measurement_residual, precision=lax.Precision.HIGHEST)
    stacked = butterfly_sum(
        jnp.concatenate([gram_local, projected[None, :]], axis=0), ("gx", "gy")
    )
    gram_sum = stacked[:sample_number] + identity
    projected_sum = stacked[sample_number]
    lower = jnp.linalg.cholesky(gram_sum)
    mean_weights = jax.scipy.linalg.cho_solve((lower, True), projected_sum)
    inverse_factor = jax.scipy.linalg.solve_triangular(lower, identity, lower=True, trans=1)
    combination_matrix = mean_weights[:, None] + inverse_factor
    updated_warmth = average_gas_warmth + jnp.dot(
        combination_matrix.T, sample_deviation_matrix, precision=lax.Precision.HIGHEST
    )
    heat_out = mean_heat + jnp.dot(
        combination_matrix.T, heat_anomaly, precision=lax.Precision.HIGHEST
    )
    return (
        updated_warmth.reshape(sample_number, block_height_number, block_width_number),
        heat_out.reshape(sample_number, block_height_number, block_width_number),
    )


def solution(mesh):
    placed = (
        P(None, "gx", "gy"),
        P(None, "gx", "gy"),
        P(("gx", "gy")),
        P(("gx", "gy")),
        P(("gx", "gy")),
    )
    return jax.shard_map(
        shards,
        mesh=mesh,
        in_specs=placed,
        out_specs=(P(None, "gx", "gy"), P(None, "gx", "gy")),
        check_vma=False,
    )
```

```python
import math

import jax
import jax.numpy as jnp
from jax import lax
from jax.sharding import PartitionSpec as P

diffusion = 0.2
heating = 0.5


def from_neighbour(block, axis, step):
    count = lax.axis_size(axis)
    if step > 0:
        pairs = [(i, i + 1) for i in range(count - 1)]
    else:
        pairs = [(i + 1, i) for i in range(count - 1)]
    return lax.ppermute(block, axis, pairs)


def from_diagonal(block, step_x, step_y):
    rows, cols = lax.axis_size("gx"), lax.axis_size("gy")
    pairs = []
    for a in range(rows):
        for b in range(cols):
            if 0 <= a + step_x < rows and 0 <= b + step_y < cols:
                pairs.append((a * cols + b, (a + step_x) * cols + b + step_y))
    return lax.ppermute(block, ("gx", "gy"), pairs)


def forecast_two_steps(warmth, heat):
    height, width = warmth.shape[1], warmth.shape[2]
    top = from_neighbour(
        jnp.concatenate([warmth[:, -2:, :], heat[:, -1:, :]], axis=1), "gx", 1
    )
    bottom = from_neighbour(
        jnp.concatenate([warmth[:, :2, :], heat[:, :1, :]], axis=1), "gx", -1
    )
    left = from_neighbour(
        jnp.concatenate([warmth[:, :, -2:], heat[:, :, -1:]], axis=2), "gy", 1
    )
    right = from_neighbour(
        jnp.concatenate([warmth[:, :, :2], heat[:, :, :1]], axis=2), "gy", -1
    )
    top_left = from_diagonal(warmth[:, -2:, -2:], 1, 1)
    top_right = from_diagonal(warmth[:, -2:, :2], 1, -1)
    bottom_left = from_diagonal(warmth[:, :2, -2:], -1, 1)
    bottom_right = from_diagonal(warmth[:, :2, :2], -1, -1)
    warmth_wide = jnp.concatenate(
        [
            jnp.concatenate([top_left, top[:, :2], top_right], axis=2),
            jnp.concatenate([left[:, :, :2], warmth, right[:, :, :2]], axis=2),
            jnp.concatenate([bottom_left, bottom[:, :2], bottom_right], axis=2),
        ],
        axis=1,
    )
    corner = jnp.zeros_like(heat[:, :1, :1])
    heat_wide = jnp.concatenate(
        [
            jnp.concatenate([corner, top[:, 2:], corner], axis=2),
            jnp.concatenate([left[:, :, 2:], heat, right[:, :, 2:]], axis=2),
            jnp.concatenate([corner, bottom[:, 2:], corner], axis=2),
        ],
        axis=1,
    )
    first = propagate_model(warmth_wide, heat_wide)
    row = lax.broadcasted_iota(jnp.int32, (height + 2, width + 2), 0)
    col = lax.broadcasted_iota(jnp.int32, (height + 2, width + 2), 1)
    at_x, at_y = lax.axis_index("gx"), lax.axis_index("gy")
    outside = (
        ((row == 0) & (at_x == 0))
        | ((row == height + 1) & (at_x == lax.axis_size("gx") - 1))
        | ((col == 0) & (at_y == 0))
        | ((col == width + 1) & (at_y == lax.axis_size("gy") - 1))
    )
    first = jnp.where(outside[None], 0.0, first)
    return propagate_model(first, heat)


def butterfly_sum(value, axes):
    for axis in axes:
        count = lax.axis_size(axis)
        if count & (count - 1):
            value = lax.psum(value, axis)
            continue
        stride = 1
        while stride < count:
            pairs = [(i, i ^ stride) for i in range(count)]
            value = value + lax.ppermute(value, axis, pairs)
            stride *= 2
    return value


def propagate_model(padded_field, source_term):
    laplacian = (
        padded_field[:, 2:, 1:-1]
        + padded_field[:, :-2, 1:-1]
        + padded_field[:, 1:-1, 2:]
        + padded_field[:, 1:-1, :-2]
        - 4.0 * padded_field[:, 1:-1, 1:-1]
    )
    return padded_field[:, 1:-1, 1:-1] + diffusion * laplacian + heating * source_term


def shards(
    prior_gas_warmth,
    fire_power_output,
    measured_warmth,
    reading_noise_spread,
    reading_local_location,
):
    sample_number, block_height_number, block_width_number = prior_gas_warmth.shape
    predicted_vector = forecast_two_steps(prior_gas_warmth, fire_power_output)
    grid_points_number = block_height_number * block_width_number
    warmth_vectorised = predicted_vector.reshape(sample_number, grid_points_number)
    heat_flat = fire_power_output.reshape(sample_number, grid_points_number)
    average_gas_warmth = jnp.mean(warmth_vectorised, axis=0)
    mean_heat = jnp.mean(heat_flat, axis=0)
    sample_deviation_matrix = warmth_vectorised - average_gas_warmth
    heat_anomaly = heat_flat - mean_heat
    picked = jnp.take(sample_deviation_matrix, reading_local_location, axis=1)
    coefficient_line = 1.0 / (reading_noise_spread * math.sqrt(sample_number - 1))
    s_matrix = picked * coefficient_line
    measurement_residual = (
        measured_warmth - jnp.take(average_gas_warmth, reading_local_location)
    ) * coefficient_line
    identity = jnp.eye(sample_number, dtype=jnp.float32)
    gram_local = jnp.dot(s_matrix, s_matrix.T, precision=lax.Precision.HIGHEST)
    projected = jnp.dot(s_matrix, measurement_residual, precision=lax.Precision.HIGHEST)
    stacked = butterfly_sum(
        jnp.concatenate([gram_local, projected[None, :]], axis=0), ("gx", "gy")
    )
    gram_sum = stacked[:sample_number] + identity
    projected_sum = stacked[sample_number]
    lower = jnp.linalg.cholesky(gram_sum)
    mean_weights = jax.scipy.linalg.cho_solve((lower, True), projected_sum)
    inverse_factor = jax.scipy.linalg.solve_triangular(lower, identity, lower=True, trans=1)
    combination_matrix = mean_weights[:, None] + inverse_factor
    updated_warmth = average_gas_warmth + jnp.dot(
        combination_matrix.T, sample_deviation_matrix, precision=lax.Precision.HIGHEST
    )
    heat_out = mean_heat + jnp.dot(
        combination_matrix.T, heat_anomaly, precision=lax.Precision.HIGHEST
    )
    return (
        updated_warmth.reshape(sample_number, block_height_number, block_width_number),
        heat_out.reshape(sample_number, block_height_number, block_width_number),
    )


def solution(mesh):
    placed = (
        P(None, "gx", "gy"),
        P(None, "gx", "gy"),
        P(("gx", "gy")),
        P(("gx", "gy")),
        P(("gx", "gy")),
    )
    return jax.shard_map(
        shards,
        mesh=mesh,
        in_specs=placed,
        out_specs=(P(None, "gx", "gy"), P(None, "gx", "gy")),
        check_vma=False,
    )
```

```python
import math

import jax
import jax.numpy as jnp
from jax import lax
from jax.sharding import PartitionSpec as P

diffusion = 0.2
heating = 0.5


def with_halo(block, sides, width):
    for axis, dim in sides:
        count = lax.axis_size(axis)
        forward = [(i, i + 1) for i in range(count - 1)]
        backward = [(target, source) for source, target in forward]
        low = lax.ppermute(
            lax.slice_in_dim(block, block.shape[dim] - width, None, axis=dim), axis, forward
        )
        high = lax.ppermute(lax.slice_in_dim(block, 0, width, axis=dim), axis, backward)
        block = jnp.concatenate([low, block, high], axis=dim)
    return block


def xor_tree(received, base, strides):
    if not strides:
        return received[base]
    return xor_tree(received, base, strides[:-1]) + xor_tree(
        received, base ^ strides[-1], strides[:-1]
    )


def butterfly_sum(value, axes):
    for axis in axes:
        count = lax.axis_size(axis)
        if count & (count - 1):
            value = lax.psum(value, axis)
            continue
        bits = [1 << b for b in range(count.bit_length() - 1)]
        for first in range(0, len(bits), 2):
            strides = bits[first : first + 2]
            received = {0: value}
            for mask in range(1, 1 << len(strides)):
                offset = 0
                for position, stride in enumerate(strides):
                    if mask >> position & 1:
                        offset ^= stride
                pairs = [(i, i ^ offset) for i in range(count)]
                received[offset] = lax.ppermute(value, axis, pairs)
            value = xor_tree(received, 0, strides)
    return value


def propagate_model(padded_field, source_term):
    laplacian = (
        padded_field[:, 2:, 1:-1]
        + padded_field[:, :-2, 1:-1]
        + padded_field[:, 1:-1, 2:]
        + padded_field[:, 1:-1, :-2]
        - 4.0 * padded_field[:, 1:-1, 1:-1]
    )
    return padded_field[:, 1:-1, 1:-1] + diffusion * laplacian + heating * source_term


def shards(
    prior_gas_warmth,
    fire_power_output,
    measured_warmth,
    reading_noise_spread,
    reading_local_location,
):
    sample_number, block_height_number, block_width_number = prior_gas_warmth.shape
    predicted_vector = prior_gas_warmth
    for section in range(2):
        bordered_vector = with_halo(predicted_vector, (("gx", 1), ("gy", 2)), 1)
        predicted_vector = propagate_model(bordered_vector, fire_power_output)
    grid_points_number = block_height_number * block_width_number
    warmth_vectorised = predicted_vector.reshape(sample_number, grid_points_number)
    heat_flat = fire_power_output.reshape(sample_number, grid_points_number)
    average_gas_warmth = jnp.mean(warmth_vectorised, axis=0)
    mean_heat = jnp.mean(heat_flat, axis=0)
    sample_deviation_matrix = warmth_vectorised - average_gas_warmth
    heat_anomaly = heat_flat - mean_heat
    picked = jnp.take(sample_deviation_matrix, reading_local_location, axis=1)
    coefficient_line = 1.0 / (reading_noise_spread * math.sqrt(sample_number - 1))
    s_matrix = picked * coefficient_line
    measurement_residual = (
        measured_warmth - jnp.take(average_gas_warmth, reading_local_location)
    ) * coefficient_line
    identity = jnp.eye(sample_number, dtype=jnp.float32)
    gram_local = jnp.dot(s_matrix, s_matrix.T, precision=lax.Precision.HIGHEST)
    projected = jnp.dot(s_matrix, measurement_residual, precision=lax.Precision.HIGHEST)
    stacked = butterfly_sum(
        jnp.concatenate([gram_local, projected[None, :]], axis=0), ("gx", "gy")
    )
    gram_sum = stacked[:sample_number] + identity
    projected_sum = stacked[sample_number]
    lower = jnp.linalg.cholesky(gram_sum)
    mean_weights = jax.scipy.linalg.cho_solve((lower, True), projected_sum)
    inverse_factor = jax.scipy.linalg.solve_triangular(lower, identity, lower=True, trans=1)
    combination_matrix = mean_weights[:, None] + inverse_factor
    updated_warmth = average_gas_warmth + jnp.dot(
        combination_matrix.T, sample_deviation_matrix, precision=lax.Precision.HIGHEST
    )
    heat_out = mean_heat + jnp.dot(
        combination_matrix.T, heat_anomaly, precision=lax.Precision.HIGHEST
    )
    return (
        updated_warmth.reshape(sample_number, block_height_number, block_width_number),
        heat_out.reshape(sample_number, block_height_number, block_width_number),
    )


def solution(mesh):
    placed = (
        P(None, "gx", "gy"),
        P(None, "gx", "gy"),
        P(("gx", "gy")),
        P(("gx", "gy")),
        P(("gx", "gy")),
    )
    return jax.shard_map(
        shards,
        mesh=mesh,
        in_specs=placed,
        out_specs=(P(None, "gx", "gy"), P(None, "gx", "gy")),
        check_vma=False,
    )
```

```python
import math

import jax
import jax.numpy as jnp
from jax import lax
from jax.experimental import pallas as pl
from jax.experimental.pallas import tpu as pltpu
from jax.sharding import PartitionSpec as P

diffusion = 0.2
heating = 0.5


def with_halo(block, sides, width):
    for axis, dim in sides:
        count = lax.axis_size(axis)
        forward = [(i, i + 1) for i in range(count - 1)]
        backward = [(target, source) for source, target in forward]
        low = lax.ppermute(
            lax.slice_in_dim(block, block.shape[dim] - width, None, axis=dim), axis, forward
        )
        high = lax.ppermute(lax.slice_in_dim(block, 0, width, axis=dim), axis, backward)
        block = jnp.concatenate([low, block, high], axis=dim)
    return block


def xor_tree(received, base, strides):
    if not strides:
        return received[base]
    return xor_tree(received, base, strides[:-1]) + xor_tree(
        received, base ^ strides[-1], strides[:-1]
    )


def butterfly_sum(value, axes):
    for axis in axes:
        count = lax.axis_size(axis)
        if count & (count - 1):
            value = lax.psum(value, axis)
            continue
        bits = [1 << b for b in range(count.bit_length() - 1)]
        for first in range(0, len(bits), 2):
            strides = bits[first : first + 2]
            received = {0: value}
            for mask in range(1, 1 << len(strides)):
                offset = 0
                for position, stride in enumerate(strides):
                    if mask >> position & 1:
                        offset ^= stride
                pairs = [(i, i ^ offset) for i in range(count)]
                received[offset] = lax.ppermute(value, axis, pairs)
            value = xor_tree(received, 0, strides)
    return value


def inverse_factor_kernel(gram_ref, inverse_ref, work_ref):
    size = gram_ref.shape[0]
    work_ref[...] = gram_ref[...]
    square_row = lax.broadcasted_iota(jnp.int32, (size, size), 0)
    square_col = lax.broadcasted_iota(jnp.int32, (size, size), 1)
    inverse_ref[...] = jnp.where(square_row == square_col, 1.0, 0.0).astype(jnp.float32)
    lane = lax.broadcasted_iota(jnp.int32, (1, size), 1)
    sublane = lax.broadcasted_iota(jnp.int32, (size, 1), 0)

    def step(k, carry):
        row = work_ref[pl.ds(k, 1), :]
        column = jnp.sum(jnp.where(square_col == k, work_ref[...], 0.0), axis=1, keepdims=True)
        pivot = jnp.sum(jnp.where(lane == k, row, 0.0), axis=1, keepdims=True)
        root = jnp.sqrt(pivot)
        factor_row = jnp.where(lane >= k, row / root, 0.0)
        factor_col = jnp.where(sublane >= k, column / root, 0.0)
        work_ref[...] = work_ref[...] - factor_col * factor_row
        inverse_row = inverse_ref[pl.ds(k, 1), :] / root
        below = jnp.where(sublane > k, factor_col, 0.0)
        inverse_ref[...] = inverse_ref[...] - below * inverse_row
        inverse_ref[pl.ds(k, 1), :] = inverse_row
        return carry

    lax.fori_loop(0, size, step, 0)


def inverse_factor(gram):
    size = gram.shape[0]
    return pl.pallas_call(
        inverse_factor_kernel,
        out_shape=jax.ShapeDtypeStruct((size, size), jnp.float32),
        in_specs=[pl.BlockSpec(memory_space=pltpu.VMEM)],
        out_specs=pl.BlockSpec(memory_space=pltpu.VMEM),
        scratch_shapes=[pltpu.VMEM((size, size), jnp.float32)],
    )(gram)

def propagate_model(padded_field, source_term):
    laplacian = (
        padded_field[:, 2:, 1:-1]
        + padded_field[:, :-2, 1:-1]
        + padded_field[:, 1:-1, 2:]
        + padded_field[:, 1:-1, :-2]
        - 4.0 * padded_field[:, 1:-1, 1:-1]
    )
    return padded_field[:, 1:-1, 1:-1] + diffusion * laplacian + heating * source_term


def shards(
    prior_gas_warmth,
    fire_power_output,
    measured_warmth,
    reading_noise_spread,
    reading_local_location,
):
    sample_number, block_height_number, block_width_number = prior_gas_warmth.shape
    predicted_vector = prior_gas_warmth
    for section in range(2):
        bordered_vector = with_halo(predicted_vector, (("gx", 1), ("gy", 2)), 1)
        predicted_vector = propagate_model(bordered_vector, fire_power_output)
    grid_points_number = block_height_number * block_width_number
    warmth_vectorised = predicted_vector.reshape(sample_number, grid_points_number)
    heat_flat = fire_power_output.reshape(sample_number, grid_points_number)
    average_gas_warmth = jnp.mean(warmth_vectorised, axis=0)
    mean_heat = jnp.mean(heat_flat, axis=0)
    sample_deviation_matrix = warmth_vectorised - average_gas_warmth
    heat_anomaly = heat_flat - mean_heat
    picked = jnp.take(sample_deviation_matrix, reading_local_location, axis=1)
    coefficient_line = 1.0 / (reading_noise_spread * math.sqrt(sample_number - 1))
    s_matrix = picked * coefficient_line
    measurement_residual = (
        measured_warmth - jnp.take(average_gas_warmth, reading_local_location)
    ) * coefficient_line
    identity = jnp.eye(sample_number, dtype=jnp.float32)
    gram_local = jnp.dot(s_matrix, s_matrix.T, precision=lax.Precision.HIGHEST)
    projected = jnp.dot(s_matrix, measurement_residual, precision=lax.Precision.HIGHEST)
    stacked = butterfly_sum(
        jnp.concatenate([gram_local, projected[None, :]], axis=0), ("gx", "gy")
    )
    gram_sum = stacked[:sample_number] + identity
    projected_sum = stacked[sample_number]
    lower_inverse = inverse_factor(gram_sum)
    whitened = jnp.dot(lower_inverse, projected_sum, precision=lax.Precision.HIGHEST)
    mean_weights = jnp.dot(lower_inverse.T, whitened, precision=lax.Precision.HIGHEST)
    combination_transposed = lower_inverse + mean_weights[None, :]
    updated_warmth = average_gas_warmth + jnp.dot(
        combination_transposed, sample_deviation_matrix, precision=lax.Precision.HIGHEST
    )
    heat_out = mean_heat + jnp.dot(
        combination_transposed, heat_anomaly, precision=lax.Precision.HIGHEST
    )
    return (
        updated_warmth.reshape(sample_number, block_height_number, block_width_number),
        heat_out.reshape(sample_number, block_height_number, block_width_number),
    )


def solution(mesh):
    placed = (
        P(None, "gx", "gy"),
        P(None, "gx", "gy"),
        P(("gx", "gy")),
        P(("gx", "gy")),
        P(("gx", "gy")),
    )
    return jax.shard_map(
        shards,
        mesh=mesh,
        in_specs=placed,
        out_specs=(P(None, "gx", "gy"), P(None, "gx", "gy")),
        check_vma=False,
    )
```

```python
import math

import jax
import jax.numpy as jnp
from jax import lax
from jax.experimental import pallas as pl
from jax.experimental.pallas import tpu as pltpu
from jax.sharding import PartitionSpec as P

diffusion = 0.2
heating = 0.5


def with_halo(block, sides, width):
    for axis, dim in sides:
        count = lax.axis_size(axis)
        forward = [(i, i + 1) for i in range(count - 1)]
        backward = [(target, source) for source, target in forward]
        low = lax.ppermute(
            lax.slice_in_dim(block, block.shape[dim] - width, None, axis=dim), axis, forward
        )
        high = lax.ppermute(lax.slice_in_dim(block, 0, width, axis=dim), axis, backward)
        block = jnp.concatenate([low, block, high], axis=dim)
    return block


def xor_tree(received, base, strides):
    if not strides:
        return received[base]
    return xor_tree(received, base, strides[:-1]) + xor_tree(
        received, base ^ strides[-1], strides[:-1]
    )


def butterfly_sum(value, axes):
    for axis in axes:
        count = lax.axis_size(axis)
        if count & (count - 1):
            value = lax.psum(value, axis)
            continue
        bits = [1 << b for b in range(count.bit_length() - 1)]
        for first in range(0, len(bits), 2):
            strides = bits[first : first + 2]
            received = {0: value}
            for mask in range(1, 1 << len(strides)):
                offset = 0
                for position, stride in enumerate(strides):
                    if mask >> position & 1:
                        offset ^= stride
                pairs = [(i, i ^ offset) for i in range(count)]
                received[offset] = lax.ppermute(value, axis, pairs)
            value = xor_tree(received, 0, strides)
    return value


def inverse_factor_kernel(gram_ref, inverse_ref, work_ref):
    size = gram_ref.shape[0]
    work_ref[...] = gram_ref[...]
    square_row = lax.broadcasted_iota(jnp.int32, (size, size), 0)
    square_col = lax.broadcasted_iota(jnp.int32, (size, size), 1)
    inverse_ref[...] = jnp.where(square_row == square_col, 1.0, 0.0).astype(jnp.float32)
    lane = lax.broadcasted_iota(jnp.int32, (1, size), 1)
    sublane = lax.broadcasted_iota(jnp.int32, (size, 1), 0)

    def step(k, carry):
        row = work_ref[pl.ds(k, 1), :]
        column = jnp.sum(jnp.where(square_col == k, work_ref[...], 0.0), axis=1, keepdims=True)
        pivot = jnp.sum(jnp.where(lane == k, row, 0.0), axis=1, keepdims=True)
        root = jnp.sqrt(pivot)
        factor_row = jnp.where(lane >= k, row / root, 0.0)
        factor_col = jnp.where(sublane >= k, column / root, 0.0)
        work_ref[...] = work_ref[...] - factor_col * factor_row
        inverse_row = inverse_ref[pl.ds(k, 1), :] / root
        below = jnp.where(sublane > k, factor_col, 0.0)
        inverse_ref[...] = inverse_ref[...] - below * inverse_row
        inverse_ref[pl.ds(k, 1), :] = inverse_row
        return carry

    lax.fori_loop(0, size, step, 0)


def inverse_factor(gram):
    size = gram.shape[0]
    return pl.pallas_call(
        inverse_factor_kernel,
        out_shape=jax.ShapeDtypeStruct((size, size), jnp.float32),
        in_specs=[pl.BlockSpec(memory_space=pltpu.VMEM)],
        out_specs=pl.BlockSpec(memory_space=pltpu.VMEM),
        scratch_shapes=[pltpu.VMEM((size, size), jnp.float32)],
    )(gram)

def propagate_model(padded_field, source_term):
    laplacian = (
        padded_field[:, 2:, 1:-1]
        + padded_field[:, :-2, 1:-1]
        + padded_field[:, 1:-1, 2:]
        + padded_field[:, 1:-1, :-2]
        - 4.0 * padded_field[:, 1:-1, 1:-1]
    )
    return padded_field[:, 1:-1, 1:-1] + diffusion * laplacian + heating * source_term


def shards(
    prior_gas_warmth,
    fire_power_output,
    measured_warmth,
    reading_noise_spread,
    reading_local_location,
):
    sample_number, block_height_number, block_width_number = prior_gas_warmth.shape
    predicted_vector = prior_gas_warmth
    for section in range(2):
        bordered_vector = with_halo(predicted_vector, (("gx", 1), ("gy", 2)), 1)
        predicted_vector = propagate_model(bordered_vector, fire_power_output)
    average_gas_warmth = jnp.mean(predicted_vector, axis=0)
    mean_heat = jnp.mean(fire_power_output, axis=0)
    sample_deviation_matrix = predicted_vector - average_gas_warmth
    heat_anomaly = fire_power_output - mean_heat
    coefficient_line = 1.0 / (reading_noise_spread * math.sqrt(sample_number - 1))
    weight_line = coefficient_line * coefficient_line
    row_hot = (
        (reading_local_location // block_width_number)[:, None]
        == lax.broadcasted_iota(jnp.int32, (1, block_height_number), 1)
    ).astype(jnp.float32)
    col_hot = (
        (reading_local_location % block_width_number)[:, None]
        == lax.broadcasted_iota(jnp.int32, (1, block_width_number), 1)
    ).astype(jnp.float32)
    weighted_rows = jnp.concatenate(
        [row_hot * weight_line[:, None], row_hot * (weight_line * measured_warmth)[:, None]],
        axis=1,
    )
    cell_sums = lax.dot_general(
        weighted_rows, col_hot, (((0,), (0,)), ((), ())), precision=lax.Precision.HIGHEST
    )
    cell_weight = cell_sums[:block_height_number]
    cell_residual = cell_sums[block_height_number:] - average_gas_warmth * cell_weight
    gram_local = lax.dot_general(
        sample_deviation_matrix * cell_weight,
        sample_deviation_matrix,
        (((1, 2), (1, 2)), ((), ())),
        precision=lax.Precision.HIGHEST,
    )
    projected = lax.dot_general(
        sample_deviation_matrix,
        cell_residual,
        (((1, 2), (0, 1)), ((), ())),
        precision=lax.Precision.HIGHEST,
    )
    identity = jnp.eye(sample_number, dtype=jnp.float32)
    stacked = butterfly_sum(
        jnp.concatenate([gram_local, projected[None, :]], axis=0), ("gx", "gy")
    )
    gram_sum = stacked[:sample_number] + identity
    projected_sum = stacked[sample_number]
    lower_inverse = inverse_factor(gram_sum)
    whitened = jnp.dot(lower_inverse, projected_sum, precision=lax.Precision.HIGHEST)
    mean_weights = jnp.dot(lower_inverse.T, whitened, precision=lax.Precision.HIGHEST)
    combination_transposed = lower_inverse + mean_weights[None, :]
    contract = (((1,), (0,)), ((), ()))
    updated_warmth = average_gas_warmth + lax.dot_general(
        combination_transposed, sample_deviation_matrix, contract, precision=lax.Precision.HIGHEST
    )
    heat_out = mean_heat + lax.dot_general(
        combination_transposed, heat_anomaly, contract, precision=lax.Precision.HIGHEST
    )
    return (updated_warmth, heat_out)


def solution(mesh):
    placed = (
        P(None, "gx", "gy"),
        P(None, "gx", "gy"),
        P(("gx", "gy")),
        P(("gx", "gy")),
        P(("gx", "gy")),
    )
    return jax.shard_map(
        shards,
        mesh=mesh,
        in_specs=placed,
        out_specs=(P(None, "gx", "gy"), P(None, "gx", "gy")),
        check_vma=False,
    )
```

```python
import math

import jax
import jax.numpy as jnp
from jax import lax
from jax.experimental import pallas as pl
from jax.experimental.pallas import tpu as pltpu
from jax.sharding import PartitionSpec as P

diffusion = 0.2
heating = 0.5


def with_halo(block, sides, width):
    for axis, dim in sides:
        count = lax.axis_size(axis)
        forward = [(i, i + 1) for i in range(count - 1)]
        backward = [(target, source) for source, target in forward]
        low = lax.ppermute(
            lax.slice_in_dim(block, block.shape[dim] - width, None, axis=dim), axis, forward
        )
        high = lax.ppermute(lax.slice_in_dim(block, 0, width, axis=dim), axis, backward)
        block = jnp.concatenate([low, block, high], axis=dim)
    return block


def xor_tree(received, base, strides):
    if not strides:
        return received[base]
    return xor_tree(received, base, strides[:-1]) + xor_tree(
        received, base ^ strides[-1], strides[:-1]
    )


def butterfly_sum(value, axes):
    for axis in axes:
        count = lax.axis_size(axis)
        if count & (count - 1):
            value = lax.psum(value, axis)
            continue
        bits = [1 << b for b in range(count.bit_length() - 1)]
        for first in range(0, len(bits), 2):
            strides = bits[first : first + 2]
            received = {0: value}
            for mask in range(1, 1 << len(strides)):
                offset = 0
                for position, stride in enumerate(strides):
                    if mask >> position & 1:
                        offset ^= stride
                pairs = [(i, i ^ offset) for i in range(count)]
                received[offset] = lax.ppermute(value, axis, pairs)
            value = xor_tree(received, 0, strides)
    return value


def inverse_factor_kernel(gram_ref, inverse_ref, work_ref):
    size = gram_ref.shape[0]
    work_ref[...] = gram_ref[...]
    square_row = lax.broadcasted_iota(jnp.int32, (size, size), 0)
    square_col = lax.broadcasted_iota(jnp.int32, (size, size), 1)
    inverse_ref[...] = jnp.where(square_row == square_col, 1.0, 0.0).astype(jnp.float32)
    lane = lax.broadcasted_iota(jnp.int32, (1, size), 1)
    sublane = lax.broadcasted_iota(jnp.int32, (size, 1), 0)

    def step(k, carry):
        row = work_ref[pl.ds(k, 1), :]
        column = jnp.sum(jnp.where(square_col == k, work_ref[...], 0.0), axis=1, keepdims=True)
        pivot = jnp.sum(jnp.where(lane == k, row, 0.0), axis=1, keepdims=True)
        root = jnp.sqrt(pivot)
        factor_row = jnp.where(lane >= k, row / root, 0.0)
        factor_col = jnp.where(sublane >= k, column / root, 0.0)
        work_ref[...] = work_ref[...] - factor_col * factor_row
        inverse_row = inverse_ref[pl.ds(k, 1), :] / root
        below = jnp.where(sublane > k, factor_col, 0.0)
        inverse_ref[...] = inverse_ref[...] - below * inverse_row
        inverse_ref[pl.ds(k, 1), :] = inverse_row
        return carry

    lax.fori_loop(0, size, step, 0)


def inverse_factor(gram):
    size = gram.shape[0]
    return pl.pallas_call(
        inverse_factor_kernel,
        out_shape=jax.ShapeDtypeStruct((size, size), jnp.float32),
        in_specs=[pl.BlockSpec(memory_space=pltpu.VMEM)],
        out_specs=pl.BlockSpec(memory_space=pltpu.VMEM),
        scratch_shapes=[pltpu.VMEM((size, size), jnp.float32)],
    )(gram)

def propagate_model(padded_field, source_term):
    laplacian = (
        padded_field[:, 2:, 1:-1]
        + padded_field[:, :-2, 1:-1]
        + padded_field[:, 1:-1, 2:]
        + padded_field[:, 1:-1, :-2]
        - 4.0 * padded_field[:, 1:-1, 1:-1]
    )
    return padded_field[:, 1:-1, 1:-1] + diffusion * laplacian + heating * source_term


def propagate_members_last(padded_field, source_term):
    laplacian = (
        padded_field[1:-1, 2:]
        + padded_field[1:-1, :-2]
        + padded_field[2:, 1:-1]
        + padded_field[:-2, 1:-1]
        - 4.0 * padded_field[1:-1, 1:-1]
    )
    return padded_field[1:-1, 1:-1] + diffusion * laplacian + heating * source_term


def shards(
    prior_gas_warmth,
    fire_power_output,
    measured_warmth,
    reading_noise_spread,
    reading_local_location,
):
    sample_number, block_height_number, block_width_number = prior_gas_warmth.shape
    warmth_t = jnp.transpose(prior_gas_warmth, (2, 1, 0))
    heat_t = jnp.transpose(fire_power_output, (2, 1, 0))
    predicted_t = warmth_t
    for section in range(2):
        bordered = with_halo(predicted_t, (("gx", 1), ("gy", 0)), 1)
        predicted_t = propagate_members_last(bordered, heat_t)
    average_t = jnp.mean(predicted_t, axis=2)
    mean_heat_t = jnp.mean(heat_t, axis=2)
    deviation_t = predicted_t - average_t[:, :, None]
    heat_anomaly_t = heat_t - mean_heat_t[:, :, None]
    coefficient_line = 1.0 / (reading_noise_spread * math.sqrt(sample_number - 1))
    weight_line = coefficient_line * coefficient_line
    row_hot = (
        (reading_local_location // block_width_number)[:, None]
        == lax.broadcasted_iota(jnp.int32, (1, block_height_number), 1)
    ).astype(jnp.float32)
    col_hot = (
        (reading_local_location % block_width_number)[:, None]
        == lax.broadcasted_iota(jnp.int32, (1, block_width_number), 1)
    ).astype(jnp.float32)
    weighted_rows = jnp.concatenate(
        [row_hot * weight_line[:, None], row_hot * (weight_line * measured_warmth)[:, None]],
        axis=1,
    )
    cell_sums = lax.dot_general(
        col_hot, weighted_rows, (((0,), (0,)), ((), ())), precision=lax.Precision.HIGHEST
    )
    cell_weight = cell_sums[:, :block_height_number]
    cell_residual = cell_sums[:, block_height_number:] - average_t * cell_weight
    gram_local = lax.dot_general(
        deviation_t * cell_weight[:, :, None],
        deviation_t,
        (((0, 1), (0, 1)), ((), ())),
        precision=lax.Precision.HIGHEST,
    )
    projected = lax.dot_general(
        deviation_t,
        cell_residual,
        (((0, 1), (0, 1)), ((), ())),
        precision=lax.Precision.HIGHEST,
    )
    identity = jnp.eye(sample_number, dtype=jnp.float32)
    stacked = butterfly_sum(
        jnp.concatenate([gram_local, projected[None, :]], axis=0), ("gx", "gy")
    )
    gram_sum = stacked[:sample_number] + identity
    projected_sum = stacked[sample_number]
    lower_inverse = inverse_factor(gram_sum)
    whitened = jnp.dot(lower_inverse, projected_sum, precision=lax.Precision.HIGHEST)
    mean_weights = jnp.dot(lower_inverse.T, whitened, precision=lax.Precision.HIGHEST)
    combination_transposed = lower_inverse + mean_weights[None, :]
    contract = (((2,), (1,)), ((), ()))
    updated_t = average_t[:, :, None] + lax.dot_general(
        deviation_t, combination_transposed, contract, precision=lax.Precision.HIGHEST
    )
    heat_out_t = mean_heat_t[:, :, None] + lax.dot_general(
        heat_anomaly_t, combination_transposed, contract, precision=lax.Precision.HIGHEST
    )
    return (jnp.transpose(updated_t, (2, 1, 0)), jnp.transpose(heat_out_t, (2, 1, 0)))


def solution(mesh):
    placed = (
        P(None, "gx", "gy"),
        P(None, "gx", "gy"),
        P(("gx", "gy")),
        P(("gx", "gy")),
        P(("gx", "gy")),
    )
    return jax.shard_map(
        shards,
        mesh=mesh,
        in_specs=placed,
        out_specs=(P(None, "gx", "gy"), P(None, "gx", "gy")),
        check_vma=False,
    )
```

```python
import math

import jax
import jax.numpy as jnp
from jax import lax
from jax.experimental import pallas as pl
from jax.experimental.pallas import tpu as pltpu
from jax.sharding import PartitionSpec as P

diffusion = 0.2
heating = 0.5


def xor_tree(received, base, strides):
    if not strides:
        return received[base]
    return xor_tree(received, base, strides[:-1]) + xor_tree(
        received, base ^ strides[-1], strides[:-1]
    )


def butterfly_sum(value, axes):
    for axis in axes:
        count = lax.axis_size(axis)
        if count & (count - 1):
            value = lax.psum(value, axis)
            continue
        bits = [1 << b for b in range(count.bit_length() - 1)]
        for first in range(0, len(bits), 2):
            strides = bits[first : first + 2]
            received = {0: value}
            for mask in range(1, 1 << len(strides)):
                offset = 0
                for position, stride in enumerate(strides):
                    if mask >> position & 1:
                        offset ^= stride
                pairs = [(i, i ^ offset) for i in range(count)]
                received[offset] = lax.ppermute(value, axis, pairs)
            value = xor_tree(received, 0, strides)
    return value


def inverse_factor_kernel(gram_ref, inverse_ref, work_ref):
    size = gram_ref.shape[0]
    work_ref[...] = gram_ref[...]
    square_row = lax.broadcasted_iota(jnp.int32, (size, size), 0)
    square_col = lax.broadcasted_iota(jnp.int32, (size, size), 1)
    inverse_ref[...] = jnp.where(square_row == square_col, 1.0, 0.0).astype(jnp.float32)
    lane = lax.broadcasted_iota(jnp.int32, (1, size), 1)
    sublane = lax.broadcasted_iota(jnp.int32, (size, 1), 0)

    def step(k, carry):
        row = work_ref[pl.ds(k, 1), :]
        column = jnp.sum(jnp.where(square_col == k, work_ref[...], 0.0), axis=1, keepdims=True)
        pivot = jnp.sum(jnp.where(lane == k, row, 0.0), axis=1, keepdims=True)
        root = jnp.sqrt(pivot)
        factor_row = jnp.where(lane >= k, row / root, 0.0)
        factor_col = jnp.where(sublane >= k, column / root, 0.0)
        work_ref[...] = work_ref[...] - factor_col * factor_row
        inverse_row = inverse_ref[pl.ds(k, 1), :] / root
        below = jnp.where(sublane > k, factor_col, 0.0)
        inverse_ref[...] = inverse_ref[...] - below * inverse_row
        inverse_ref[pl.ds(k, 1), :] = inverse_row
        return carry

    lax.fori_loop(0, size, step, 0)


def inverse_factor(gram):
    size = gram.shape[0]
    return pl.pallas_call(
        inverse_factor_kernel,
        out_shape=jax.ShapeDtypeStruct((size, size), jnp.float32),
        in_specs=[pl.BlockSpec(memory_space=pltpu.VMEM)],
        out_specs=pl.BlockSpec(memory_space=pltpu.VMEM),
        scratch_shapes=[pltpu.VMEM((size, size), jnp.float32)],
    )(gram)

def propagate_model(padded_field, source_term):
    laplacian = (
        padded_field[:, 2:, 1:-1]
        + padded_field[:, :-2, 1:-1]
        + padded_field[:, 1:-1, 2:]
        + padded_field[:, 1:-1, :-2]
        - 4.0 * padded_field[:, 1:-1, 1:-1]
    )
    return padded_field[:, 1:-1, 1:-1] + diffusion * laplacian + heating * source_term


def propagate_members_last(padded_field, source_term):
    laplacian = (
        padded_field[1:-1, 2:]
        + padded_field[1:-1, :-2]
        + padded_field[2:, 1:-1]
        + padded_field[:-2, 1:-1]
        - 4.0 * padded_field[1:-1, 1:-1]
    )
    return padded_field[1:-1, 1:-1] + diffusion * laplacian + heating * source_term


def from_neighbour(block, axis, step):
    count = lax.axis_size(axis)
    if step > 0:
        pairs = [(i, i + 1) for i in range(count - 1)]
    else:
        pairs = [(i + 1, i) for i in range(count - 1)]
    return lax.ppermute(block, axis, pairs)


def from_diagonal(block, step_x, step_y):
    rows, cols = lax.axis_size("gx"), lax.axis_size("gy")
    pairs = []
    for a in range(rows):
        for b in range(cols):
            if 0 <= a + step_x < rows and 0 <= b + step_y < cols:
                pairs.append((a * cols + b, (a + step_x) * cols + b + step_y))
    return lax.ppermute(block, ("gx", "gy"), pairs)


def forecast_two_steps(warmth, heat):
    width, height = warmth.shape[0], warmth.shape[1]
    top = from_neighbour(
        jnp.concatenate([warmth[:, -2:], heat[:, -1:]], axis=1), "gx", 1
    )
    bottom = from_neighbour(
        jnp.concatenate([warmth[:, :2], heat[:, :1]], axis=1), "gx", -1
    )
    left = from_neighbour(jnp.concatenate([warmth[-2:], heat[-1:]], axis=0), "gy", 1)
    right = from_neighbour(jnp.concatenate([warmth[:2], heat[:1]], axis=0), "gy", -1)
    top_left = from_diagonal(warmth[-2:, -2:], 1, 1)
    top_right = from_diagonal(warmth[:2, -2:], 1, -1)
    bottom_left = from_diagonal(warmth[-2:, :2], -1, 1)
    bottom_right = from_diagonal(warmth[:2, :2], -1, -1)
    warmth_wide = jnp.concatenate(
        [
            jnp.concatenate([top_left, left[:2], bottom_left], axis=1),
            jnp.concatenate([top[:, :2], warmth, bottom[:, :2]], axis=1),
            jnp.concatenate([top_right, right[:2], bottom_right], axis=1),
        ],
        axis=0,
    )
    corner = jnp.zeros_like(heat[:1, :1])
    heat_wide = jnp.concatenate(
        [
            jnp.concatenate([corner, left[2:], corner], axis=1),
            jnp.concatenate([top[:, 2:], heat, bottom[:, 2:]], axis=1),
            jnp.concatenate([corner, right[2:], corner], axis=1),
        ],
        axis=0,
    )
    first = propagate_members_last(warmth_wide, heat_wide)
    col = lax.broadcasted_iota(jnp.int32, (width + 2, height + 2), 0)
    row = lax.broadcasted_iota(jnp.int32, (width + 2, height + 2), 1)
    at_x, at_y = lax.axis_index("gx"), lax.axis_index("gy")
    outside = (
        ((row == 0) & (at_x == 0))
        | ((row == height + 1) & (at_x == lax.axis_size("gx") - 1))
        | ((col == 0) & (at_y == 0))
        | ((col == width + 1) & (at_y == lax.axis_size("gy") - 1))
    )
    first = jnp.where(outside[:, :, None], 0.0, first)
    return propagate_members_last(first, heat)


def shards(
    prior_gas_warmth,
    fire_power_output,
    measured_warmth,
    reading_noise_spread,
    reading_local_location,
):
    sample_number, block_height_number, block_width_number = prior_gas_warmth.shape
    warmth_t = jnp.transpose(prior_gas_warmth, (2, 1, 0))
    heat_t = jnp.transpose(fire_power_output, (2, 1, 0))
    predicted_t = forecast_two_steps(warmth_t, heat_t)
    average_t = jnp.mean(predicted_t, axis=2)
    mean_heat_t = jnp.mean(heat_t, axis=2)
    deviation_t = predicted_t - average_t[:, :, None]
    heat_anomaly_t = heat_t - mean_heat_t[:, :, None]
    coefficient_line = 1.0 / (reading_noise_spread * math.sqrt(sample_number - 1))
    weight_line = coefficient_line * coefficient_line
    row_hot = (
        (reading_local_location // block_width_number)[:, None]
        == lax.broadcasted_iota(jnp.int32, (1, block_height_number), 1)
    ).astype(jnp.float32)
    col_hot = (
        (reading_local_location % block_width_number)[:, None]
        == lax.broadcasted_iota(jnp.int32, (1, block_width_number), 1)
    ).astype(jnp.float32)
    weighted_rows = jnp.concatenate(
        [row_hot * weight_line[:, None], row_hot * (weight_line * measured_warmth)[:, None]],
        axis=1,
    )
    cell_sums = lax.dot_general(
        col_hot, weighted_rows, (((0,), (0,)), ((), ())), precision=lax.Precision.HIGHEST
    )
    cell_weight = cell_sums[:, :block_height_number]
    cell_residual = cell_sums[:, block_height_number:] - average_t * cell_weight
    gram_local = lax.dot_general(
        deviation_t * cell_weight[:, :, None],
        deviation_t,
        (((0, 1), (0, 1)), ((), ())),
        precision=lax.Precision.HIGHEST,
    )
    projected = lax.dot_general(
        deviation_t,
        cell_residual,
        (((0, 1), (0, 1)), ((), ())),
        precision=lax.Precision.HIGHEST,
    )
    identity = jnp.eye(sample_number, dtype=jnp.float32)
    stacked = butterfly_sum(
        jnp.concatenate([gram_local, projected[None, :]], axis=0), ("gx", "gy")
    )
    gram_sum = stacked[:sample_number] + identity
    projected_sum = stacked[sample_number]
    lower_inverse = inverse_factor(gram_sum)
    whitened = jnp.dot(lower_inverse, projected_sum, precision=lax.Precision.HIGHEST)
    mean_weights = jnp.dot(lower_inverse.T, whitened, precision=lax.Precision.HIGHEST)
    combination_transposed = lower_inverse + mean_weights[None, :]
    contract = (((2,), (1,)), ((), ()))
    updated_t = average_t[:, :, None] + lax.dot_general(
        deviation_t, combination_transposed, contract, precision=lax.Precision.HIGHEST
    )
    heat_out_t = mean_heat_t[:, :, None] + lax.dot_general(
        heat_anomaly_t, combination_transposed, contract, precision=lax.Precision.HIGHEST
    )
    return (jnp.transpose(updated_t, (2, 1, 0)), jnp.transpose(heat_out_t, (2, 1, 0)))


def solution(mesh):
    placed = (
        P(None, "gx", "gy"),
        P(None, "gx", "gy"),
        P(("gx", "gy")),
        P(("gx", "gy")),
        P(("gx", "gy")),
    )
    return jax.shard_map(
        shards,
        mesh=mesh,
        in_specs=placed,
        out_specs=(P(None, "gx", "gy"), P(None, "gx", "gy")),
        check_vma=False,
    )
```

```python
import math

import jax
import jax.numpy as jnp
from jax import lax
from jax.experimental import pallas as pl
from jax.experimental.pallas import tpu as pltpu
from jax.sharding import PartitionSpec as P

diffusion = 0.2
heating = 0.5


def xor_tree(received, base, strides):
    if not strides:
        return received[base]
    return xor_tree(received, base, strides[:-1]) + xor_tree(
        received, base ^ strides[-1], strides[:-1]
    )


def butterfly_sum(value, axes):
    for axis in axes:
        count = lax.axis_size(axis)
        if count & (count - 1):
            value = lax.psum(value, axis)
            continue
        bits = [1 << b for b in range(count.bit_length() - 1)]
        for first in range(0, len(bits), 2):
            strides = bits[first : first + 2]
            received = {0: value}
            for mask in range(1, 1 << len(strides)):
                offset = 0
                for position, stride in enumerate(strides):
                    if mask >> position & 1:
                        offset ^= stride
                pairs = [(i, i ^ offset) for i in range(count)]
                received[offset] = lax.ppermute(value, axis, pairs)
            value = xor_tree(received, 0, strides)
    return value


def inverse_factor_kernel(gram_ref, inverse_ref, work_ref):
    size = gram_ref.shape[0]
    work_ref[...] = gram_ref[...]
    square_row = lax.broadcasted_iota(jnp.int32, (size, size), 0)
    square_col = lax.broadcasted_iota(jnp.int32, (size, size), 1)
    inverse_ref[...] = jnp.where(square_row == square_col, 1.0, 0.0).astype(jnp.float32)
    lane = lax.broadcasted_iota(jnp.int32, (1, size), 1)
    sublane = lax.broadcasted_iota(jnp.int32, (size, 1), 0)

    def step(k, carry):
        row = work_ref[pl.ds(k, 1), :]
        column = jnp.sum(jnp.where(square_col == k, work_ref[...], 0.0), axis=1, keepdims=True)
        pivot = jnp.sum(jnp.where(lane == k, row, 0.0), axis=1, keepdims=True)
        root = jnp.sqrt(pivot)
        factor_row = jnp.where(lane >= k, row / root, 0.0)
        factor_col = jnp.where(sublane >= k, column / root, 0.0)
        work_ref[...] = work_ref[...] - factor_col * factor_row
        inverse_row = inverse_ref[pl.ds(k, 1), :] / root
        below = jnp.where(sublane > k, factor_col, 0.0)
        inverse_ref[...] = inverse_ref[...] - below * inverse_row
        inverse_ref[pl.ds(k, 1), :] = inverse_row
        return carry

    lax.fori_loop(0, size, step, 0)


def inverse_factor(gram):
    size = gram.shape[0]
    return pl.pallas_call(
        inverse_factor_kernel,
        out_shape=jax.ShapeDtypeStruct((size, size), jnp.float32),
        in_specs=[pl.BlockSpec(memory_space=pltpu.VMEM)],
        out_specs=pl.BlockSpec(memory_space=pltpu.VMEM),
        scratch_shapes=[pltpu.VMEM((size, size), jnp.float32)],
    )(gram)

def propagate_model(padded_field, source_term):
    laplacian = (
        padded_field[:, 2:, 1:-1]
        + padded_field[:, :-2, 1:-1]
        + padded_field[:, 1:-1, 2:]
        + padded_field[:, 1:-1, :-2]
        - 4.0 * padded_field[:, 1:-1, 1:-1]
    )
    return padded_field[:, 1:-1, 1:-1] + diffusion * laplacian + heating * source_term


def propagate_members_last(padded_field, source_term):
    laplacian = (
        padded_field[1:-1, 2:]
        + padded_field[1:-1, :-2]
        + padded_field[2:, 1:-1]
        + padded_field[:-2, 1:-1]
        - 4.0 * padded_field[1:-1, 1:-1]
    )
    return padded_field[1:-1, 1:-1] + diffusion * laplacian + heating * source_term


def from_neighbour(block, axis, step):
    count = lax.axis_size(axis)
    if step > 0:
        pairs = [(i, i + 1) for i in range(count - 1)]
    else:
        pairs = [(i + 1, i) for i in range(count - 1)]
    return lax.ppermute(block, axis, pairs)


def forecast_two_steps(warmth, heat):
    width, height = warmth.shape[0], warmth.shape[1]
    top = from_neighbour(
        jnp.concatenate([warmth[:, -2:], heat[:, -1:]], axis=1), "gx", 1
    )
    bottom = from_neighbour(
        jnp.concatenate([warmth[:, :2], heat[:, :1]], axis=1), "gx", -1
    )
    warmth_tall = jnp.concatenate([top[:, :2], warmth, bottom[:, :2]], axis=1)
    heat_tall = jnp.concatenate([top[:, 2:], heat, bottom[:, 2:]], axis=1)
    edge = jnp.zeros_like(heat_tall[:1, :1])
    left = from_neighbour(
        jnp.concatenate(
            [warmth_tall[-2:], jnp.concatenate([edge, heat_tall[-1:], edge], axis=1)],
            axis=0,
        ),
        "gy",
        1,
    )
    right = from_neighbour(
        jnp.concatenate(
            [warmth_tall[:2], jnp.concatenate([edge, heat_tall[:1], edge], axis=1)],
            axis=0,
        ),
        "gy",
        -1,
    )
    warmth_wide = jnp.concatenate([left[:2], warmth_tall, right[:2]], axis=0)
    heat_wide = jnp.concatenate([left[2:, 1:-1], heat_tall, right[2:, 1:-1]], axis=0)
    first = propagate_members_last(warmth_wide, heat_wide)
    col = lax.broadcasted_iota(jnp.int32, (width + 2, height + 2), 0)
    row = lax.broadcasted_iota(jnp.int32, (width + 2, height + 2), 1)
    at_x, at_y = lax.axis_index("gx"), lax.axis_index("gy")
    outside = (
        ((row == 0) & (at_x == 0))
        | ((row == height + 1) & (at_x == lax.axis_size("gx") - 1))
        | ((col == 0) & (at_y == 0))
        | ((col == width + 1) & (at_y == lax.axis_size("gy") - 1))
    )
    first = jnp.where(outside[:, :, None], 0.0, first)
    return propagate_members_last(first, heat)


def shards(
    prior_gas_warmth,
    fire_power_output,
    measured_warmth,
    reading_noise_spread,
    reading_local_location,
):
    sample_number, block_height_number, block_width_number = prior_gas_warmth.shape
    warmth_t = jnp.transpose(prior_gas_warmth, (2, 1, 0))
    heat_t = jnp.transpose(fire_power_output, (2, 1, 0))
    predicted_t = forecast_two_steps(warmth_t, heat_t)
    average_t = jnp.mean(predicted_t, axis=2)
    mean_heat_t = jnp.mean(heat_t, axis=2)
    deviation_t = predicted_t - average_t[:, :, None]
    heat_anomaly_t = heat_t - mean_heat_t[:, :, None]
    coefficient_line = 1.0 / (reading_noise_spread * math.sqrt(sample_number - 1))
    weight_line = coefficient_line * coefficient_line
    row_hot = (
        (reading_local_location // block_width_number)[:, None]
        == lax.broadcasted_iota(jnp.int32, (1, block_height_number), 1)
    ).astype(jnp.float32)
    col_hot = (
        (reading_local_location % block_width_number)[:, None]
        == lax.broadcasted_iota(jnp.int32, (1, block_width_number), 1)
    ).astype(jnp.float32)
    weighted_rows = jnp.concatenate(
        [row_hot * weight_line[:, None], row_hot * (weight_line * measured_warmth)[:, None]],
        axis=1,
    )
    cell_sums = lax.dot_general(
        col_hot, weighted_rows, (((0,), (0,)), ((), ())), precision=lax.Precision.HIGHEST
    )
    cell_weight = cell_sums[:, :block_height_number]
    cell_residual = cell_sums[:, block_height_number:] - average_t * cell_weight
    gram_local = lax.dot_general(
        deviation_t * cell_weight[:, :, None],
        deviation_t,
        (((0, 1), (0, 1)), ((), ())),
        precision=lax.Precision.HIGHEST,
    )
    projected = lax.dot_general(
        deviation_t,
        cell_residual,
        (((0, 1), (0, 1)), ((), ())),
        precision=lax.Precision.HIGHEST,
    )
    identity = jnp.eye(sample_number, dtype=jnp.float32)
    stacked = butterfly_sum(
        jnp.concatenate([gram_local, projected[None, :]], axis=0), ("gx", "gy")
    )
    gram_sum = stacked[:sample_number] + identity
    projected_sum = stacked[sample_number]
    lower_inverse = inverse_factor(gram_sum)
    whitened = jnp.dot(lower_inverse, projected_sum, precision=lax.Precision.HIGHEST)
    mean_weights = jnp.dot(lower_inverse.T, whitened, precision=lax.Precision.HIGHEST)
    combination_transposed = lower_inverse + mean_weights[None, :]
    contract = (((2,), (1,)), ((), ()))
    updated_t = average_t[:, :, None] + lax.dot_general(
        deviation_t, combination_transposed, contract, precision=lax.Precision.HIGHEST
    )
    heat_out_t = mean_heat_t[:, :, None] + lax.dot_general(
        heat_anomaly_t, combination_transposed, contract, precision=lax.Precision.HIGHEST
    )
    return (jnp.transpose(updated_t, (2, 1, 0)), jnp.transpose(heat_out_t, (2, 1, 0)))


def solution(mesh):
    placed = (
        P(None, "gx", "gy"),
        P(None, "gx", "gy"),
        P(("gx", "gy")),
        P(("gx", "gy")),
        P(("gx", "gy")),
    )
    return jax.shard_map(
        shards,
        mesh=mesh,
        in_specs=placed,
        out_specs=(P(None, "gx", "gy"), P(None, "gx", "gy")),
        check_vma=False,
    )
```

```python
import math

import jax
import jax.numpy as jnp
from jax import lax
from jax.experimental import pallas as pl
from jax.experimental.pallas import tpu as pltpu
from jax.sharding import PartitionSpec as P

diffusion = 0.2
heating = 0.5


def xor_tree(received, base, strides):
    if not strides:
        return received[base]
    return xor_tree(received, base, strides[:-1]) + xor_tree(
        received, base ^ strides[-1], strides[:-1]
    )


def butterfly_sum(value, axes):
    for axis in axes:
        count = lax.axis_size(axis)
        if count & (count - 1):
            value = lax.psum(value, axis)
            continue
        bits = [1 << b for b in range(count.bit_length() - 1)]
        for first in range(0, len(bits), 2):
            strides = bits[first : first + 2]
            received = {0: value}
            for mask in range(1, 1 << len(strides)):
                offset = 0
                for position, stride in enumerate(strides):
                    if mask >> position & 1:
                        offset ^= stride
                pairs = [(i, i ^ offset) for i in range(count)]
                received[offset] = lax.ppermute(value, axis, pairs)
            value = xor_tree(received, 0, strides)
    return value


def inverse_factor_kernel(gram_ref, inverse_ref, work_ref):
    size = gram_ref.shape[0]
    work_ref[...] = gram_ref[...]
    square_row = lax.broadcasted_iota(jnp.int32, (size, size), 0)
    square_col = lax.broadcasted_iota(jnp.int32, (size, size), 1)
    inverse_ref[...] = jnp.where(square_row == square_col, 1.0, 0.0).astype(jnp.float32)
    lane = lax.broadcasted_iota(jnp.int32, (1, size), 1)
    for first in range(0, size, 8):
        span = size - first
        sublane = lax.broadcasted_iota(jnp.int32, (span, 1), 0) + first
        band_col = lax.broadcasted_iota(jnp.int32, (span, size), 1)

        def step(k, carry, first=first, sublane=sublane, band_col=band_col):
            row = work_ref[pl.ds(k, 1), :]
            band = work_ref[first:, :]
            column = jnp.sum(jnp.where(band_col == k, band, 0.0), axis=1, keepdims=True)
            pivot = jnp.sum(jnp.where(lane == k, row, 0.0), axis=1, keepdims=True)
            root = jnp.sqrt(pivot)
            factor_row = jnp.where(lane >= k, row / root, 0.0)
            factor_col = jnp.where(sublane >= k, column / root, 0.0)
            work_ref[first:, :] = band - factor_col * factor_row
            inverse_row = inverse_ref[pl.ds(k, 1), :] / root
            below = jnp.where(sublane > k, factor_col, 0.0)
            inverse_ref[first:, :] = inverse_ref[first:, :] - below * inverse_row
            inverse_ref[pl.ds(k, 1), :] = inverse_row
            return carry

        lax.fori_loop(first, min(first + 8, size), step, 0)


def inverse_factor(gram):
    size = gram.shape[0]
    return pl.pallas_call(
        inverse_factor_kernel,
        out_shape=jax.ShapeDtypeStruct((size, size), jnp.float32),
        in_specs=[pl.BlockSpec(memory_space=pltpu.VMEM)],
        out_specs=pl.BlockSpec(memory_space=pltpu.VMEM),
        scratch_shapes=[pltpu.VMEM((size, size), jnp.float32)],
    )(gram)

def propagate_model(padded_field, source_term):
    laplacian = (
        padded_field[:, 2:, 1:-1]
        + padded_field[:, :-2, 1:-1]
        + padded_field[:, 1:-1, 2:]
        + padded_field[:, 1:-1, :-2]
        - 4.0 * padded_field[:, 1:-1, 1:-1]
    )
    return padded_field[:, 1:-1, 1:-1] + diffusion * laplacian + heating * source_term


def propagate_members_last(padded_field, source_term):
    laplacian = (
        padded_field[1:-1, 2:]
        + padded_field[1:-1, :-2]
        + padded_field[2:, 1:-1]
        + padded_field[:-2, 1:-1]
        - 4.0 * padded_field[1:-1, 1:-1]
    )
    return padded_field[1:-1, 1:-1] + diffusion * laplacian + heating * source_term


def from_neighbour(block, axis, step):
    count = lax.axis_size(axis)
    if step > 0:
        pairs = [(i, i + 1) for i in range(count - 1)]
    else:
        pairs = [(i + 1, i) for i in range(count - 1)]
    return lax.ppermute(block, axis, pairs)


def forecast_two_steps(warmth, heat):
    width, height = warmth.shape[0], warmth.shape[1]
    top = from_neighbour(
        jnp.concatenate([warmth[:, -2:], heat[:, -1:]], axis=1), "gx", 1
    )
    bottom = from_neighbour(
        jnp.concatenate([warmth[:, :2], heat[:, :1]], axis=1), "gx", -1
    )
    warmth_tall = jnp.concatenate([top[:, :2], warmth, bottom[:, :2]], axis=1)
    heat_tall = jnp.concatenate([top[:, 2:], heat, bottom[:, 2:]], axis=1)
    edge = jnp.zeros_like(heat_tall[:1, :1])
    left = from_neighbour(
        jnp.concatenate(
            [warmth_tall[-2:], jnp.concatenate([edge, heat_tall[-1:], edge], axis=1)],
            axis=0,
        ),
        "gy",
        1,
    )
    right = from_neighbour(
        jnp.concatenate(
            [warmth_tall[:2], jnp.concatenate([edge, heat_tall[:1], edge], axis=1)],
            axis=0,
        ),
        "gy",
        -1,
    )
    warmth_wide = jnp.concatenate([left[:2], warmth_tall, right[:2]], axis=0)
    heat_wide = jnp.concatenate([left[2:, 1:-1], heat_tall, right[2:, 1:-1]], axis=0)
    first = propagate_members_last(warmth_wide, heat_wide)
    col = lax.broadcasted_iota(jnp.int32, (width + 2, height + 2), 0)
    row = lax.broadcasted_iota(jnp.int32, (width + 2, height + 2), 1)
    at_x, at_y = lax.axis_index("gx"), lax.axis_index("gy")
    outside = (
        ((row == 0) & (at_x == 0))
        | ((row == height + 1) & (at_x == lax.axis_size("gx") - 1))
        | ((col == 0) & (at_y == 0))
        | ((col == width + 1) & (at_y == lax.axis_size("gy") - 1))
    )
    first = jnp.where(outside[:, :, None], 0.0, first)
    return propagate_members_last(first, heat)


def shards(
    prior_gas_warmth,
    fire_power_output,
    measured_warmth,
    reading_noise_spread,
    reading_local_location,
):
    sample_number, block_height_number, block_width_number = prior_gas_warmth.shape
    warmth_t = jnp.transpose(prior_gas_warmth, (2, 1, 0))
    heat_t = jnp.transpose(fire_power_output, (2, 1, 0))
    predicted_t = forecast_two_steps(warmth_t, heat_t)
    average_t = jnp.mean(predicted_t, axis=2)
    mean_heat_t = jnp.mean(heat_t, axis=2)
    deviation_t = predicted_t - average_t[:, :, None]
    heat_anomaly_t = heat_t - mean_heat_t[:, :, None]
    coefficient_line = 1.0 / (reading_noise_spread * math.sqrt(sample_number - 1))
    weight_line = coefficient_line * coefficient_line
    row_hot = (
        (reading_local_location // block_width_number)[:, None]
        == lax.broadcasted_iota(jnp.int32, (1, block_height_number), 1)
    ).astype(jnp.float32)
    col_hot = (
        (reading_local_location % block_width_number)[:, None]
        == lax.broadcasted_iota(jnp.int32, (1, block_width_number), 1)
    ).astype(jnp.float32)
    weighted_rows = jnp.concatenate(
        [row_hot * weight_line[:, None], row_hot * (weight_line * measured_warmth)[:, None]],
        axis=1,
    )
    cell_sums = lax.dot_general(
        col_hot, weighted_rows, (((0,), (0,)), ((), ())), precision=lax.Precision.HIGHEST
    )
    cell_weight = cell_sums[:, :block_height_number]
    cell_residual = cell_sums[:, block_height_number:] - average_t * cell_weight
    gram_local = lax.dot_general(
        deviation_t * cell_weight[:, :, None],
        deviation_t,
        (((0, 1), (0, 1)), ((), ())),
        precision=lax.Precision.HIGHEST,
    )
    projected = lax.dot_general(
        deviation_t,
        cell_residual,
        (((0, 1), (0, 1)), ((), ())),
        precision=lax.Precision.HIGHEST,
    )
    identity = jnp.eye(sample_number, dtype=jnp.float32)
    stacked = butterfly_sum(
        jnp.concatenate([gram_local, projected[None, :]], axis=0), ("gx", "gy")
    )
    gram_sum = stacked[:sample_number] + identity
    projected_sum = stacked[sample_number]
    lower_inverse = inverse_factor(gram_sum)
    whitened = jnp.dot(lower_inverse, projected_sum, precision=lax.Precision.HIGHEST)
    mean_weights = jnp.dot(lower_inverse.T, whitened, precision=lax.Precision.HIGHEST)
    combination_transposed = lower_inverse + mean_weights[None, :]
    contract = (((2,), (1,)), ((), ()))
    updated_t = average_t[:, :, None] + lax.dot_general(
        deviation_t, combination_transposed, contract, precision=lax.Precision.HIGHEST
    )
    heat_out_t = mean_heat_t[:, :, None] + lax.dot_general(
        heat_anomaly_t, combination_transposed, contract, precision=lax.Precision.HIGHEST
    )
    return (jnp.transpose(updated_t, (2, 1, 0)), jnp.transpose(heat_out_t, (2, 1, 0)))


def solution(mesh):
    placed = (
        P(None, "gx", "gy"),
        P(None, "gx", "gy"),
        P(("gx", "gy")),
        P(("gx", "gy")),
        P(("gx", "gy")),
    )
    return jax.shard_map(
        shards,
        mesh=mesh,
        in_specs=placed,
        out_specs=(P(None, "gx", "gy"), P(None, "gx", "gy")),
        check_vma=False,
    )
```

```python
import math

import jax
import jax.numpy as jnp
from jax import lax
from jax.experimental import pallas as pl
from jax.experimental.pallas import tpu as pltpu
from jax.sharding import PartitionSpec as P

diffusion = 0.2
heating = 0.5


def xor_tree(received, base, strides):
    if not strides:
        return received[base]
    return xor_tree(received, base, strides[:-1]) + xor_tree(
        received, base ^ strides[-1], strides[:-1]
    )


def butterfly_sum(value, axes):
    for axis in axes:
        count = lax.axis_size(axis)
        if count & (count - 1):
            value = lax.psum(value, axis)
            continue
        bits = [1 << b for b in range(count.bit_length() - 1)]
        for first in range(0, len(bits), 2):
            strides = bits[first : first + 2]
            received = {0: value}
            for mask in range(1, 1 << len(strides)):
                offset = 0
                for position, stride in enumerate(strides):
                    if mask >> position & 1:
                        offset ^= stride
                pairs = [(i, i ^ offset) for i in range(count)]
                received[offset] = lax.ppermute(value, axis, pairs)
            value = xor_tree(received, 0, strides)
    return value


def combination_kernel(stacked_ref, combination_ref, work_ref, inverse_ref):
    size = stacked_ref.shape[1]
    square_row = lax.broadcasted_iota(jnp.int32, (size, size), 0)
    square_col = lax.broadcasted_iota(jnp.int32, (size, size), 1)
    unit = jnp.where(square_row == square_col, 1.0, 0.0).astype(jnp.float32)
    work_ref[...] = stacked_ref[:size, :] + unit
    inverse_ref[...] = unit
    lane = lax.broadcasted_iota(jnp.int32, (1, size), 1)
    for first in range(0, size, 8):
        span = size - first
        sublane = lax.broadcasted_iota(jnp.int32, (span, 1), 0) + first
        band_col = lax.broadcasted_iota(jnp.int32, (span, size), 1)

        def step(k, carry, first=first, sublane=sublane, band_col=band_col):
            row = work_ref[pl.ds(k, 1), :]
            band = work_ref[first:, :]
            column = jnp.sum(jnp.where(band_col == k, band, 0.0), axis=1, keepdims=True)
            pivot = jnp.sum(jnp.where(lane == k, row, 0.0), axis=1, keepdims=True)
            scale = 1.0 / jnp.sqrt(pivot)
            factor_row = jnp.where(lane >= k, row * scale, 0.0)
            factor_col = jnp.where(sublane >= k, column * scale, 0.0)
            work_ref[first:, :] = band - factor_col * factor_row
            inverse_row = inverse_ref[pl.ds(k, 1), :] * scale
            below = jnp.where(sublane > k, factor_col, 0.0)
            inverse_ref[first:, :] = inverse_ref[first:, :] - below * inverse_row
            inverse_ref[pl.ds(k, 1), :] = inverse_row
            return carry

        lax.fori_loop(first, min(first + 8, size), step, 0)
    lower_inverse = inverse_ref[...]
    projected_row = stacked_ref[size : size + 1, :]
    whitened = jnp.sum(lower_inverse * projected_row, axis=1, keepdims=True)
    mean_weights = jnp.sum(lower_inverse * whitened, axis=0, keepdims=True)
    combination_ref[...] = lower_inverse + mean_weights


def combination_transposed_of(stacked):
    size = stacked.shape[1]
    return pl.pallas_call(
        combination_kernel,
        out_shape=jax.ShapeDtypeStruct((size, size), jnp.float32),
        in_specs=[pl.BlockSpec(memory_space=pltpu.VMEM)],
        out_specs=pl.BlockSpec(memory_space=pltpu.VMEM),
        scratch_shapes=[pltpu.VMEM((size, size), jnp.float32)] * 2,
    )(stacked)

def propagate_model(padded_field, source_term):
    laplacian = (
        padded_field[:, 2:, 1:-1]
        + padded_field[:, :-2, 1:-1]
        + padded_field[:, 1:-1, 2:]
        + padded_field[:, 1:-1, :-2]
        - 4.0 * padded_field[:, 1:-1, 1:-1]
    )
    return padded_field[:, 1:-1, 1:-1] + diffusion * laplacian + heating * source_term


def propagate_members_last(padded_field, source_term):
    laplacian = (
        padded_field[1:-1, 2:]
        + padded_field[1:-1, :-2]
        + padded_field[2:, 1:-1]
        + padded_field[:-2, 1:-1]
        - 4.0 * padded_field[1:-1, 1:-1]
    )
    return padded_field[1:-1, 1:-1] + diffusion * laplacian + heating * source_term


def from_neighbour(block, axis, step):
    count = lax.axis_size(axis)
    if step > 0:
        pairs = [(i, i + 1) for i in range(count - 1)]
    else:
        pairs = [(i + 1, i) for i in range(count - 1)]
    return lax.ppermute(block, axis, pairs)


def forecast_two_steps(warmth, heat):
    width, height = warmth.shape[0], warmth.shape[1]
    top = from_neighbour(
        jnp.concatenate([warmth[:, -2:], heat[:, -1:]], axis=1), "gx", 1
    )
    bottom = from_neighbour(
        jnp.concatenate([warmth[:, :2], heat[:, :1]], axis=1), "gx", -1
    )
    warmth_tall = jnp.concatenate([top[:, :2], warmth, bottom[:, :2]], axis=1)
    heat_tall = jnp.concatenate([top[:, 2:], heat, bottom[:, 2:]], axis=1)
    edge = jnp.zeros_like(heat_tall[:1, :1])
    left = from_neighbour(
        jnp.concatenate(
            [warmth_tall[-2:], jnp.concatenate([edge, heat_tall[-1:], edge], axis=1)],
            axis=0,
        ),
        "gy",
        1,
    )
    right = from_neighbour(
        jnp.concatenate(
            [warmth_tall[:2], jnp.concatenate([edge, heat_tall[:1], edge], axis=1)],
            axis=0,
        ),
        "gy",
        -1,
    )
    warmth_wide = jnp.concatenate([left[:2], warmth_tall, right[:2]], axis=0)
    heat_wide = jnp.concatenate([left[2:, 1:-1], heat_tall, right[2:, 1:-1]], axis=0)
    first = propagate_members_last(warmth_wide, heat_wide)
    col = lax.broadcasted_iota(jnp.int32, (width + 2, height + 2), 0)
    row = lax.broadcasted_iota(jnp.int32, (width + 2, height + 2), 1)
    at_x, at_y = lax.axis_index("gx"), lax.axis_index("gy")
    outside = (
        ((row == 0) & (at_x == 0))
        | ((row == height + 1) & (at_x == lax.axis_size("gx") - 1))
        | ((col == 0) & (at_y == 0))
        | ((col == width + 1) & (at_y == lax.axis_size("gy") - 1))
    )
    first = jnp.where(outside[:, :, None], 0.0, first)
    return propagate_members_last(first, heat)


def shards(
    prior_gas_warmth,
    fire_power_output,
    measured_warmth,
    reading_noise_spread,
    reading_local_location,
):
    sample_number, block_height_number, block_width_number = prior_gas_warmth.shape
    warmth_t = jnp.transpose(prior_gas_warmth, (2, 1, 0))
    heat_t = jnp.transpose(fire_power_output, (2, 1, 0))
    predicted_t = forecast_two_steps(warmth_t, heat_t)
    average_t = jnp.mean(predicted_t, axis=2)
    mean_heat_t = jnp.mean(heat_t, axis=2)
    deviation_t = predicted_t - average_t[:, :, None]
    heat_anomaly_t = heat_t - mean_heat_t[:, :, None]
    coefficient_line = 1.0 / (reading_noise_spread * math.sqrt(sample_number - 1))
    weight_line = coefficient_line * coefficient_line
    row_hot = (
        (reading_local_location // block_width_number)[:, None]
        == lax.broadcasted_iota(jnp.int32, (1, block_height_number), 1)
    ).astype(jnp.float32)
    col_hot = (
        (reading_local_location % block_width_number)[:, None]
        == lax.broadcasted_iota(jnp.int32, (1, block_width_number), 1)
    ).astype(jnp.float32)
    weighted_rows = jnp.concatenate(
        [row_hot * weight_line[:, None], row_hot * (weight_line * measured_warmth)[:, None]],
        axis=1,
    )
    cell_sums = lax.dot_general(
        col_hot, weighted_rows, (((0,), (0,)), ((), ())), precision=lax.Precision.HIGHEST
    )
    cell_weight = cell_sums[:, :block_height_number]
    cell_residual = cell_sums[:, block_height_number:] - average_t * cell_weight
    gram_local = lax.dot_general(
        deviation_t * cell_weight[:, :, None],
        deviation_t,
        (((0, 1), (0, 1)), ((), ())),
        precision=lax.Precision.HIGHEST,
    )
    projected = lax.dot_general(
        deviation_t,
        cell_residual,
        (((0, 1), (0, 1)), ((), ())),
        precision=lax.Precision.HIGHEST,
    )
    combination_transposed = combination_transposed_of(
        butterfly_sum(jnp.concatenate([gram_local, projected[None, :]], axis=0), ("gx", "gy"))
    )
    contract = (((2,), (1,)), ((), ()))
    updated_t = average_t[:, :, None] + lax.dot_general(
        deviation_t, combination_transposed, contract, precision=lax.Precision.HIGHEST
    )
    heat_out_t = mean_heat_t[:, :, None] + lax.dot_general(
        heat_anomaly_t, combination_transposed, contract, precision=lax.Precision.HIGHEST
    )
    return (jnp.transpose(updated_t, (2, 1, 0)), jnp.transpose(heat_out_t, (2, 1, 0)))


def solution(mesh):
    placed = (
        P(None, "gx", "gy"),
        P(None, "gx", "gy"),
        P(("gx", "gy")),
        P(("gx", "gy")),
        P(("gx", "gy")),
    )
    return jax.shard_map(
        shards,
        mesh=mesh,
        in_specs=placed,
        out_specs=(P(None, "gx", "gy"), P(None, "gx", "gy")),
        check_vma=False,
    )
```

```python
import math

import jax
import jax.numpy as jnp
from jax import lax
from jax.experimental import pallas as pl
from jax.experimental.pallas import tpu as pltpu
from jax.sharding import PartitionSpec as P

diffusion = 0.2
heating = 0.5


def xor_tree(received, base, strides):
    if not strides:
        return received[base]
    return xor_tree(received, base, strides[:-1]) + xor_tree(
        received, base ^ strides[-1], strides[:-1]
    )


def butterfly_sum(value, axes):
    for axis in axes:
        count = lax.axis_size(axis)
        if count & (count - 1):
            value = lax.psum(value, axis)
            continue
        bits = [1 << b for b in range(count.bit_length() - 1)]
        for first in range(len(bits)):
            strides = bits[first : first + 1]
            received = {0: value}
            for mask in range(1, 1 << len(strides)):
                offset = 0
                for position, stride in enumerate(strides):
                    if mask >> position & 1:
                        offset ^= stride
                pairs = [(i, i ^ offset) for i in range(count)]
                received[offset] = lax.ppermute(value, axis, pairs)
            value = xor_tree(received, 0, strides)
    return value


def combination_kernel(stacked_ref, combination_ref, work_ref, inverse_ref):
    size = stacked_ref.shape[1]
    square_row = lax.broadcasted_iota(jnp.int32, (size, size), 0)
    square_col = lax.broadcasted_iota(jnp.int32, (size, size), 1)
    unit = jnp.where(square_row == square_col, 1.0, 0.0).astype(jnp.float32)
    work_ref[...] = stacked_ref[:size, :] + unit
    inverse_ref[...] = unit
    lane = lax.broadcasted_iota(jnp.int32, (1, size), 1)
    for first in range(0, size, 8):
        span = size - first
        sublane = lax.broadcasted_iota(jnp.int32, (span, 1), 0) + first
        band_col = lax.broadcasted_iota(jnp.int32, (span, size), 1)

        def step(k, carry, first=first, sublane=sublane, band_col=band_col):
            row = work_ref[pl.ds(k, 1), :]
            band = work_ref[first:, :]
            column = jnp.sum(jnp.where(band_col == k, band, 0.0), axis=1, keepdims=True)
            pivot = jnp.sum(jnp.where(lane == k, row, 0.0), axis=1, keepdims=True)
            scale = 1.0 / jnp.sqrt(pivot)
            factor_row = jnp.where(lane >= k, row * scale, 0.0)
            factor_col = jnp.where(sublane >= k, column * scale, 0.0)
            work_ref[first:, :] = band - factor_col * factor_row
            inverse_row = inverse_ref[pl.ds(k, 1), :] * scale
            below = jnp.where(sublane > k, factor_col, 0.0)
            inverse_ref[first:, :] = inverse_ref[first:, :] - below * inverse_row
            inverse_ref[pl.ds(k, 1), :] = inverse_row
            return carry

        lax.fori_loop(first, min(first + 8, size), step, 0)
    lower_inverse = inverse_ref[...]
    projected_row = stacked_ref[size : size + 1, :]
    whitened = jnp.sum(lower_inverse * projected_row, axis=1, keepdims=True)
    mean_weights = jnp.sum(lower_inverse * whitened, axis=0, keepdims=True)
    combination_ref[...] = lower_inverse + mean_weights


def combination_transposed_of(stacked):
    size = stacked.shape[1]
    return pl.pallas_call(
        combination_kernel,
        out_shape=jax.ShapeDtypeStruct((size, size), jnp.float32),
        in_specs=[pl.BlockSpec(memory_space=pltpu.VMEM)],
        out_specs=pl.BlockSpec(memory_space=pltpu.VMEM),
        scratch_shapes=[pltpu.VMEM((size, size), jnp.float32)] * 2,
    )(stacked)

def propagate_model(padded_field, source_term):
    laplacian = (
        padded_field[:, 2:, 1:-1]
        + padded_field[:, :-2, 1:-1]
        + padded_field[:, 1:-1, 2:]
        + padded_field[:, 1:-1, :-2]
        - 4.0 * padded_field[:, 1:-1, 1:-1]
    )
    return padded_field[:, 1:-1, 1:-1] + diffusion * laplacian + heating * source_term


def propagate_members_last(padded_field, source_term):
    laplacian = (
        padded_field[1:-1, 2:]
        + padded_field[1:-1, :-2]
        + padded_field[2:, 1:-1]
        + padded_field[:-2, 1:-1]
        - 4.0 * padded_field[1:-1, 1:-1]
    )
    return padded_field[1:-1, 1:-1] + diffusion * laplacian + heating * source_term


def from_neighbour(block, axis, step):
    count = lax.axis_size(axis)
    if step > 0:
        pairs = [(i, i + 1) for i in range(count - 1)]
    else:
        pairs = [(i + 1, i) for i in range(count - 1)]
    return lax.ppermute(block, axis, pairs)


def forecast_two_steps(warmth, heat):
    width, height = warmth.shape[0], warmth.shape[1]
    top = from_neighbour(
        jnp.concatenate([warmth[:, -2:], heat[:, -1:]], axis=1), "gx", 1
    )
    bottom = from_neighbour(
        jnp.concatenate([warmth[:, :2], heat[:, :1]], axis=1), "gx", -1
    )
    warmth_tall = jnp.concatenate([top[:, :2], warmth, bottom[:, :2]], axis=1)
    heat_tall = jnp.concatenate([top[:, 2:], heat, bottom[:, 2:]], axis=1)
    edge = jnp.zeros_like(heat_tall[:1, :1])
    left = from_neighbour(
        jnp.concatenate(
            [warmth_tall[-2:], jnp.concatenate([edge, heat_tall[-1:], edge], axis=1)],
            axis=0,
        ),
        "gy",
        1,
    )
    right = from_neighbour(
        jnp.concatenate(
            [warmth_tall[:2], jnp.concatenate([edge, heat_tall[:1], edge], axis=1)],
            axis=0,
        ),
        "gy",
        -1,
    )
    warmth_wide = jnp.concatenate([left[:2], warmth_tall, right[:2]], axis=0)
    heat_wide = jnp.concatenate([left[2:, 1:-1], heat_tall, right[2:, 1:-1]], axis=0)
    first = propagate_members_last(warmth_wide, heat_wide)
    col = lax.broadcasted_iota(jnp.int32, (width + 2, height + 2), 0)
    row = lax.broadcasted_iota(jnp.int32, (width + 2, height + 2), 1)
    at_x, at_y = lax.axis_index("gx"), lax.axis_index("gy")
    outside = (
        ((row == 0) & (at_x == 0))
        | ((row == height + 1) & (at_x == lax.axis_size("gx") - 1))
        | ((col == 0) & (at_y == 0))
        | ((col == width + 1) & (at_y == lax.axis_size("gy") - 1))
    )
    first = jnp.where(outside[:, :, None], 0.0, first)
    return propagate_members_last(first, heat)


def shards(
    prior_gas_warmth,
    fire_power_output,
    measured_warmth,
    reading_noise_spread,
    reading_local_location,
):
    sample_number, block_height_number, block_width_number = prior_gas_warmth.shape
    warmth_t = jnp.transpose(prior_gas_warmth, (2, 1, 0))
    heat_t = jnp.transpose(fire_power_output, (2, 1, 0))
    predicted_t = forecast_two_steps(warmth_t, heat_t)
    average_t = jnp.mean(predicted_t, axis=2)
    mean_heat_t = jnp.mean(heat_t, axis=2)
    deviation_t = predicted_t - average_t[:, :, None]
    heat_anomaly_t = heat_t - mean_heat_t[:, :, None]
    coefficient_line = 1.0 / (reading_noise_spread * math.sqrt(sample_number - 1))
    weight_line = coefficient_line * coefficient_line
    row_hot = (
        (reading_local_location // block_width_number)[:, None]
        == lax.broadcasted_iota(jnp.int32, (1, block_height_number), 1)
    ).astype(jnp.float32)
    col_hot = (
        (reading_local_location % block_width_number)[:, None]
        == lax.broadcasted_iota(jnp.int32, (1, block_width_number), 1)
    ).astype(jnp.float32)
    weighted_rows = jnp.concatenate(
        [row_hot * weight_line[:, None], row_hot * (weight_line * measured_warmth)[:, None]],
        axis=1,
    )
    cell_sums = lax.dot_general(
        col_hot, weighted_rows, (((0,), (0,)), ((), ())), precision=lax.Precision.HIGHEST
    )
    cell_weight = cell_sums[:, :block_height_number]
    cell_residual = cell_sums[:, block_height_number:] - average_t * cell_weight
    gram_local = lax.dot_general(
        deviation_t * cell_weight[:, :, None],
        deviation_t,
        (((0, 1), (0, 1)), ((), ())),
        precision=lax.Precision.HIGHEST,
    )
    projected = lax.dot_general(
        deviation_t,
        cell_residual,
        (((0, 1), (0, 1)), ((), ())),
        precision=lax.Precision.HIGHEST,
    )
    combination_transposed = combination_transposed_of(
        butterfly_sum(jnp.concatenate([gram_local, projected[None, :]], axis=0), ("gx", "gy"))
    )
    contract = (((2,), (1,)), ((), ()))
    updated_t = average_t[:, :, None] + lax.dot_general(
        deviation_t, combination_transposed, contract, precision=lax.Precision.HIGHEST
    )
    heat_out_t = mean_heat_t[:, :, None] + lax.dot_general(
        heat_anomaly_t, combination_transposed, contract, precision=lax.Precision.HIGHEST
    )
    return (jnp.transpose(updated_t, (2, 1, 0)), jnp.transpose(heat_out_t, (2, 1, 0)))


def solution(mesh):
    placed = (
        P(None, "gx", "gy"),
        P(None, "gx", "gy"),
        P(("gx", "gy")),
        P(("gx", "gy")),
        P(("gx", "gy")),
    )
    return jax.shard_map(
        shards,
        mesh=mesh,
        in_specs=placed,
        out_specs=(P(None, "gx", "gy"), P(None, "gx", "gy")),
        check_vma=False,
    )
```

```python
import math

import jax
import jax.numpy as jnp
from jax import lax
from jax.experimental import pallas as pl
from jax.experimental.pallas import tpu as pltpu
from jax.sharding import PartitionSpec as P

diffusion = 0.2
heating = 0.5


def xor_tree(received, base, strides):
    if not strides:
        return received[base]
    return xor_tree(received, base, strides[:-1]) + xor_tree(
        received, base ^ strides[-1], strides[:-1]
    )


def butterfly_sum(value, axes):
    for axis in axes:
        count = lax.axis_size(axis)
        if count & (count - 1):
            value = lax.psum(value, axis)
            continue
        bits = [1 << b for b in range(count.bit_length() - 1)]
        for first in range(len(bits)):
            strides = bits[first : first + 1]
            received = {0: value}
            for mask in range(1, 1 << len(strides)):
                offset = 0
                for position, stride in enumerate(strides):
                    if mask >> position & 1:
                        offset ^= stride
                pairs = [(i, i ^ offset) for i in range(count)]
                received[offset] = lax.ppermute(value, axis, pairs)
            value = xor_tree(received, 0, strides)
    return value


def combination_kernel(stacked_ref, combination_ref, work_ref, inverse_ref):
    size = stacked_ref.shape[1]
    square_row = lax.broadcasted_iota(jnp.int32, (size, size), 0)
    square_col = lax.broadcasted_iota(jnp.int32, (size, size), 1)
    unit = jnp.where(square_row == square_col, 1.0, 0.0).astype(jnp.float32)
    work_ref[...] = stacked_ref[:size, :] + unit
    inverse_ref[...] = unit
    lane = lax.broadcasted_iota(jnp.int32, (1, size), 1)
    for first in range(0, size, 8):
        span = size - first
        sublane = lax.broadcasted_iota(jnp.int32, (span, 1), 0) + first
        band_col = lax.broadcasted_iota(jnp.int32, (span, size), 1)

        def step(k, carry, first=first, sublane=sublane, band_col=band_col):
            row = work_ref[pl.ds(k, 1), :]
            band = work_ref[first:, :]
            column = jnp.sum(jnp.where(band_col == k, band, 0.0), axis=1, keepdims=True)
            pivot = jnp.sum(jnp.where(lane == k, row, 0.0), axis=1, keepdims=True)
            scale = 1.0 / jnp.sqrt(pivot)
            factor_row = jnp.where(lane >= k, row * scale, 0.0)
            factor_col = jnp.where(sublane >= k, column * scale, 0.0)
            work_ref[first:, :] = band - factor_col * factor_row
            inverse_row = inverse_ref[pl.ds(k, 1), :] * scale
            below = jnp.where(sublane > k, factor_col, 0.0)
            inverse_ref[first:, :] = inverse_ref[first:, :] - below * inverse_row
            inverse_ref[pl.ds(k, 1), :] = inverse_row
            return carry

        lax.fori_loop(first, min(first + 8, size), step, 0, unroll=True)
    lower_inverse = inverse_ref[...]
    projected_row = stacked_ref[size : size + 1, :]
    whitened = jnp.sum(lower_inverse * projected_row, axis=1, keepdims=True)
    mean_weights = jnp.sum(lower_inverse * whitened, axis=0, keepdims=True)
    combination_ref[...] = lower_inverse + mean_weights


def combination_transposed_of(stacked):
    size = stacked.shape[1]
    return pl.pallas_call(
        combination_kernel,
        out_shape=jax.ShapeDtypeStruct((size, size), jnp.float32),
        in_specs=[pl.BlockSpec(memory_space=pltpu.VMEM)],
        out_specs=pl.BlockSpec(memory_space=pltpu.VMEM),
        scratch_shapes=[pltpu.VMEM((size, size), jnp.float32)] * 2,
    )(stacked)

def propagate_model(padded_field, source_term):
    laplacian = (
        padded_field[:, 2:, 1:-1]
        + padded_field[:, :-2, 1:-1]
        + padded_field[:, 1:-1, 2:]
        + padded_field[:, 1:-1, :-2]
        - 4.0 * padded_field[:, 1:-1, 1:-1]
    )
    return padded_field[:, 1:-1, 1:-1] + diffusion * laplacian + heating * source_term


def propagate_members_last(padded_field, source_term):
    laplacian = (
        padded_field[1:-1, 2:]
        + padded_field[1:-1, :-2]
        + padded_field[2:, 1:-1]
        + padded_field[:-2, 1:-1]
        - 4.0 * padded_field[1:-1, 1:-1]
    )
    return padded_field[1:-1, 1:-1] + diffusion * laplacian + heating * source_term


def from_neighbour(block, axis, step):
    count = lax.axis_size(axis)
    if step > 0:
        pairs = [(i, i + 1) for i in range(count - 1)]
    else:
        pairs = [(i + 1, i) for i in range(count - 1)]
    return lax.ppermute(block, axis, pairs)


def forecast_two_steps(warmth, heat):
    width, height = warmth.shape[0], warmth.shape[1]
    top = from_neighbour(
        jnp.concatenate([warmth[:, -2:], heat[:, -1:]], axis=1), "gx", 1
    )
    bottom = from_neighbour(
        jnp.concatenate([warmth[:, :2], heat[:, :1]], axis=1), "gx", -1
    )
    warmth_tall = jnp.concatenate([top[:, :2], warmth, bottom[:, :2]], axis=1)
    heat_tall = jnp.concatenate([top[:, 2:], heat, bottom[:, 2:]], axis=1)
    edge = jnp.zeros_like(heat_tall[:1, :1])
    left = from_neighbour(
        jnp.concatenate(
            [warmth_tall[-2:], jnp.concatenate([edge, heat_tall[-1:], edge], axis=1)],
            axis=0,
        ),
        "gy",
        1,
    )
    right = from_neighbour(
        jnp.concatenate(
            [warmth_tall[:2], jnp.concatenate([edge, heat_tall[:1], edge], axis=1)],
            axis=0,
        ),
        "gy",
        -1,
    )
    warmth_wide = jnp.concatenate([left[:2], warmth_tall, right[:2]], axis=0)
    heat_wide = jnp.concatenate([left[2:, 1:-1], heat_tall, right[2:, 1:-1]], axis=0)
    first = propagate_members_last(warmth_wide, heat_wide)
    col = lax.broadcasted_iota(jnp.int32, (width + 2, height + 2), 0)
    row = lax.broadcasted_iota(jnp.int32, (width + 2, height + 2), 1)
    at_x, at_y = lax.axis_index("gx"), lax.axis_index("gy")
    outside = (
        ((row == 0) & (at_x == 0))
        | ((row == height + 1) & (at_x == lax.axis_size("gx") - 1))
        | ((col == 0) & (at_y == 0))
        | ((col == width + 1) & (at_y == lax.axis_size("gy") - 1))
    )
    first = jnp.where(outside[:, :, None], 0.0, first)
    return propagate_members_last(first, heat)


def shards(
    prior_gas_warmth,
    fire_power_output,
    measured_warmth,
    reading_noise_spread,
    reading_local_location,
):
    sample_number, block_height_number, block_width_number = prior_gas_warmth.shape
    warmth_t = jnp.transpose(prior_gas_warmth, (2, 1, 0))
    heat_t = jnp.transpose(fire_power_output, (2, 1, 0))
    predicted_t = forecast_two_steps(warmth_t, heat_t)
    average_t = jnp.mean(predicted_t, axis=2)
    mean_heat_t = jnp.mean(heat_t, axis=2)
    deviation_t = predicted_t - average_t[:, :, None]
    heat_anomaly_t = heat_t - mean_heat_t[:, :, None]
    coefficient_line = 1.0 / (reading_noise_spread * math.sqrt(sample_number - 1))
    weight_line = coefficient_line * coefficient_line
    row_hot = (
        (reading_local_location // block_width_number)[:, None]
        == lax.broadcasted_iota(jnp.int32, (1, block_height_number), 1)
    ).astype(jnp.float32)
    col_hot = (
        (reading_local_location % block_width_number)[:, None]
        == lax.broadcasted_iota(jnp.int32, (1, block_width_number), 1)
    ).astype(jnp.float32)
    weighted_rows = jnp.concatenate(
        [row_hot * weight_line[:, None], row_hot * (weight_line * measured_warmth)[:, None]],
        axis=1,
    )
    cell_sums = lax.dot_general(
        col_hot, weighted_rows, (((0,), (0,)), ((), ())), precision=lax.Precision.HIGHEST
    )
    cell_weight = cell_sums[:, :block_height_number]
    cell_residual = cell_sums[:, block_height_number:] - average_t * cell_weight
    gram_local = lax.dot_general(
        deviation_t * cell_weight[:, :, None],
        deviation_t,
        (((0, 1), (0, 1)), ((), ())),
        precision=lax.Precision.HIGHEST,
    )
    projected = lax.dot_general(
        deviation_t,
        cell_residual,
        (((0, 1), (0, 1)), ((), ())),
        precision=lax.Precision.HIGHEST,
    )
    combination_transposed = combination_transposed_of(
        butterfly_sum(jnp.concatenate([gram_local, projected[None, :]], axis=0), ("gx", "gy"))
    )
    contract = (((2,), (1,)), ((), ()))
    updated_t = average_t[:, :, None] + lax.dot_general(
        deviation_t, combination_transposed, contract, precision=lax.Precision.HIGHEST
    )
    heat_out_t = mean_heat_t[:, :, None] + lax.dot_general(
        heat_anomaly_t, combination_transposed, contract, precision=lax.Precision.HIGHEST
    )
    return (jnp.transpose(updated_t, (2, 1, 0)), jnp.transpose(heat_out_t, (2, 1, 0)))


def solution(mesh):
    placed = (
        P(None, "gx", "gy"),
        P(None, "gx", "gy"),
        P(("gx", "gy")),
        P(("gx", "gy")),
        P(("gx", "gy")),
    )
    return jax.shard_map(
        shards,
        mesh=mesh,
        in_specs=placed,
        out_specs=(P(None, "gx", "gy"), P(None, "gx", "gy")),
        check_vma=False,
    )
```

```python
import math

import jax
import jax.numpy as jnp
from jax import lax
from jax.experimental import pallas as pl
from jax.experimental.pallas import tpu as pltpu
from jax.sharding import PartitionSpec as P

diffusion = 0.2
heating = 0.5


def xor_tree(received, base, strides):
    if not strides:
        return received[base]
    return xor_tree(received, base, strides[:-1]) + xor_tree(
        received, base ^ strides[-1], strides[:-1]
    )


def butterfly_sum(value, axes):
    for axis in axes:
        count = lax.axis_size(axis)
        if count & (count - 1):
            value = lax.psum(value, axis)
            continue
        bits = [1 << b for b in range(count.bit_length() - 1)]
        for first in range(len(bits)):
            strides = bits[first : first + 1]
            received = {0: value}
            for mask in range(1, 1 << len(strides)):
                offset = 0
                for position, stride in enumerate(strides):
                    if mask >> position & 1:
                        offset ^= stride
                pairs = [(i, i ^ offset) for i in range(count)]
                received[offset] = lax.ppermute(value, axis, pairs)
            value = xor_tree(received, 0, strides)
    return value


def combination_kernel(stacked_ref, combination_ref, work_ref, inverse_ref):
    size = stacked_ref.shape[1]
    square_row = lax.broadcasted_iota(jnp.int32, (size, size), 0)
    square_col = lax.broadcasted_iota(jnp.int32, (size, size), 1)
    unit = jnp.where(square_row == square_col, 1.0, 0.0).astype(jnp.float32)
    work_ref[...] = stacked_ref[:size, :] + unit
    inverse_ref[...] = unit
    lane = lax.broadcasted_iota(jnp.int32, (1, size), 1)
    row = work_ref[0:1, :]
    column = jnp.sum(jnp.where(square_col == 0, work_ref[...], 0.0), axis=1, keepdims=True)
    for first in range(0, size, 8):
        span = size - first
        column = column[column.shape[0] - span :]
        sublane = lax.broadcasted_iota(jnp.int32, (span, 1), 0) + first
        band_col = lax.broadcasted_iota(jnp.int32, (span, size), 1)

        def step(k, carry, first=first, sublane=sublane, band_col=band_col):
            row, column = carry
            band = work_ref[first:, :]
            old_next_row = work_ref[pl.ds(jnp.minimum(k + 1, size - 1), 1), :]
            old_next_col = jnp.sum(
                jnp.where(band_col == k + 1, band, 0.0), axis=1, keepdims=True
            )
            pivot = jnp.sum(jnp.where(lane == k, row, 0.0), axis=1, keepdims=True)
            scale = 1.0 / jnp.sqrt(pivot)
            factor_row = jnp.where(lane >= k, row * scale, 0.0)
            factor_col = jnp.where(sublane >= k, column * scale, 0.0)
            work_ref[first:, :] = band - factor_col * factor_row
            inverse_row = inverse_ref[pl.ds(k, 1), :] * scale
            below = jnp.where(sublane > k, factor_col, 0.0)
            inverse_ref[first:, :] = inverse_ref[first:, :] - below * inverse_row
            inverse_ref[pl.ds(k, 1), :] = inverse_row
            col_at_next = jnp.sum(
                jnp.where(sublane == k + 1, factor_col, 0.0), axis=0, keepdims=True
            )
            row_at_next = jnp.sum(
                jnp.where(lane == k + 1, factor_row, 0.0), axis=1, keepdims=True
            )
            return (old_next_row - col_at_next * factor_row, old_next_col - factor_col * row_at_next)

        row, column = lax.fori_loop(first, min(first + 8, size), step, (row, column), unroll=True)
    lower_inverse = inverse_ref[...]
    projected_row = stacked_ref[size : size + 1, :]
    whitened = jnp.sum(lower_inverse * projected_row, axis=1, keepdims=True)
    mean_weights = jnp.sum(lower_inverse * whitened, axis=0, keepdims=True)
    combination_ref[...] = lower_inverse + mean_weights


def combination_transposed_of(stacked):
    size = stacked.shape[1]
    return pl.pallas_call(
        combination_kernel,
        out_shape=jax.ShapeDtypeStruct((size, size), jnp.float32),
        in_specs=[pl.BlockSpec(memory_space=pltpu.VMEM)],
        out_specs=pl.BlockSpec(memory_space=pltpu.VMEM),
        scratch_shapes=[pltpu.VMEM((size, size), jnp.float32)] * 2,
    )(stacked)

def propagate_model(padded_field, source_term):
    laplacian = (
        padded_field[:, 2:, 1:-1]
        + padded_field[:, :-2, 1:-1]
        + padded_field[:, 1:-1, 2:]
        + padded_field[:, 1:-1, :-2]
        - 4.0 * padded_field[:, 1:-1, 1:-1]
    )
    return padded_field[:, 1:-1, 1:-1] + diffusion * laplacian + heating * source_term


def propagate_members_last(padded_field, source_term):
    laplacian = (
        padded_field[1:-1, 2:]
        + padded_field[1:-1, :-2]
        + padded_field[2:, 1:-1]
        + padded_field[:-2, 1:-1]
        - 4.0 * padded_field[1:-1, 1:-1]
    )
    return padded_field[1:-1, 1:-1] + diffusion * laplacian + heating * source_term


def from_neighbour(block, axis, step):
    count = lax.axis_size(axis)
    if step > 0:
        pairs = [(i, i + 1) for i in range(count - 1)]
    else:
        pairs = [(i + 1, i) for i in range(count - 1)]
    return lax.ppermute(block, axis, pairs)


def forecast_two_steps(warmth, heat):
    width, height = warmth.shape[0], warmth.shape[1]
    top = from_neighbour(
        jnp.concatenate([warmth[:, -2:], heat[:, -1:]], axis=1), "gx", 1
    )
    bottom = from_neighbour(
        jnp.concatenate([warmth[:, :2], heat[:, :1]], axis=1), "gx", -1
    )
    warmth_tall = jnp.concatenate([top[:, :2], warmth, bottom[:, :2]], axis=1)
    heat_tall = jnp.concatenate([top[:, 2:], heat, bottom[:, 2:]], axis=1)
    edge = jnp.zeros_like(heat_tall[:1, :1])
    left = from_neighbour(
        jnp.concatenate(
            [warmth_tall[-2:], jnp.concatenate([edge, heat_tall[-1:], edge], axis=1)],
            axis=0,
        ),
        "gy",
        1,
    )
    right = from_neighbour(
        jnp.concatenate(
            [warmth_tall[:2], jnp.concatenate([edge, heat_tall[:1], edge], axis=1)],
            axis=0,
        ),
        "gy",
        -1,
    )
    warmth_wide = jnp.concatenate([left[:2], warmth_tall, right[:2]], axis=0)
    heat_wide = jnp.concatenate([left[2:, 1:-1], heat_tall, right[2:, 1:-1]], axis=0)
    first = propagate_members_last(warmth_wide, heat_wide)
    col = lax.broadcasted_iota(jnp.int32, (width + 2, height + 2), 0)
    row = lax.broadcasted_iota(jnp.int32, (width + 2, height + 2), 1)
    at_x, at_y = lax.axis_index("gx"), lax.axis_index("gy")
    outside = (
        ((row == 0) & (at_x == 0))
        | ((row == height + 1) & (at_x == lax.axis_size("gx") - 1))
        | ((col == 0) & (at_y == 0))
        | ((col == width + 1) & (at_y == lax.axis_size("gy") - 1))
    )
    first = jnp.where(outside[:, :, None], 0.0, first)
    return propagate_members_last(first, heat)


def shards(
    prior_gas_warmth,
    fire_power_output,
    measured_warmth,
    reading_noise_spread,
    reading_local_location,
):
    sample_number, block_height_number, block_width_number = prior_gas_warmth.shape
    warmth_t = jnp.transpose(prior_gas_warmth, (2, 1, 0))
    heat_t = jnp.transpose(fire_power_output, (2, 1, 0))
    predicted_t = forecast_two_steps(warmth_t, heat_t)
    average_t = jnp.mean(predicted_t, axis=2)
    mean_heat_t = jnp.mean(heat_t, axis=2)
    deviation_t = predicted_t - average_t[:, :, None]
    heat_anomaly_t = heat_t - mean_heat_t[:, :, None]
    coefficient_line = 1.0 / (reading_noise_spread * math.sqrt(sample_number - 1))
    weight_line = coefficient_line * coefficient_line
    row_hot = (
        (reading_local_location // block_width_number)[:, None]
        == lax.broadcasted_iota(jnp.int32, (1, block_height_number), 1)
    ).astype(jnp.float32)
    col_hot = (
        (reading_local_location % block_width_number)[:, None]
        == lax.broadcasted_iota(jnp.int32, (1, block_width_number), 1)
    ).astype(jnp.float32)
    weighted_rows = jnp.concatenate(
        [row_hot * weight_line[:, None], row_hot * (weight_line * measured_warmth)[:, None]],
        axis=1,
    )
    cell_sums = lax.dot_general(
        col_hot, weighted_rows, (((0,), (0,)), ((), ())), precision=lax.Precision.HIGHEST
    )
    cell_weight = cell_sums[:, :block_height_number]
    cell_residual = cell_sums[:, block_height_number:] - average_t * cell_weight
    gram_local = lax.dot_general(
        deviation_t * cell_weight[:, :, None],
        deviation_t,
        (((0, 1), (0, 1)), ((), ())),
        precision=lax.Precision.HIGHEST,
    )
    projected = lax.dot_general(
        deviation_t,
        cell_residual,
        (((0, 1), (0, 1)), ((), ())),
        precision=lax.Precision.HIGHEST,
    )
    combination_transposed = combination_transposed_of(
        butterfly_sum(jnp.concatenate([gram_local, projected[None, :]], axis=0), ("gx", "gy"))
    )
    contract = (((2,), (1,)), ((), ()))
    updated_t = average_t[:, :, None] + lax.dot_general(
        deviation_t, combination_transposed, contract, precision=lax.Precision.HIGHEST
    )
    heat_out_t = mean_heat_t[:, :, None] + lax.dot_general(
        heat_anomaly_t, combination_transposed, contract, precision=lax.Precision.HIGHEST
    )
    return (jnp.transpose(updated_t, (2, 1, 0)), jnp.transpose(heat_out_t, (2, 1, 0)))


def solution(mesh):
    placed = (
        P(None, "gx", "gy"),
        P(None, "gx", "gy"),
        P(("gx", "gy")),
        P(("gx", "gy")),
        P(("gx", "gy")),
    )
    return jax.shard_map(
        shards,
        mesh=mesh,
        in_specs=placed,
        out_specs=(P(None, "gx", "gy"), P(None, "gx", "gy")),
        check_vma=False,
    )
```

```python
import math

import jax
import jax.numpy as jnp
from jax import lax
from jax.experimental import pallas as pl
from jax.experimental.pallas import tpu as pltpu
from jax.sharding import PartitionSpec as P

diffusion = 0.2
heating = 0.5


def xor_tree(received, base, strides):
    if not strides:
        return received[base]
    return xor_tree(received, base, strides[:-1]) + xor_tree(
        received, base ^ strides[-1], strides[:-1]
    )


def butterfly_sum(value, axes):
    for axis in axes:
        count = lax.axis_size(axis)
        if count & (count - 1):
            value = lax.psum(value, axis)
            continue
        bits = [1 << b for b in range(count.bit_length() - 1)]
        for first in range(len(bits)):
            strides = bits[first : first + 1]
            received = {0: value}
            for mask in range(1, 1 << len(strides)):
                offset = 0
                for position, stride in enumerate(strides):
                    if mask >> position & 1:
                        offset ^= stride
                pairs = [(i, i ^ offset) for i in range(count)]
                received[offset] = lax.ppermute(value, axis, pairs)
            value = xor_tree(received, 0, strides)
    return value


def combination_kernel(stacked_ref, combination_ref, work_ref, inverse_ref):
    size = stacked_ref.shape[1]
    square_row = lax.broadcasted_iota(jnp.int32, (size, size), 0)
    square_col = lax.broadcasted_iota(jnp.int32, (size, size), 1)
    unit = jnp.where(square_row == square_col, 1.0, 0.0).astype(jnp.float32)
    work_ref[...] = stacked_ref[:size, :] + unit
    inverse_ref[...] = unit
    lane = lax.broadcasted_iota(jnp.int32, (1, size), 1)
    for first in range(0, size, 8):
        span = size - first
        sublane = lax.broadcasted_iota(jnp.int32, (span, 1), 0) + first

        def step(k, carry, first=first, sublane=sublane):
            row = work_ref[pl.ds(k, 1), :]
            pivot = jnp.sum(jnp.where(lane == k, row, 0.0), axis=1, keepdims=True)
            scale = 1.0 / jnp.sqrt(pivot)
            factor_row = jnp.where(lane >= k, row * scale, 0.0)
            factor_col = jnp.transpose(jnp.broadcast_to(factor_row, (8, size)))[first:, :1]
            work_ref[first:, :] = work_ref[first:, :] - factor_col * factor_row
            inverse_row = inverse_ref[pl.ds(k, 1), :] * scale
            below = jnp.where(sublane > k, factor_col, 0.0)
            inverse_ref[first:, :] = inverse_ref[first:, :] - below * inverse_row
            inverse_ref[pl.ds(k, 1), :] = inverse_row
            return carry

        lax.fori_loop(first, min(first + 8, size), step, 0)
    lower_inverse = inverse_ref[...]
    projected_row = stacked_ref[size : size + 1, :]
    whitened = jnp.sum(lower_inverse * projected_row, axis=1, keepdims=True)
    mean_weights = jnp.sum(lower_inverse * whitened, axis=0, keepdims=True)
    combination_ref[...] = lower_inverse + mean_weights


def combination_transposed_of(stacked):
    size = stacked.shape[1]
    return pl.pallas_call(
        combination_kernel,
        out_shape=jax.ShapeDtypeStruct((size, size), jnp.float32),
        in_specs=[pl.BlockSpec(memory_space=pltpu.VMEM)],
        out_specs=pl.BlockSpec(memory_space=pltpu.VMEM),
        scratch_shapes=[pltpu.VMEM((size, size), jnp.float32)] * 2,
    )(stacked)

def propagate_model(padded_field, source_term):
    laplacian = (
        padded_field[:, 2:, 1:-1]
        + padded_field[:, :-2, 1:-1]
        + padded_field[:, 1:-1, 2:]
        + padded_field[:, 1:-1, :-2]
        - 4.0 * padded_field[:, 1:-1, 1:-1]
    )
    return padded_field[:, 1:-1, 1:-1] + diffusion * laplacian + heating * source_term


def propagate_members_last(padded_field, source_term):
    laplacian = (
        padded_field[1:-1, 2:]
        + padded_field[1:-1, :-2]
        + padded_field[2:, 1:-1]
        + padded_field[:-2, 1:-1]
        - 4.0 * padded_field[1:-1, 1:-1]
    )
    return padded_field[1:-1, 1:-1] + diffusion * laplacian + heating * source_term


def from_neighbour(block, axis, step):
    count = lax.axis_size(axis)
    if step > 0:
        pairs = [(i, i + 1) for i in range(count - 1)]
    else:
        pairs = [(i + 1, i) for i in range(count - 1)]
    return lax.ppermute(block, axis, pairs)


def forecast_two_steps(warmth, heat):
    width, height = warmth.shape[0], warmth.shape[1]
    top = from_neighbour(
        jnp.concatenate([warmth[:, -2:], heat[:, -1:]], axis=1), "gx", 1
    )
    bottom = from_neighbour(
        jnp.concatenate([warmth[:, :2], heat[:, :1]], axis=1), "gx", -1
    )
    warmth_tall = jnp.concatenate([top[:, :2], warmth, bottom[:, :2]], axis=1)
    heat_tall = jnp.concatenate([top[:, 2:], heat, bottom[:, 2:]], axis=1)
    edge = jnp.zeros_like(heat_tall[:1, :1])
    left = from_neighbour(
        jnp.concatenate(
            [warmth_tall[-2:], jnp.concatenate([edge, heat_tall[-1:], edge], axis=1)],
            axis=0,
        ),
        "gy",
        1,
    )
    right = from_neighbour(
        jnp.concatenate(
            [warmth_tall[:2], jnp.concatenate([edge, heat_tall[:1], edge], axis=1)],
            axis=0,
        ),
        "gy",
        -1,
    )
    warmth_wide = jnp.concatenate([left[:2], warmth_tall, right[:2]], axis=0)
    heat_wide = jnp.concatenate([left[2:, 1:-1], heat_tall, right[2:, 1:-1]], axis=0)
    first = propagate_members_last(warmth_wide, heat_wide)
    col = lax.broadcasted_iota(jnp.int32, (width + 2, height + 2), 0)
    row = lax.broadcasted_iota(jnp.int32, (width + 2, height + 2), 1)
    at_x, at_y = lax.axis_index("gx"), lax.axis_index("gy")
    outside = (
        ((row == 0) & (at_x == 0))
        | ((row == height + 1) & (at_x == lax.axis_size("gx") - 1))
        | ((col == 0) & (at_y == 0))
        | ((col == width + 1) & (at_y == lax.axis_size("gy") - 1))
    )
    first = jnp.where(outside[:, :, None], 0.0, first)
    return propagate_members_last(first, heat)


def shards(
    prior_gas_warmth,
    fire_power_output,
    measured_warmth,
    reading_noise_spread,
    reading_local_location,
):
    sample_number, block_height_number, block_width_number = prior_gas_warmth.shape
    warmth_t = jnp.transpose(prior_gas_warmth, (2, 1, 0))
    heat_t = jnp.transpose(fire_power_output, (2, 1, 0))
    predicted_t = forecast_two_steps(warmth_t, heat_t)
    average_t = jnp.mean(predicted_t, axis=2)
    mean_heat_t = jnp.mean(heat_t, axis=2)
    deviation_t = predicted_t - average_t[:, :, None]
    heat_anomaly_t = heat_t - mean_heat_t[:, :, None]
    coefficient_line = 1.0 / (reading_noise_spread * math.sqrt(sample_number - 1))
    weight_line = coefficient_line * coefficient_line
    row_hot = (
        (reading_local_location // block_width_number)[:, None]
        == lax.broadcasted_iota(jnp.int32, (1, block_height_number), 1)
    ).astype(jnp.float32)
    col_hot = (
        (reading_local_location % block_width_number)[:, None]
        == lax.broadcasted_iota(jnp.int32, (1, block_width_number), 1)
    ).astype(jnp.float32)
    weighted_rows = jnp.concatenate(
        [row_hot * weight_line[:, None], row_hot * (weight_line * measured_warmth)[:, None]],
        axis=1,
    )
    cell_sums = lax.dot_general(
        col_hot, weighted_rows, (((0,), (0,)), ((), ())), precision=lax.Precision.HIGHEST
    )
    cell_weight = cell_sums[:, :block_height_number]
    cell_residual = cell_sums[:, block_height_number:] - average_t * cell_weight
    gram_local = lax.dot_general(
        deviation_t * cell_weight[:, :, None],
        deviation_t,
        (((0, 1), (0, 1)), ((), ())),
        precision=lax.Precision.HIGHEST,
    )
    projected = lax.dot_general(
        deviation_t,
        cell_residual,
        (((0, 1), (0, 1)), ((), ())),
        precision=lax.Precision.HIGHEST,
    )
    combination_transposed = combination_transposed_of(
        butterfly_sum(jnp.concatenate([gram_local, projected[None, :]], axis=0), ("gx", "gy"))
    )
    contract = (((2,), (1,)), ((), ()))
    updated_t = average_t[:, :, None] + lax.dot_general(
        deviation_t, combination_transposed, contract, precision=lax.Precision.HIGHEST
    )
    heat_out_t = mean_heat_t[:, :, None] + lax.dot_general(
        heat_anomaly_t, combination_transposed, contract, precision=lax.Precision.HIGHEST
    )
    return (jnp.transpose(updated_t, (2, 1, 0)), jnp.transpose(heat_out_t, (2, 1, 0)))


def solution(mesh):
    placed = (
        P(None, "gx", "gy"),
        P(None, "gx", "gy"),
        P(("gx", "gy")),
        P(("gx", "gy")),
        P(("gx", "gy")),
    )
    return jax.shard_map(
        shards,
        mesh=mesh,
        in_specs=placed,
        out_specs=(P(None, "gx", "gy"), P(None, "gx", "gy")),
        check_vma=False,
    )
```

```python
import math

import jax
import jax.numpy as jnp
from jax import lax
from jax.experimental import pallas as pl
from jax.experimental.pallas import tpu as pltpu
from jax.sharding import PartitionSpec as P

diffusion = 0.2
heating = 0.5


def xor_tree(received, base, strides):
    if not strides:
        return received[base]
    return xor_tree(received, base, strides[:-1]) + xor_tree(
        received, base ^ strides[-1], strides[:-1]
    )


def butterfly_sum(value, axes):
    for axis in axes:
        count = lax.axis_size(axis)
        if count & (count - 1):
            value = lax.psum(value, axis)
            continue
        bits = [1 << b for b in range(count.bit_length() - 1)]
        for first in range(len(bits)):
            strides = bits[first : first + 1]
            received = {0: value}
            for mask in range(1, 1 << len(strides)):
                offset = 0
                for position, stride in enumerate(strides):
                    if mask >> position & 1:
                        offset ^= stride
                pairs = [(i, i ^ offset) for i in range(count)]
                received[offset] = lax.ppermute(value, axis, pairs)
            value = xor_tree(received, 0, strides)
    return value


def combination_kernel(stacked_ref, combination_ref, work_ref, inverse_ref):
    size = stacked_ref.shape[1]
    square_row = lax.broadcasted_iota(jnp.int32, (size, size), 0)
    square_col = lax.broadcasted_iota(jnp.int32, (size, size), 1)
    unit = jnp.where(square_row == square_col, 1.0, 0.0).astype(jnp.float32)
    work_ref[...] = stacked_ref[:size, :] + unit
    inverse_ref[...] = unit
    lane = lax.broadcasted_iota(jnp.int32, (1, size), 1)
    for first in range(0, size, 8):
        span = size - first
        sublane = lax.broadcasted_iota(jnp.int32, (span, 1), 0) + first
        band_col = lax.broadcasted_iota(jnp.int32, (span, size), 1)

        def step(k, carry, first=first, sublane=sublane, band_col=band_col):
            row = work_ref[pl.ds(k, 1), :]
            band = work_ref[first:, :]
            column = jnp.sum(jnp.where(band_col == k, band, 0.0), axis=1, keepdims=True)
            pivot = jnp.sum(jnp.where(lane == k, row, 0.0), axis=1, keepdims=True)
            scale = 1.0 / jnp.sqrt(pivot)
            factor_row = jnp.where(lane >= k, row * scale, 0.0)
            factor_col = jnp.where(sublane >= k, column * scale, 0.0)
            work_ref[first:, :] = band - factor_col * factor_row
            inverse_row = inverse_ref[pl.ds(k, 1), :] * scale
            below = jnp.where(sublane > k, factor_col, 0.0)
            inverse_ref[first:, :] = inverse_ref[first:, :] - below * inverse_row
            inverse_ref[pl.ds(k, 1), :] = inverse_row
            return carry

        lax.fori_loop(first, min(first + 8, size), step, 0, unroll=True)
    lower_inverse = inverse_ref[...]
    projected_row = stacked_ref[size : size + 1, :]
    whitened = jnp.sum(lower_inverse * projected_row, axis=1, keepdims=True)
    mean_weights = jnp.sum(lower_inverse * whitened, axis=0, keepdims=True)
    combination_ref[...] = lower_inverse + mean_weights


def combination_transposed_of(stacked):
    size = stacked.shape[1]
    return pl.pallas_call(
        combination_kernel,
        out_shape=jax.ShapeDtypeStruct((size, size), jnp.float32),
        in_specs=[pl.BlockSpec(memory_space=pltpu.VMEM)],
        out_specs=pl.BlockSpec(memory_space=pltpu.VMEM),
        scratch_shapes=[pltpu.VMEM((size, size), jnp.float32)] * 2,
    )(stacked)

def propagate_model(padded_field, source_term):
    laplacian = (
        padded_field[:, 2:, 1:-1]
        + padded_field[:, :-2, 1:-1]
        + padded_field[:, 1:-1, 2:]
        + padded_field[:, 1:-1, :-2]
        - 4.0 * padded_field[:, 1:-1, 1:-1]
    )
    return padded_field[:, 1:-1, 1:-1] + diffusion * laplacian + heating * source_term


def propagate_members_last(padded_field, source_term):
    laplacian = (
        padded_field[1:-1, 2:]
        + padded_field[1:-1, :-2]
        + padded_field[2:, 1:-1]
        + padded_field[:-2, 1:-1]
        - 4.0 * padded_field[1:-1, 1:-1]
    )
    return padded_field[1:-1, 1:-1] + diffusion * laplacian + heating * source_term


def from_neighbour(block, axis, step):
    count = lax.axis_size(axis)
    if step > 0:
        pairs = [(i, i + 1) for i in range(count - 1)]
    else:
        pairs = [(i + 1, i) for i in range(count - 1)]
    return lax.ppermute(block, axis, pairs)


def forecast_two_steps(warmth, heat):
    width, height = warmth.shape[0], warmth.shape[1]
    top = from_neighbour(
        jnp.concatenate([warmth[:, -2:], heat[:, -1:]], axis=1), "gx", 1
    )
    bottom = from_neighbour(
        jnp.concatenate([warmth[:, :2], heat[:, :1]], axis=1), "gx", -1
    )
    warmth_tall = jnp.concatenate([top[:, :2], warmth, bottom[:, :2]], axis=1)
    heat_tall = jnp.concatenate([top[:, 2:], heat, bottom[:, 2:]], axis=1)
    edge = jnp.zeros_like(heat_tall[:1, :1])
    left = from_neighbour(
        jnp.concatenate(
            [warmth_tall[-2:], jnp.concatenate([edge, heat_tall[-1:], edge], axis=1)],
            axis=0,
        ),
        "gy",
        1,
    )
    right = from_neighbour(
        jnp.concatenate(
            [warmth_tall[:2], jnp.concatenate([edge, heat_tall[:1], edge], axis=1)],
            axis=0,
        ),
        "gy",
        -1,
    )
    warmth_wide = jnp.concatenate([left[:2], warmth_tall, right[:2]], axis=0)
    heat_wide = jnp.concatenate([left[2:, 1:-1], heat_tall, right[2:, 1:-1]], axis=0)
    first = propagate_members_last(warmth_wide, heat_wide)
    col = lax.broadcasted_iota(jnp.int32, (width + 2, height + 2), 0)
    row = lax.broadcasted_iota(jnp.int32, (width + 2, height + 2), 1)
    at_x, at_y = lax.axis_index("gx"), lax.axis_index("gy")
    outside = (
        ((row == 0) & (at_x == 0))
        | ((row == height + 1) & (at_x == lax.axis_size("gx") - 1))
        | ((col == 0) & (at_y == 0))
        | ((col == width + 1) & (at_y == lax.axis_size("gy") - 1))
    )
    first = jnp.where(outside[:, :, None], 0.0, first)
    return propagate_members_last(first, heat)


def shards(
    prior_gas_warmth,
    fire_power_output,
    measured_warmth,
    reading_noise_spread,
    reading_local_location,
):
    sample_number, block_height_number, block_width_number = prior_gas_warmth.shape
    warmth_t = jnp.transpose(prior_gas_warmth, (2, 1, 0))
    heat_t = jnp.transpose(fire_power_output, (2, 1, 0))
    predicted_t = forecast_two_steps(warmth_t, heat_t)
    average_t = jnp.mean(predicted_t, axis=2)
    mean_heat_t = jnp.mean(heat_t, axis=2)
    deviation_t = predicted_t - average_t[:, :, None]
    heat_anomaly_t = heat_t - mean_heat_t[:, :, None]
    coefficient_line = 1.0 / (reading_noise_spread * math.sqrt(sample_number - 1))
    weight_line = coefficient_line * coefficient_line
    row_hot = (
        (reading_local_location // block_width_number)[:, None]
        == lax.broadcasted_iota(jnp.int32, (1, block_height_number), 1)
    ).astype(jnp.float32)
    col_hot = (
        (reading_local_location % block_width_number)[:, None]
        == lax.broadcasted_iota(jnp.int32, (1, block_width_number), 1)
    ).astype(jnp.float32)
    weighted_rows = jnp.concatenate(
        [row_hot * weight_line[:, None], row_hot * (weight_line * measured_warmth)[:, None]],
        axis=1,
    )
    cell_sums = lax.dot_general(
        col_hot, weighted_rows, (((0,), (0,)), ((), ())), precision=lax.Precision.HIGHEST
    )
    cell_weight = cell_sums[:, :block_height_number]
    cell_residual = cell_sums[:, block_height_number:] - average_t * cell_weight
    gram_local = lax.dot_general(
        deviation_t * cell_weight[:, :, None],
        deviation_t,
        (((0, 1), (0, 1)), ((), ())),
        precision=lax.Precision.HIGHEST,
    )
    projected = lax.dot_general(
        deviation_t,
        cell_residual,
        (((0, 1), (0, 1)), ((), ())),
        precision=lax.Precision.HIGHEST,
    )
    combination_transposed = combination_transposed_of(
        butterfly_sum(jnp.concatenate([gram_local, projected[None, :]], axis=0), ("gx", "gy"))
    )
    contract = (((2,), (1,)), ((), ()))
    updated_t = average_t[:, :, None] + lax.dot_general(
        deviation_t, combination_transposed, contract, precision=lax.Precision.HIGH
    )
    heat_out_t = mean_heat_t[:, :, None] + lax.dot_general(
        heat_anomaly_t, combination_transposed, contract, precision=lax.Precision.HIGH
    )
    return (jnp.transpose(updated_t, (2, 1, 0)), jnp.transpose(heat_out_t, (2, 1, 0)))


def solution(mesh):
    placed = (
        P(None, "gx", "gy"),
        P(None, "gx", "gy"),
        P(("gx", "gy")),
        P(("gx", "gy")),
        P(("gx", "gy")),
    )
    return jax.shard_map(
        shards,
        mesh=mesh,
        in_specs=placed,
        out_specs=(P(None, "gx", "gy"), P(None, "gx", "gy")),
        check_vma=False,
    )
```

```python
import math

import jax
import jax.numpy as jnp
from jax import lax
from jax.experimental import pallas as pl
from jax.experimental.pallas import tpu as pltpu
from jax.sharding import PartitionSpec as P

diffusion = 0.2
heating = 0.5


def xor_tree(received, base, strides):
    if not strides:
        return received[base]
    return xor_tree(received, base, strides[:-1]) + xor_tree(
        received, base ^ strides[-1], strides[:-1]
    )


def butterfly_sum(value, axes):
    for axis in axes:
        count = lax.axis_size(axis)
        if count & (count - 1):
            value = lax.psum(value, axis)
            continue
        bits = [1 << b for b in range(count.bit_length() - 1)]
        for first in range(len(bits)):
            strides = bits[first : first + 1]
            received = {0: value}
            for mask in range(1, 1 << len(strides)):
                offset = 0
                for position, stride in enumerate(strides):
                    if mask >> position & 1:
                        offset ^= stride
                pairs = [(i, i ^ offset) for i in range(count)]
                received[offset] = lax.ppermute(value, axis, pairs)
            value = xor_tree(received, 0, strides)
    return value


def combination_kernel(stacked_ref, combination_ref, work_ref, inverse_ref):
    size = stacked_ref.shape[1]
    square_row = lax.broadcasted_iota(jnp.int32, (size, size), 0)
    square_col = lax.broadcasted_iota(jnp.int32, (size, size), 1)
    unit = jnp.where(square_row == square_col, 1.0, 0.0).astype(jnp.float32)
    work_ref[...] = stacked_ref[:size, :] + unit
    inverse_ref[...] = unit
    lane = lax.broadcasted_iota(jnp.int32, (1, size), 1)

    def pick(vector, where_true, axis):
        return jnp.sum(jnp.where(where_true, vector, 0.0), axis=axis, keepdims=True)

    for first in range(0, size, 8):
        span = size - first
        sublane = lax.broadcasted_iota(jnp.int32, (span, 1), 0) + first
        band_col = lax.broadcasted_iota(jnp.int32, (span, size), 1)

        def step(pair, carry, first=first, sublane=sublane, band_col=band_col):
            k = 2 * pair
            row0 = work_ref[pl.ds(k, 1), :]
            row1 = work_ref[pl.ds(k + 1, 1), :]
            band = work_ref[first:, :]
            col0 = pick(band, band_col == k, 1)
            col1 = pick(band, band_col == k + 1, 1)
            scale0 = 1.0 / jnp.sqrt(pick(row0, lane == k, 1))
            coupling = pick(row0, lane == k + 1, 1) * scale0
            scale1 = 1.0 / jnp.sqrt(pick(row1, lane == k + 1, 1) - coupling * coupling)
            factor_row0 = jnp.where(lane >= k, row0 * scale0, 0.0)
            factor_row1 = jnp.where(lane >= k + 1, (row1 - coupling * factor_row0) * scale1, 0.0)
            factor_col0 = jnp.where(sublane >= k, col0 * scale0, 0.0)
            factor_col1 = jnp.where(
                sublane >= k + 1, (col1 - factor_col0 * coupling) * scale1, 0.0
            )
            work_ref[first:, :] = band - factor_col0 * factor_row0 - factor_col1 * factor_row1
            inverse_row0 = inverse_ref[pl.ds(k, 1), :] * scale0
            inverse_row1 = (inverse_ref[pl.ds(k + 1, 1), :] - coupling * inverse_row0) * scale1
            below0 = jnp.where(sublane > k + 1, factor_col0, 0.0)
            below1 = jnp.where(sublane > k + 1, factor_col1, 0.0)
            inverse_ref[first:, :] = (
                inverse_ref[first:, :] - below0 * inverse_row0 - below1 * inverse_row1
            )
            inverse_ref[pl.ds(k, 1), :] = inverse_row0
            inverse_ref[pl.ds(k + 1, 1), :] = inverse_row1
            return carry

        lax.fori_loop(first // 2, min(first + 8, size) // 2, step, 0)
    lower_inverse = inverse_ref[...]
    projected_row = stacked_ref[size : size + 1, :]
    whitened = jnp.sum(lower_inverse * projected_row, axis=1, keepdims=True)
    mean_weights = jnp.sum(lower_inverse * whitened, axis=0, keepdims=True)
    combination_ref[...] = lower_inverse + mean_weights


def combination_transposed_of(stacked):
    size = stacked.shape[1]
    return pl.pallas_call(
        combination_kernel,
        out_shape=jax.ShapeDtypeStruct((size, size), jnp.float32),
        in_specs=[pl.BlockSpec(memory_space=pltpu.VMEM)],
        out_specs=pl.BlockSpec(memory_space=pltpu.VMEM),
        scratch_shapes=[pltpu.VMEM((size, size), jnp.float32)] * 2,
    )(stacked)

def propagate_model(padded_field, source_term):
    laplacian = (
        padded_field[:, 2:, 1:-1]
        + padded_field[:, :-2, 1:-1]
        + padded_field[:, 1:-1, 2:]
        + padded_field[:, 1:-1, :-2]
        - 4.0 * padded_field[:, 1:-1, 1:-1]
    )
    return padded_field[:, 1:-1, 1:-1] + diffusion * laplacian + heating * source_term


def propagate_members_last(padded_field, source_term):
    laplacian = (
        padded_field[1:-1, 2:]
        + padded_field[1:-1, :-2]
        + padded_field[2:, 1:-1]
        + padded_field[:-2, 1:-1]
        - 4.0 * padded_field[1:-1, 1:-1]
    )
    return padded_field[1:-1, 1:-1] + diffusion * laplacian + heating * source_term


def from_neighbour(block, axis, step):
    count = lax.axis_size(axis)
    if step > 0:
        pairs = [(i, i + 1) for i in range(count - 1)]
    else:
        pairs = [(i + 1, i) for i in range(count - 1)]
    return lax.ppermute(block, axis, pairs)


def forecast_two_steps(warmth, heat):
    width, height = warmth.shape[0], warmth.shape[1]
    top = from_neighbour(
        jnp.concatenate([warmth[:, -2:], heat[:, -1:]], axis=1), "gx", 1
    )
    bottom = from_neighbour(
        jnp.concatenate([warmth[:, :2], heat[:, :1]], axis=1), "gx", -1
    )
    warmth_tall = jnp.concatenate([top[:, :2], warmth, bottom[:, :2]], axis=1)
    heat_tall = jnp.concatenate([top[:, 2:], heat, bottom[:, 2:]], axis=1)
    edge = jnp.zeros_like(heat_tall[:1, :1])
    left = from_neighbour(
        jnp.concatenate(
            [warmth_tall[-2:], jnp.concatenate([edge, heat_tall[-1:], edge], axis=1)],
            axis=0,
        ),
        "gy",
        1,
    )
    right = from_neighbour(
        jnp.concatenate(
            [warmth_tall[:2], jnp.concatenate([edge, heat_tall[:1], edge], axis=1)],
            axis=0,
        ),
        "gy",
        -1,
    )
    warmth_wide = jnp.concatenate([left[:2], warmth_tall, right[:2]], axis=0)
    heat_wide = jnp.concatenate([left[2:, 1:-1], heat_tall, right[2:, 1:-1]], axis=0)
    first = propagate_members_last(warmth_wide, heat_wide)
    col = lax.broadcasted_iota(jnp.int32, (width + 2, height + 2), 0)
    row = lax.broadcasted_iota(jnp.int32, (width + 2, height + 2), 1)
    at_x, at_y = lax.axis_index("gx"), lax.axis_index("gy")
    outside = (
        ((row == 0) & (at_x == 0))
        | ((row == height + 1) & (at_x == lax.axis_size("gx") - 1))
        | ((col == 0) & (at_y == 0))
        | ((col == width + 1) & (at_y == lax.axis_size("gy") - 1))
    )
    first = jnp.where(outside[:, :, None], 0.0, first)
    return propagate_members_last(first, heat)


def shards(
    prior_gas_warmth,
    fire_power_output,
    measured_warmth,
    reading_noise_spread,
    reading_local_location,
):
    sample_number, block_height_number, block_width_number = prior_gas_warmth.shape
    warmth_t = jnp.transpose(prior_gas_warmth, (2, 1, 0))
    heat_t = jnp.transpose(fire_power_output, (2, 1, 0))
    predicted_t = forecast_two_steps(warmth_t, heat_t)
    average_t = jnp.mean(predicted_t, axis=2)
    mean_heat_t = jnp.mean(heat_t, axis=2)
    deviation_t = predicted_t - average_t[:, :, None]
    heat_anomaly_t = heat_t - mean_heat_t[:, :, None]
    coefficient_line = 1.0 / (reading_noise_spread * math.sqrt(sample_number - 1))
    weight_line = coefficient_line * coefficient_line
    row_hot = (
        (reading_local_location // block_width_number)[:, None]
        == lax.broadcasted_iota(jnp.int32, (1, block_height_number), 1)
    ).astype(jnp.float32)
    col_hot = (
        (reading_local_location % block_width_number)[:, None]
        == lax.broadcasted_iota(jnp.int32, (1, block_width_number), 1)
    ).astype(jnp.float32)
    weighted_rows = jnp.concatenate(
        [row_hot * weight_line[:, None], row_hot * (weight_line * measured_warmth)[:, None]],
        axis=1,
    )
    cell_sums = lax.dot_general(
        col_hot, weighted_rows, (((0,), (0,)), ((), ())), precision=lax.Precision.HIGHEST
    )
    cell_weight = cell_sums[:, :block_height_number]
    cell_residual = cell_sums[:, block_height_number:] - average_t * cell_weight
    gram_local = lax.dot_general(
        deviation_t * cell_weight[:, :, None],
        deviation_t,
        (((0, 1), (0, 1)), ((), ())),
        precision=lax.Precision.HIGHEST,
    )
    projected = lax.dot_general(
        deviation_t,
        cell_residual,
        (((0, 1), (0, 1)), ((), ())),
        precision=lax.Precision.HIGHEST,
    )
    combination_transposed = combination_transposed_of(
        butterfly_sum(jnp.concatenate([gram_local, projected[None, :]], axis=0), ("gx", "gy"))
    )
    contract = (((2,), (1,)), ((), ()))
    updated_t = average_t[:, :, None] + lax.dot_general(
        deviation_t, combination_transposed, contract, precision=lax.Precision.HIGHEST
    )
    heat_out_t = mean_heat_t[:, :, None] + lax.dot_general(
        heat_anomaly_t, combination_transposed, contract, precision=lax.Precision.HIGHEST
    )
    return (jnp.transpose(updated_t, (2, 1, 0)), jnp.transpose(heat_out_t, (2, 1, 0)))


def solution(mesh):
    placed = (
        P(None, "gx", "gy"),
        P(None, "gx", "gy"),
        P(("gx", "gy")),
        P(("gx", "gy")),
        P(("gx", "gy")),
    )
    return jax.shard_map(
        shards,
        mesh=mesh,
        in_specs=placed,
        out_specs=(P(None, "gx", "gy"), P(None, "gx", "gy")),
        check_vma=False,
    )
```

```python
import math

import jax
import jax.numpy as jnp
from jax import lax
from jax.experimental import pallas as pl
from jax.experimental.pallas import tpu as pltpu
from jax.sharding import PartitionSpec as P

diffusion = 0.2
heating = 0.5


def xor_tree(received, base, strides):
    if not strides:
        return received[base]
    return xor_tree(received, base, strides[:-1]) + xor_tree(
        received, base ^ strides[-1], strides[:-1]
    )


def butterfly_sum(value, axes):
    for axis in axes:
        count = lax.axis_size(axis)
        if count & (count - 1):
            value = lax.psum(value, axis)
            continue
        bits = [1 << b for b in range(count.bit_length() - 1)]
        for first in range(len(bits)):
            strides = bits[first : first + 1]
            received = {0: value}
            for mask in range(1, 1 << len(strides)):
                offset = 0
                for position, stride in enumerate(strides):
                    if mask >> position & 1:
                        offset ^= stride
                pairs = [(i, i ^ offset) for i in range(count)]
                received[offset] = lax.ppermute(value, axis, pairs)
            value = xor_tree(received, 0, strides)
    return value


def combination_kernel(stacked_ref, combination_ref, work_ref, inverse_ref, block=4):
    size = stacked_ref.shape[1]
    square_row = lax.broadcasted_iota(jnp.int32, (size, size), 0)
    square_col = lax.broadcasted_iota(jnp.int32, (size, size), 1)
    unit = jnp.where(square_row == square_col, 1.0, 0.0).astype(jnp.float32)
    work_ref[...] = stacked_ref[:size, :] + unit
    inverse_ref[...] = unit
    lane = lax.broadcasted_iota(jnp.int32, (1, size), 1)

    def pick(vector, where_true, axis):
        return jnp.sum(jnp.where(where_true, vector, 0.0), axis=axis, keepdims=True)

    for first in range(0, size, 8):
        span = size - first
        sublane = lax.broadcasted_iota(jnp.int32, (span, 1), 0) + first
        band_col = lax.broadcasted_iota(jnp.int32, (span, size), 1)

        def step(group, carry, first=first, sublane=sublane, band_col=band_col):
            k = block * group
            band = work_ref[first:, :]
            factor_rows, factor_cols, inverse_rows = [], [], []
            for j in range(block):
                row = work_ref[pl.ds(k + j, 1), :]
                col = pick(band, band_col == k + j, 1)
                inverse_row = inverse_ref[pl.ds(k + j, 1), :]
                for i in range(j):
                    coupling = pick(factor_rows[i], lane == k + j, 1)
                    row = row - coupling * factor_rows[i]
                    col = col - factor_cols[i] * coupling
                    inverse_row = inverse_row - coupling * inverse_rows[i]
                scale = 1.0 / jnp.sqrt(pick(row, lane == k + j, 1))
                factor_rows.append(jnp.where(lane >= k + j, row * scale, 0.0))
                factor_cols.append(jnp.where(sublane >= k + j, col * scale, 0.0))
                inverse_rows.append(inverse_row * scale)
            update = band
            inverse_band = inverse_ref[first:, :]
            for j in range(block):
                update = update - factor_cols[j] * factor_rows[j]
                below = jnp.where(sublane >= k + block, factor_cols[j], 0.0)
                inverse_band = inverse_band - below * inverse_rows[j]
            work_ref[first:, :] = update
            inverse_ref[first:, :] = inverse_band
            for j in range(block):
                inverse_ref[pl.ds(k + j, 1), :] = inverse_rows[j]
            return carry

        lax.fori_loop(first // block, min(first + 8, size) // block, step, 0)
    lower_inverse = inverse_ref[...]
    projected_row = stacked_ref[size : size + 1, :]
    whitened = jnp.sum(lower_inverse * projected_row, axis=1, keepdims=True)
    mean_weights = jnp.sum(lower_inverse * whitened, axis=0, keepdims=True)
    combination_ref[...] = lower_inverse + mean_weights


def combination_transposed_of(stacked):
    size = stacked.shape[1]
    return pl.pallas_call(
        combination_kernel,
        out_shape=jax.ShapeDtypeStruct((size, size), jnp.float32),
        in_specs=[pl.BlockSpec(memory_space=pltpu.VMEM)],
        out_specs=pl.BlockSpec(memory_space=pltpu.VMEM),
        scratch_shapes=[pltpu.VMEM((size, size), jnp.float32)] * 2,
    )(stacked)

def propagate_model(padded_field, source_term):
    laplacian = (
        padded_field[:, 2:, 1:-1]
        + padded_field[:, :-2, 1:-1]
        + padded_field[:, 1:-1, 2:]
        + padded_field[:, 1:-1, :-2]
        - 4.0 * padded_field[:, 1:-1, 1:-1]
    )
    return padded_field[:, 1:-1, 1:-1] + diffusion * laplacian + heating * source_term


def propagate_members_last(padded_field, source_term):
    laplacian = (
        padded_field[1:-1, 2:]
        + padded_field[1:-1, :-2]
        + padded_field[2:, 1:-1]
        + padded_field[:-2, 1:-1]
        - 4.0 * padded_field[1:-1, 1:-1]
    )
    return padded_field[1:-1, 1:-1] + diffusion * laplacian + heating * source_term


def from_neighbour(block, axis, step):
    count = lax.axis_size(axis)
    if step > 0:
        pairs = [(i, i + 1) for i in range(count - 1)]
    else:
        pairs = [(i + 1, i) for i in range(count - 1)]
    return lax.ppermute(block, axis, pairs)


def forecast_two_steps(warmth, heat):
    width, height = warmth.shape[0], warmth.shape[1]
    top = from_neighbour(
        jnp.concatenate([warmth[:, -2:], heat[:, -1:]], axis=1), "gx", 1
    )
    bottom = from_neighbour(
        jnp.concatenate([warmth[:, :2], heat[:, :1]], axis=1), "gx", -1
    )
    warmth_tall = jnp.concatenate([top[:, :2], warmth, bottom[:, :2]], axis=1)
    heat_tall = jnp.concatenate([top[:, 2:], heat, bottom[:, 2:]], axis=1)
    edge = jnp.zeros_like(heat_tall[:1, :1])
    left = from_neighbour(
        jnp.concatenate(
            [warmth_tall[-2:], jnp.concatenate([edge, heat_tall[-1:], edge], axis=1)],
            axis=0,
        ),
        "gy",
        1,
    )
    right = from_neighbour(
        jnp.concatenate(
            [warmth_tall[:2], jnp.concatenate([edge, heat_tall[:1], edge], axis=1)],
            axis=0,
        ),
        "gy",
        -1,
    )
    warmth_wide = jnp.concatenate([left[:2], warmth_tall, right[:2]], axis=0)
    heat_wide = jnp.concatenate([left[2:, 1:-1], heat_tall, right[2:, 1:-1]], axis=0)
    first = propagate_members_last(warmth_wide, heat_wide)
    col = lax.broadcasted_iota(jnp.int32, (width + 2, height + 2), 0)
    row = lax.broadcasted_iota(jnp.int32, (width + 2, height + 2), 1)
    at_x, at_y = lax.axis_index("gx"), lax.axis_index("gy")
    outside = (
        ((row == 0) & (at_x == 0))
        | ((row == height + 1) & (at_x == lax.axis_size("gx") - 1))
        | ((col == 0) & (at_y == 0))
        | ((col == width + 1) & (at_y == lax.axis_size("gy") - 1))
    )
    first = jnp.where(outside[:, :, None], 0.0, first)
    return propagate_members_last(first, heat)


def shards(
    prior_gas_warmth,
    fire_power_output,
    measured_warmth,
    reading_noise_spread,
    reading_local_location,
):
    sample_number, block_height_number, block_width_number = prior_gas_warmth.shape
    warmth_t = jnp.transpose(prior_gas_warmth, (2, 1, 0))
    heat_t = jnp.transpose(fire_power_output, (2, 1, 0))
    predicted_t = forecast_two_steps(warmth_t, heat_t)
    average_t = jnp.mean(predicted_t, axis=2)
    mean_heat_t = jnp.mean(heat_t, axis=2)
    deviation_t = predicted_t - average_t[:, :, None]
    heat_anomaly_t = heat_t - mean_heat_t[:, :, None]
    coefficient_line = 1.0 / (reading_noise_spread * math.sqrt(sample_number - 1))
    weight_line = coefficient_line * coefficient_line
    row_hot = (
        (reading_local_location // block_width_number)[:, None]
        == lax.broadcasted_iota(jnp.int32, (1, block_height_number), 1)
    ).astype(jnp.float32)
    col_hot = (
        (reading_local_location % block_width_number)[:, None]
        == lax.broadcasted_iota(jnp.int32, (1, block_width_number), 1)
    ).astype(jnp.float32)
    weighted_rows = jnp.concatenate(
        [row_hot * weight_line[:, None], row_hot * (weight_line * measured_warmth)[:, None]],
        axis=1,
    )
    cell_sums = lax.dot_general(
        col_hot, weighted_rows, (((0,), (0,)), ((), ())), precision=lax.Precision.HIGHEST
    )
    cell_weight = cell_sums[:, :block_height_number]
    cell_residual = cell_sums[:, block_height_number:] - average_t * cell_weight
    gram_local = lax.dot_general(
        deviation_t * cell_weight[:, :, None],
        deviation_t,
        (((0, 1), (0, 1)), ((), ())),
        precision=lax.Precision.HIGHEST,
    )
    projected = lax.dot_general(
        deviation_t,
        cell_residual,
        (((0, 1), (0, 1)), ((), ())),
        precision=lax.Precision.HIGHEST,
    )
    combination_transposed = combination_transposed_of(
        butterfly_sum(jnp.concatenate([gram_local, projected[None, :]], axis=0), ("gx", "gy"))
    )
    contract = (((2,), (1,)), ((), ()))
    updated_t = average_t[:, :, None] + lax.dot_general(
        deviation_t, combination_transposed, contract, precision=lax.Precision.HIGHEST
    )
    heat_out_t = mean_heat_t[:, :, None] + lax.dot_general(
        heat_anomaly_t, combination_transposed, contract, precision=lax.Precision.HIGHEST
    )
    return (jnp.transpose(updated_t, (2, 1, 0)), jnp.transpose(heat_out_t, (2, 1, 0)))


def solution(mesh):
    placed = (
        P(None, "gx", "gy"),
        P(None, "gx", "gy"),
        P(("gx", "gy")),
        P(("gx", "gy")),
        P(("gx", "gy")),
    )
    return jax.shard_map(
        shards,
        mesh=mesh,
        in_specs=placed,
        out_specs=(P(None, "gx", "gy"), P(None, "gx", "gy")),
        check_vma=False,
    )
```

```python
import math

import jax
import jax.numpy as jnp
from jax import lax
from jax.experimental import pallas as pl
from jax.experimental.pallas import tpu as pltpu
from jax.sharding import PartitionSpec as P

diffusion = 0.2
heating = 0.5


def xor_tree(received, base, strides):
    if not strides:
        return received[base]
    return xor_tree(received, base, strides[:-1]) + xor_tree(
        received, base ^ strides[-1], strides[:-1]
    )


def butterfly_sum(value, axes):
    for axis in axes:
        count = lax.axis_size(axis)
        if count & (count - 1):
            value = lax.psum(value, axis)
            continue
        bits = [1 << b for b in range(count.bit_length() - 1)]
        for first in range(len(bits)):
            strides = bits[first : first + 1]
            received = {0: value}
            for mask in range(1, 1 << len(strides)):
                offset = 0
                for position, stride in enumerate(strides):
                    if mask >> position & 1:
                        offset ^= stride
                pairs = [(i, i ^ offset) for i in range(count)]
                received[offset] = lax.ppermute(value, axis, pairs)
            value = xor_tree(received, 0, strides)
    return value


def combination_kernel(stacked_ref, combination_ref, work_ref, inverse_ref):
    size = stacked_ref.shape[1]
    square_row = lax.broadcasted_iota(jnp.int32, (size, size), 0)
    square_col = lax.broadcasted_iota(jnp.int32, (size, size), 1)
    unit = jnp.where(square_row == square_col, 1.0, 0.0).astype(jnp.float32)
    work_ref[...] = stacked_ref[:size, :] + unit
    inverse_ref[...] = unit
    lane = lax.broadcasted_iota(jnp.int32, (1, size), 1)

    def pick(vector, where_true, axis):
        return jnp.sum(jnp.where(where_true, vector, 0.0), axis=axis, keepdims=True)

    for first in range(0, size, 8):
        span = size - first
        sublane = lax.broadcasted_iota(jnp.int32, (span, 1), 0) + first
        band_col = lax.broadcasted_iota(jnp.int32, (span, size), 1)

        def step(pair, carry, sublane=sublane, band_col=band_col):
            band, inverse_band = carry
            k = 2 * pair
            row0 = pick(band, sublane == k, 0)
            row1 = pick(band, sublane == k + 1, 0)
            col0 = pick(band, band_col == k, 1)
            col1 = pick(band, band_col == k + 1, 1)
            scale0 = 1.0 / jnp.sqrt(pick(row0, lane == k, 1))
            coupling = pick(row0, lane == k + 1, 1) * scale0
            scale1 = 1.0 / jnp.sqrt(pick(row1, lane == k + 1, 1) - coupling * coupling)
            factor_row0 = jnp.where(lane >= k, row0 * scale0, 0.0)
            factor_row1 = jnp.where(lane >= k + 1, (row1 - coupling * factor_row0) * scale1, 0.0)
            factor_col0 = jnp.where(sublane >= k, col0 * scale0, 0.0)
            factor_col1 = jnp.where(
                sublane >= k + 1, (col1 - factor_col0 * coupling) * scale1, 0.0
            )
            band = band - factor_col0 * factor_row0 - factor_col1 * factor_row1
            inverse_row0 = pick(inverse_band, sublane == k, 0) * scale0
            inverse_row1 = (pick(inverse_band, sublane == k + 1, 0) - coupling * inverse_row0) * scale1
            below0 = jnp.where(sublane > k + 1, factor_col0, 0.0)
            below1 = jnp.where(sublane > k + 1, factor_col1, 0.0)
            inverse_band = inverse_band - below0 * inverse_row0 - below1 * inverse_row1
            inverse_band = jnp.where(
                sublane == k, inverse_row0, jnp.where(sublane == k + 1, inverse_row1, inverse_band)
            )
            return (band, inverse_band)

        band, inverse_band = lax.fori_loop(
            first // 2,
            min(first + 8, size) // 2,
            step,
            (work_ref[first:, :], inverse_ref[first:, :]),
        )
        work_ref[first:, :] = band
        inverse_ref[first:, :] = inverse_band
    lower_inverse = inverse_ref[...]
    projected_row = stacked_ref[size : size + 1, :]
    whitened = jnp.sum(lower_inverse * projected_row, axis=1, keepdims=True)
    mean_weights = jnp.sum(lower_inverse * whitened, axis=0, keepdims=True)
    combination_ref[...] = lower_inverse + mean_weights


def combination_transposed_of(stacked):
    size = stacked.shape[1]
    return pl.pallas_call(
        combination_kernel,
        out_shape=jax.ShapeDtypeStruct((size, size), jnp.float32),
        in_specs=[pl.BlockSpec(memory_space=pltpu.VMEM)],
        out_specs=pl.BlockSpec(memory_space=pltpu.VMEM),
        scratch_shapes=[pltpu.VMEM((size, size), jnp.float32)] * 2,
    )(stacked)

def propagate_model(padded_field, source_term):
    laplacian = (
        padded_field[:, 2:, 1:-1]
        + padded_field[:, :-2, 1:-1]
        + padded_field[:, 1:-1, 2:]
        + padded_field[:, 1:-1, :-2]
        - 4.0 * padded_field[:, 1:-1, 1:-1]
    )
    return padded_field[:, 1:-1, 1:-1] + diffusion * laplacian + heating * source_term


def propagate_members_last(padded_field, source_term):
    laplacian = (
        padded_field[1:-1, 2:]
        + padded_field[1:-1, :-2]
        + padded_field[2:, 1:-1]
        + padded_field[:-2, 1:-1]
        - 4.0 * padded_field[1:-1, 1:-1]
    )
    return padded_field[1:-1, 1:-1] + diffusion * laplacian + heating * source_term


def from_neighbour(block, axis, step):
    count = lax.axis_size(axis)
    if step > 0:
        pairs = [(i, i + 1) for i in range(count - 1)]
    else:
        pairs = [(i + 1, i) for i in range(count - 1)]
    return lax.ppermute(block, axis, pairs)


def forecast_two_steps(warmth, heat):
    width, height = warmth.shape[0], warmth.shape[1]
    top = from_neighbour(
        jnp.concatenate([warmth[:, -2:], heat[:, -1:]], axis=1), "gx", 1
    )
    bottom = from_neighbour(
        jnp.concatenate([warmth[:, :2], heat[:, :1]], axis=1), "gx", -1
    )
    warmth_tall = jnp.concatenate([top[:, :2], warmth, bottom[:, :2]], axis=1)
    heat_tall = jnp.concatenate([top[:, 2:], heat, bottom[:, 2:]], axis=1)
    edge = jnp.zeros_like(heat_tall[:1, :1])
    left = from_neighbour(
        jnp.concatenate(
            [warmth_tall[-2:], jnp.concatenate([edge, heat_tall[-1:], edge], axis=1)],
            axis=0,
        ),
        "gy",
        1,
    )
    right = from_neighbour(
        jnp.concatenate(
            [warmth_tall[:2], jnp.concatenate([edge, heat_tall[:1], edge], axis=1)],
            axis=0,
        ),
        "gy",
        -1,
    )
    warmth_wide = jnp.concatenate([left[:2], warmth_tall, right[:2]], axis=0)
    heat_wide = jnp.concatenate([left[2:, 1:-1], heat_tall, right[2:, 1:-1]], axis=0)
    first = propagate_members_last(warmth_wide, heat_wide)
    col = lax.broadcasted_iota(jnp.int32, (width + 2, height + 2), 0)
    row = lax.broadcasted_iota(jnp.int32, (width + 2, height + 2), 1)
    at_x, at_y = lax.axis_index("gx"), lax.axis_index("gy")
    outside = (
        ((row == 0) & (at_x == 0))
        | ((row == height + 1) & (at_x == lax.axis_size("gx") - 1))
        | ((col == 0) & (at_y == 0))
        | ((col == width + 1) & (at_y == lax.axis_size("gy") - 1))
    )
    first = jnp.where(outside[:, :, None], 0.0, first)
    return propagate_members_last(first, heat)


def shards(
    prior_gas_warmth,
    fire_power_output,
    measured_warmth,
    reading_noise_spread,
    reading_local_location,
):
    sample_number, block_height_number, block_width_number = prior_gas_warmth.shape
    warmth_t = jnp.transpose(prior_gas_warmth, (2, 1, 0))
    heat_t = jnp.transpose(fire_power_output, (2, 1, 0))
    predicted_t = forecast_two_steps(warmth_t, heat_t)
    average_t = jnp.mean(predicted_t, axis=2)
    mean_heat_t = jnp.mean(heat_t, axis=2)
    deviation_t = predicted_t - average_t[:, :, None]
    heat_anomaly_t = heat_t - mean_heat_t[:, :, None]
    coefficient_line = 1.0 / (reading_noise_spread * math.sqrt(sample_number - 1))
    weight_line = coefficient_line * coefficient_line
    row_hot = (
        (reading_local_location // block_width_number)[:, None]
        == lax.broadcasted_iota(jnp.int32, (1, block_height_number), 1)
    ).astype(jnp.float32)
    col_hot = (
        (reading_local_location % block_width_number)[:, None]
        == lax.broadcasted_iota(jnp.int32, (1, block_width_number), 1)
    ).astype(jnp.float32)
    weighted_rows = jnp.concatenate(
        [row_hot * weight_line[:, None], row_hot * (weight_line * measured_warmth)[:, None]],
        axis=1,
    )
    cell_sums = lax.dot_general(
        col_hot, weighted_rows, (((0,), (0,)), ((), ())), precision=lax.Precision.HIGHEST
    )
    cell_weight = cell_sums[:, :block_height_number]
    cell_residual = cell_sums[:, block_height_number:] - average_t * cell_weight
    gram_local = lax.dot_general(
        deviation_t * cell_weight[:, :, None],
        deviation_t,
        (((0, 1), (0, 1)), ((), ())),
        precision=lax.Precision.HIGHEST,
    )
    projected = lax.dot_general(
        deviation_t,
        cell_residual,
        (((0, 1), (0, 1)), ((), ())),
        precision=lax.Precision.HIGHEST,
    )
    combination_transposed = combination_transposed_of(
        butterfly_sum(jnp.concatenate([gram_local, projected[None, :]], axis=0), ("gx", "gy"))
    )
    contract = (((2,), (1,)), ((), ()))
    updated_t = average_t[:, :, None] + lax.dot_general(
        deviation_t, combination_transposed, contract, precision=lax.Precision.HIGHEST
    )
    heat_out_t = mean_heat_t[:, :, None] + lax.dot_general(
        heat_anomaly_t, combination_transposed, contract, precision=lax.Precision.HIGHEST
    )
    return (jnp.transpose(updated_t, (2, 1, 0)), jnp.transpose(heat_out_t, (2, 1, 0)))


def solution(mesh):
    placed = (
        P(None, "gx", "gy"),
        P(None, "gx", "gy"),
        P(("gx", "gy")),
        P(("gx", "gy")),
        P(("gx", "gy")),
    )
    return jax.shard_map(
        shards,
        mesh=mesh,
        in_specs=placed,
        out_specs=(P(None, "gx", "gy"), P(None, "gx", "gy")),
        check_vma=False,
    )
```

```python
import math

import jax
import jax.numpy as jnp
from jax import lax
from jax.experimental import pallas as pl
from jax.experimental.pallas import tpu as pltpu
from jax.sharding import PartitionSpec as P

diffusion = 0.2
heating = 0.5


def xor_tree(received, base, strides):
    if not strides:
        return received[base]
    return xor_tree(received, base, strides[:-1]) + xor_tree(
        received, base ^ strides[-1], strides[:-1]
    )


def butterfly_sum(value, axes):
    for axis in axes:
        count = lax.axis_size(axis)
        if count & (count - 1):
            value = lax.psum(value, axis)
            continue
        bits = [1 << b for b in range(count.bit_length() - 1)]
        for first in range(len(bits)):
            strides = bits[first : first + 1]
            received = {0: value}
            for mask in range(1, 1 << len(strides)):
                offset = 0
                for position, stride in enumerate(strides):
                    if mask >> position & 1:
                        offset ^= stride
                pairs = [(i, i ^ offset) for i in range(count)]
                received[offset] = lax.ppermute(value, axis, pairs)
            value = xor_tree(received, 0, strides)
    return value


def combination_kernel(stacked_ref, combination_ref, work_ref, inverse_ref):
    size = stacked_ref.shape[1]
    square_row = lax.broadcasted_iota(jnp.int32, (size, size), 0)
    square_col = lax.broadcasted_iota(jnp.int32, (size, size), 1)
    unit = jnp.where(square_row == square_col, 1.0, 0.0).astype(jnp.float32)
    work_ref[...] = stacked_ref[:size, :] + unit
    inverse_ref[...] = unit
    lane = lax.broadcasted_iota(jnp.int32, (1, size), 1)

    def pick(vector, where_true, axis):
        return jnp.sum(jnp.where(where_true, vector, 0.0), axis=axis, keepdims=True)

    for first in range(0, size, 8):
        span = size - first
        sublane = lax.broadcasted_iota(jnp.int32, (span, 1), 0) + first
        band_col = lax.broadcasted_iota(jnp.int32, (span, size), 1)

        def step(pair, carry, first=first, sublane=sublane, band_col=band_col):
            k = 2 * pair
            row0 = work_ref[pl.ds(k, 1), :]
            row1 = work_ref[pl.ds(k + 1, 1), :]
            band = work_ref[first:, :]
            col0 = pick(band, band_col == k, 1)
            col1 = pick(band, band_col == k + 1, 1)
            scale0 = 1.0 / jnp.sqrt(pick(row0, lane == k, 1))
            coupling = pick(row0, lane == k + 1, 1) * scale0
            scale1 = 1.0 / jnp.sqrt(pick(row1, lane == k + 1, 1) - coupling * coupling)
            factor_row0 = jnp.where(lane >= k, row0 * scale0, 0.0)
            factor_row1 = jnp.where(lane >= k + 1, (row1 - coupling * factor_row0) * scale1, 0.0)
            factor_col0 = jnp.where(sublane >= k, col0 * scale0, 0.0)
            factor_col1 = jnp.where(
                sublane >= k + 1, (col1 - factor_col0 * coupling) * scale1, 0.0
            )
            work_ref[first:, :] = band - factor_col0 * factor_row0 - factor_col1 * factor_row1
            inverse_row0 = inverse_ref[pl.ds(k, 1), :] * scale0
            inverse_row1 = (inverse_ref[pl.ds(k + 1, 1), :] - coupling * inverse_row0) * scale1
            below0 = jnp.where(sublane > k + 1, factor_col0, 0.0)
            below1 = jnp.where(sublane > k + 1, factor_col1, 0.0)
            inverse_ref[first:, :] = (
                inverse_ref[first:, :] - below0 * inverse_row0 - below1 * inverse_row1
            )
            inverse_ref[pl.ds(k, 1), :] = inverse_row0
            inverse_ref[pl.ds(k + 1, 1), :] = inverse_row1
            return carry

        lax.fori_loop(first // 2, min(first + 8, size) // 2, step, 0)
    lower_inverse = inverse_ref[...]
    projected_row = stacked_ref[size : size + 1, :]
    whitened = jnp.sum(lower_inverse * projected_row, axis=1, keepdims=True)
    mean_weights = jnp.sum(lower_inverse * whitened, axis=0, keepdims=True)
    combination_ref[...] = lower_inverse + mean_weights


def combination_transposed_of(stacked):
    size = stacked.shape[1]
    return pl.pallas_call(
        combination_kernel,
        out_shape=jax.ShapeDtypeStruct((size, size), jnp.float32),
        in_specs=[pl.BlockSpec(memory_space=pltpu.VMEM)],
        out_specs=pl.BlockSpec(memory_space=pltpu.VMEM),
        scratch_shapes=[pltpu.VMEM((size, size), jnp.float32)] * 2,
    )(stacked)

def propagate_model(padded_field, source_term):
    laplacian = (
        padded_field[:, 2:, 1:-1]
        + padded_field[:, :-2, 1:-1]
        + padded_field[:, 1:-1, 2:]
        + padded_field[:, 1:-1, :-2]
        - 4.0 * padded_field[:, 1:-1, 1:-1]
    )
    return padded_field[:, 1:-1, 1:-1] + diffusion * laplacian + heating * source_term


def propagate_members_last(padded_field, source_term):
    laplacian = (
        padded_field[1:-1, 2:]
        + padded_field[1:-1, :-2]
        + padded_field[2:, 1:-1]
        + padded_field[:-2, 1:-1]
        - 4.0 * padded_field[1:-1, 1:-1]
    )
    return padded_field[1:-1, 1:-1] + diffusion * laplacian + heating * source_term


def from_neighbour(block, axis, step):
    count = lax.axis_size(axis)
    if step > 0:
        pairs = [(i, i + 1) for i in range(count - 1)]
    else:
        pairs = [(i + 1, i) for i in range(count - 1)]
    return lax.ppermute(block, axis, pairs)


def forecast_in_pieces(warmth, heat):
    width, height = warmth.shape[0], warmth.shape[1]
    top = from_neighbour(
        jnp.concatenate([warmth[:, -2:], heat[:, -1:]], axis=1), "gx", 1
    )
    bottom = from_neighbour(
        jnp.concatenate([warmth[:, :2], heat[:, :1]], axis=1), "gx", -1
    )
    warmth_tall = jnp.concatenate([top[:, :2], warmth, bottom[:, :2]], axis=1)
    heat_tall = jnp.concatenate([top[:, 2:], heat, bottom[:, 2:]], axis=1)
    edge = jnp.zeros_like(heat_tall[:1, :1])
    left = from_neighbour(
        jnp.concatenate(
            [warmth_tall[-2:], jnp.concatenate([edge, heat_tall[-1:], edge], axis=1)],
            axis=0,
        ),
        "gy",
        1,
    )
    right = from_neighbour(
        jnp.concatenate(
            [warmth_tall[:2], jnp.concatenate([edge, heat_tall[:1], edge], axis=1)],
            axis=0,
        ),
        "gy",
        -1,
    )
    at_x, at_y = lax.axis_index("gx"), lax.axis_index("gy")
    row = lax.broadcasted_iota(jnp.int32, (1, height + 2, 1), 1)
    off_grid = ((row == 0) & (at_x == 0)) | (
        (row == height + 1) & (at_x == lax.axis_size("gx") - 1)
    )
    first_inner = jnp.where(
        off_grid, 0.0, propagate_members_last(warmth_tall, heat_tall[1:-1])
    )
    second_inner = propagate_members_last(first_inner, heat[2:-2])
    first_left = propagate_members_last(
        jnp.concatenate([left[:2], warmth_tall[:2]], axis=0),
        jnp.concatenate([left[2:, 1:-1], heat_tall[:1]], axis=0),
    )
    first_right = propagate_members_last(
        jnp.concatenate([warmth_tall[-2:], right[:2]], axis=0),
        jnp.concatenate([heat_tall[-1:], right[2:, 1:-1]], axis=0),
    )
    col = lax.broadcasted_iota(jnp.int32, (2, 1, 1), 0)
    first_left = jnp.where(off_grid | ((col == 0) & (at_y == 0)), 0.0, first_left)
    first_right = jnp.where(
        off_grid | ((col == 1) & (at_y == lax.axis_size("gy") - 1)), 0.0, first_right
    )
    second_left = propagate_members_last(
        jnp.concatenate([first_left, first_inner[:2]], axis=0), heat[:2]
    )
    second_right = propagate_members_last(
        jnp.concatenate([first_inner[-2:], first_right], axis=0), heat[-2:]
    )
    return [(0, second_left), (2, second_inner), (width - 2, second_right)]


def shards(
    prior_gas_warmth,
    fire_power_output,
    measured_warmth,
    reading_noise_spread,
    reading_local_location,
):
    sample_number, block_height_number, block_width_number = prior_gas_warmth.shape
    warmth_t = jnp.transpose(prior_gas_warmth, (2, 1, 0))
    heat_t = jnp.transpose(fire_power_output, (2, 1, 0))
    pieces = forecast_in_pieces(warmth_t, heat_t)
    mean_heat_t = jnp.mean(heat_t, axis=2)
    heat_anomaly_t = heat_t - mean_heat_t[:, :, None]
    coefficient_line = 1.0 / (reading_noise_spread * math.sqrt(sample_number - 1))
    weight_line = coefficient_line * coefficient_line
    row_hot = (
        (reading_local_location // block_width_number)[:, None]
        == lax.broadcasted_iota(jnp.int32, (1, block_height_number), 1)
    ).astype(jnp.float32)
    col_hot = (
        (reading_local_location % block_width_number)[:, None]
        == lax.broadcasted_iota(jnp.int32, (1, block_width_number), 1)
    ).astype(jnp.float32)
    weighted_rows = jnp.concatenate(
        [row_hot * weight_line[:, None], row_hot * (weight_line * measured_warmth)[:, None]],
        axis=1,
    )
    cell_sums = lax.dot_general(
        col_hot, weighted_rows, (((0,), (0,)), ((), ())), precision=lax.Precision.HIGHEST
    )
    averages, deviations, gram_local, projected = [], [], 0.0, 0.0
    for start, piece in pieces:
        count = piece.shape[0]
        average = jnp.mean(piece, axis=2)
        deviation = piece - average[:, :, None]
        cell_weight = cell_sums[start : start + count, :block_height_number]
        cell_residual = cell_sums[start : start + count, block_height_number:] - average * cell_weight
        gram_local = gram_local + lax.dot_general(
            deviation * cell_weight[:, :, None],
            deviation,
            (((0, 1), (0, 1)), ((), ())),
            precision=lax.Precision.HIGHEST,
        )
        projected = projected + lax.dot_general(
            deviation,
            cell_residual,
            (((0, 1), (0, 1)), ((), ())),
            precision=lax.Precision.HIGHEST,
        )
        averages.append(average)
        deviations.append(deviation)
    average_t = jnp.concatenate(averages, axis=0)
    deviation_t = jnp.concatenate(deviations, axis=0)
    combination_transposed = combination_transposed_of(
        butterfly_sum(jnp.concatenate([gram_local, projected[None, :]], axis=0), ("gx", "gy"))
    )
    contract = (((2,), (1,)), ((), ()))
    updated_t = average_t[:, :, None] + lax.dot_general(
        deviation_t, combination_transposed, contract, precision=lax.Precision.HIGHEST
    )
    heat_out_t = mean_heat_t[:, :, None] + lax.dot_general(
        heat_anomaly_t, combination_transposed, contract, precision=lax.Precision.HIGHEST
    )
    return (jnp.transpose(updated_t, (2, 1, 0)), jnp.transpose(heat_out_t, (2, 1, 0)))


def solution(mesh):
    placed = (
        P(None, "gx", "gy"),
        P(None, "gx", "gy"),
        P(("gx", "gy")),
        P(("gx", "gy")),
        P(("gx", "gy")),
    )
    return jax.shard_map(
        shards,
        mesh=mesh,
        in_specs=placed,
        out_specs=(P(None, "gx", "gy"), P(None, "gx", "gy")),
        check_vma=False,
    )
```

```python
import math

import jax
import jax.numpy as jnp
from jax import lax
from jax.experimental import pallas as pl
from jax.experimental.pallas import tpu as pltpu
from jax.sharding import PartitionSpec as P

diffusion = 0.2
heating = 0.5


def xor_tree(received, base, strides):
    if not strides:
        return received[base]
    return xor_tree(received, base, strides[:-1]) + xor_tree(
        received, base ^ strides[-1], strides[:-1]
    )


def butterfly_sum(value, axes):
    for axis in axes:
        count = lax.axis_size(axis)
        if count & (count - 1):
            value = lax.psum(value, axis)
            continue
        bits = [1 << b for b in range(count.bit_length() - 1)]
        for first in range(len(bits)):
            strides = bits[first : first + 1]
            received = {0: value}
            for mask in range(1, 1 << len(strides)):
                offset = 0
                for position, stride in enumerate(strides):
                    if mask >> position & 1:
                        offset ^= stride
                pairs = [(i, i ^ offset) for i in range(count)]
                received[offset] = lax.ppermute(value, axis, pairs)
            value = xor_tree(received, 0, strides)
    return value


def combination_kernel(stacked_ref, combination_ref, work_ref, inverse_ref):
    size = stacked_ref.shape[1]
    square_row = lax.broadcasted_iota(jnp.int32, (size, size), 0)
    square_col = lax.broadcasted_iota(jnp.int32, (size, size), 1)
    unit = jnp.where(square_row == square_col, 1.0, 0.0).astype(jnp.float32)
    work_ref[...] = stacked_ref[:size, :] + unit
    inverse_ref[...] = unit
    lane = lax.broadcasted_iota(jnp.int32, (1, size), 1)

    def pick(vector, where_true, axis):
        return jnp.sum(jnp.where(where_true, vector, 0.0), axis=axis, keepdims=True)

    for first in range(0, size, 8):
        span = size - first
        sublane = lax.broadcasted_iota(jnp.int32, (span, 1), 0) + first
        band_col = lax.broadcasted_iota(jnp.int32, (span, size), 1)

        def step(pair, carry, first=first, sublane=sublane, band_col=band_col):
            k = 2 * pair
            row0 = work_ref[pl.ds(k, 1), :]
            row1 = work_ref[pl.ds(k + 1, 1), :]
            band = work_ref[first:, :]
            col0 = pick(band, band_col == k, 1)
            col1 = pick(band, band_col == k + 1, 1)
            scale0 = 1.0 / jnp.sqrt(pick(row0, lane == k, 1))
            coupling = pick(row0, lane == k + 1, 1) * scale0
            scale1 = 1.0 / jnp.sqrt(pick(row1, lane == k + 1, 1) - coupling * coupling)
            factor_row0 = jnp.where(lane >= k, row0 * scale0, 0.0)
            factor_row1 = jnp.where(lane >= k + 1, (row1 - coupling * factor_row0) * scale1, 0.0)
            factor_col0 = jnp.where(sublane >= k, col0 * scale0, 0.0)
            factor_col1 = jnp.where(
                sublane >= k + 1, (col1 - factor_col0 * coupling) * scale1, 0.0
            )
            work_ref[first:, :] = band - factor_col0 * factor_row0 - factor_col1 * factor_row1
            inverse_row0 = inverse_ref[pl.ds(k, 1), :] * scale0
            inverse_row1 = (inverse_ref[pl.ds(k + 1, 1), :] - coupling * inverse_row0) * scale1
            below0 = jnp.where(sublane > k + 1, factor_col0, 0.0)
            below1 = jnp.where(sublane > k + 1, factor_col1, 0.0)
            inverse_ref[first:, :] = (
                inverse_ref[first:, :] - below0 * inverse_row0 - below1 * inverse_row1
            )
            inverse_ref[pl.ds(k, 1), :] = inverse_row0
            inverse_ref[pl.ds(k + 1, 1), :] = inverse_row1
            return carry

        lax.fori_loop(first // 2, min(first + 8, size) // 2, step, 0)
    lower_inverse = inverse_ref[...]
    projected_row = stacked_ref[size : size + 1, :]
    whitened = jnp.sum(lower_inverse * projected_row, axis=1, keepdims=True)
    mean_weights = jnp.sum(lower_inverse * whitened, axis=0, keepdims=True)
    combination_ref[...] = lower_inverse + mean_weights


def combination_transposed_of(stacked):
    size = stacked.shape[1]
    return pl.pallas_call(
        combination_kernel,
        out_shape=jax.ShapeDtypeStruct((size, size), jnp.float32),
        in_specs=[pl.BlockSpec(memory_space=pltpu.VMEM)],
        out_specs=pl.BlockSpec(memory_space=pltpu.VMEM),
        scratch_shapes=[pltpu.VMEM((size, size), jnp.float32)] * 2,
    )(stacked)

def analysis_kernel(combination_ref, deviation_ref, average_ref, out_ref):
    for level in range(deviation_ref.shape[0]):
        product = lax.dot_general(
            combination_ref[...],
            deviation_ref[level],
            (((1,), (1,)), ((), ())),
            precision=lax.Precision.HIGHEST,
            preferred_element_type=jnp.float32,
        )
        out_ref[:, level, :] = product + average_ref[level : level + 1, :]


def analysis_of(combination, deviation_hwm, average_hw):
    levels, width, members = deviation_hwm.shape
    return pl.pallas_call(
        analysis_kernel,
        out_shape=jax.ShapeDtypeStruct((members, levels, width), jnp.float32),
        in_specs=[pl.BlockSpec(memory_space=pltpu.VMEM)] * 3,
        out_specs=pl.BlockSpec(memory_space=pltpu.VMEM),
    )(combination, deviation_hwm, average_hw)

def propagate_model(padded_field, source_term):
    laplacian = (
        padded_field[:, 2:, 1:-1]
        + padded_field[:, :-2, 1:-1]
        + padded_field[:, 1:-1, 2:]
        + padded_field[:, 1:-1, :-2]
        - 4.0 * padded_field[:, 1:-1, 1:-1]
    )
    return padded_field[:, 1:-1, 1:-1] + diffusion * laplacian + heating * source_term


def propagate_members_last(padded_field, source_term):
    laplacian = (
        padded_field[1:-1, 2:]
        + padded_field[1:-1, :-2]
        + padded_field[2:, 1:-1]
        + padded_field[:-2, 1:-1]
        - 4.0 * padded_field[1:-1, 1:-1]
    )
    return padded_field[1:-1, 1:-1] + diffusion * laplacian + heating * source_term


def from_neighbour(block, axis, step):
    count = lax.axis_size(axis)
    if step > 0:
        pairs = [(i, i + 1) for i in range(count - 1)]
    else:
        pairs = [(i + 1, i) for i in range(count - 1)]
    return lax.ppermute(block, axis, pairs)


def forecast_in_pieces(warmth, heat):
    width, height = warmth.shape[0], warmth.shape[1]
    top = from_neighbour(
        jnp.concatenate([warmth[:, -2:], heat[:, -1:]], axis=1), "gx", 1
    )
    bottom = from_neighbour(
        jnp.concatenate([warmth[:, :2], heat[:, :1]], axis=1), "gx", -1
    )
    warmth_tall = jnp.concatenate([top[:, :2], warmth, bottom[:, :2]], axis=1)
    heat_tall = jnp.concatenate([top[:, 2:], heat, bottom[:, 2:]], axis=1)
    edge = jnp.zeros_like(heat_tall[:1, :1])
    left = from_neighbour(
        jnp.concatenate(
            [warmth_tall[-2:], jnp.concatenate([edge, heat_tall[-1:], edge], axis=1)],
            axis=0,
        ),
        "gy",
        1,
    )
    right = from_neighbour(
        jnp.concatenate(
            [warmth_tall[:2], jnp.concatenate([edge, heat_tall[:1], edge], axis=1)],
            axis=0,
        ),
        "gy",
        -1,
    )
    at_x, at_y = lax.axis_index("gx"), lax.axis_index("gy")
    row = lax.broadcasted_iota(jnp.int32, (1, height + 2, 1), 1)
    off_grid = ((row == 0) & (at_x == 0)) | (
        (row == height + 1) & (at_x == lax.axis_size("gx") - 1)
    )
    first_inner = jnp.where(
        off_grid, 0.0, propagate_members_last(warmth_tall, heat_tall[1:-1])
    )
    second_inner = propagate_members_last(first_inner, heat[2:-2])
    first_left = propagate_members_last(
        jnp.concatenate([left[:2], warmth_tall[:2]], axis=0),
        jnp.concatenate([left[2:, 1:-1], heat_tall[:1]], axis=0),
    )
    first_right = propagate_members_last(
        jnp.concatenate([warmth_tall[-2:], right[:2]], axis=0),
        jnp.concatenate([heat_tall[-1:], right[2:, 1:-1]], axis=0),
    )
    col = lax.broadcasted_iota(jnp.int32, (2, 1, 1), 0)
    first_left = jnp.where(off_grid | ((col == 0) & (at_y == 0)), 0.0, first_left)
    first_right = jnp.where(
        off_grid | ((col == 1) & (at_y == lax.axis_size("gy") - 1)), 0.0, first_right
    )
    second_left = propagate_members_last(
        jnp.concatenate([first_left, first_inner[:2]], axis=0), heat[:2]
    )
    second_right = propagate_members_last(
        jnp.concatenate([first_inner[-2:], first_right], axis=0), heat[-2:]
    )
    return [(0, second_left), (2, second_inner), (width - 2, second_right)]


def shards(
    prior_gas_warmth,
    fire_power_output,
    measured_warmth,
    reading_noise_spread,
    reading_local_location,
):
    sample_number, block_height_number, block_width_number = prior_gas_warmth.shape
    warmth_t = jnp.transpose(prior_gas_warmth, (2, 1, 0))
    heat_t = jnp.transpose(fire_power_output, (2, 1, 0))
    pieces = forecast_in_pieces(warmth_t, heat_t)
    mean_heat_t = jnp.mean(heat_t, axis=2)
    heat_anomaly_t = heat_t - mean_heat_t[:, :, None]
    coefficient_line = 1.0 / (reading_noise_spread * math.sqrt(sample_number - 1))
    weight_line = coefficient_line * coefficient_line
    row_hot = (
        (reading_local_location // block_width_number)[:, None]
        == lax.broadcasted_iota(jnp.int32, (1, block_height_number), 1)
    ).astype(jnp.float32)
    col_hot = (
        (reading_local_location % block_width_number)[:, None]
        == lax.broadcasted_iota(jnp.int32, (1, block_width_number), 1)
    ).astype(jnp.float32)
    weighted_rows = jnp.concatenate(
        [row_hot * weight_line[:, None], row_hot * (weight_line * measured_warmth)[:, None]],
        axis=1,
    )
    cell_sums = lax.dot_general(
        col_hot, weighted_rows, (((0,), (0,)), ((), ())), precision=lax.Precision.HIGHEST
    )
    averages, deviations, gram_local, projected = [], [], 0.0, 0.0
    for start, piece in pieces:
        count = piece.shape[0]
        average = jnp.mean(piece, axis=2)
        deviation = piece - average[:, :, None]
        cell_weight = cell_sums[start : start + count, :block_height_number]
        cell_residual = cell_sums[start : start + count, block_height_number:] - average * cell_weight
        gram_local = gram_local + lax.dot_general(
            deviation * cell_weight[:, :, None],
            deviation,
            (((0, 1), (0, 1)), ((), ())),
            precision=lax.Precision.HIGHEST,
        )
        projected = projected + lax.dot_general(
            deviation,
            cell_residual,
            (((0, 1), (0, 1)), ((), ())),
            precision=lax.Precision.HIGHEST,
        )
        averages.append(average)
        deviations.append(deviation)
    average_t = jnp.concatenate(averages, axis=0)
    deviation_t = jnp.concatenate(deviations, axis=0)
    combination_transposed = combination_transposed_of(
        butterfly_sum(jnp.concatenate([gram_local, projected[None, :]], axis=0), ("gx", "gy"))
    )
    updated = analysis_of(
        combination_transposed,
        jnp.transpose(deviation_t, (1, 0, 2)),
        jnp.transpose(average_t),
    )
    heat_out = analysis_of(
        combination_transposed,
        jnp.transpose(heat_anomaly_t, (1, 0, 2)),
        jnp.transpose(mean_heat_t),
    )
    return (updated, heat_out)


def solution(mesh):
    placed = (
        P(None, "gx", "gy"),
        P(None, "gx", "gy"),
        P(("gx", "gy")),
        P(("gx", "gy")),
        P(("gx", "gy")),
    )
    return jax.shard_map(
        shards,
        mesh=mesh,
        in_specs=placed,
        out_specs=(P(None, "gx", "gy"), P(None, "gx", "gy")),
        check_vma=False,
    )
```

```python
import math

import jax
import jax.numpy as jnp
from jax import lax
from jax.experimental import pallas as pl
from jax.experimental.pallas import tpu as pltpu
from jax.sharding import PartitionSpec as P

diffusion = 0.2
heating = 0.5


def xor_tree(received, base, strides):
    if not strides:
        return received[base]
    return xor_tree(received, base, strides[:-1]) + xor_tree(
        received, base ^ strides[-1], strides[:-1]
    )


def butterfly_sum(value, axes):
    for axis in axes:
        count = lax.axis_size(axis)
        if count & (count - 1):
            value = lax.psum(value, axis)
            continue
        bits = [1 << b for b in range(count.bit_length() - 1)]
        for first in range(len(bits)):
            strides = bits[first : first + 1]
            received = {0: value}
            for mask in range(1, 1 << len(strides)):
                offset = 0
                for position, stride in enumerate(strides):
                    if mask >> position & 1:
                        offset ^= stride
                pairs = [(i, i ^ offset) for i in range(count)]
                received[offset] = lax.ppermute(value, axis, pairs)
            value = xor_tree(received, 0, strides)
    return value


def combination_kernel(stacked_ref, combination_ref, work_ref, inverse_ref):
    size = stacked_ref.shape[1]
    square_row = lax.broadcasted_iota(jnp.int32, (size, size), 0)
    square_col = lax.broadcasted_iota(jnp.int32, (size, size), 1)
    unit = jnp.where(square_row == square_col, 1.0, 0.0).astype(jnp.float32)
    work_ref[...] = stacked_ref[:size, :] + unit
    inverse_ref[...] = unit
    lane = lax.broadcasted_iota(jnp.int32, (1, size), 1)

    def pick(vector, where_true, axis):
        return jnp.sum(jnp.where(where_true, vector, 0.0), axis=axis, keepdims=True)

    for first in range(0, size, 8):
        span = size - first
        sublane = lax.broadcasted_iota(jnp.int32, (span, 1), 0) + first
        band_col = lax.broadcasted_iota(jnp.int32, (span, size), 1)

        def step(pair, carry, first=first, sublane=sublane, band_col=band_col):
            k = 2 * pair
            row0 = work_ref[pl.ds(k, 1), :]
            row1 = work_ref[pl.ds(k + 1, 1), :]
            band = work_ref[first:, :]
            col0 = pick(band, band_col == k, 1)
            col1 = pick(band, band_col == k + 1, 1)
            scale0 = 1.0 / jnp.sqrt(pick(row0, lane == k, 1))
            coupling = pick(row0, lane == k + 1, 1) * scale0
            scale1 = 1.0 / jnp.sqrt(pick(row1, lane == k + 1, 1) - coupling * coupling)
            factor_row0 = jnp.where(lane >= k, row0 * scale0, 0.0)
            factor_row1 = jnp.where(lane >= k + 1, (row1 - coupling * factor_row0) * scale1, 0.0)
            factor_col0 = jnp.where(sublane >= k, col0 * scale0, 0.0)
            factor_col1 = jnp.where(
                sublane >= k + 1, (col1 - factor_col0 * coupling) * scale1, 0.0
            )
            work_ref[first:, :] = band - factor_col0 * factor_row0 - factor_col1 * factor_row1
            inverse_row0 = inverse_ref[pl.ds(k, 1), :] * scale0
            inverse_row1 = (inverse_ref[pl.ds(k + 1, 1), :] - coupling * inverse_row0) * scale1
            below0 = jnp.where(sublane > k + 1, factor_col0, 0.0)
            below1 = jnp.where(sublane > k + 1, factor_col1, 0.0)
            inverse_ref[first:, :] = (
                inverse_ref[first:, :] - below0 * inverse_row0 - below1 * inverse_row1
            )
            inverse_ref[pl.ds(k, 1), :] = inverse_row0
            inverse_ref[pl.ds(k + 1, 1), :] = inverse_row1
            return carry

        lax.fori_loop(first // 2, min(first + 8, size) // 2, step, 0)
    lower_inverse = inverse_ref[...]
    projected_row = stacked_ref[size : size + 1, :]
    whitened = jnp.sum(lower_inverse * projected_row, axis=1, keepdims=True)
    mean_weights = jnp.sum(lower_inverse * whitened, axis=0, keepdims=True)
    combination_ref[...] = lower_inverse + mean_weights


def combination_transposed_of(stacked):
    size = stacked.shape[1]
    return pl.pallas_call(
        combination_kernel,
        out_shape=jax.ShapeDtypeStruct((size, size), jnp.float32),
        in_specs=[pl.BlockSpec(memory_space=pltpu.VMEM)],
        out_specs=pl.BlockSpec(memory_space=pltpu.VMEM),
        scratch_shapes=[pltpu.VMEM((size, size), jnp.float32)] * 2,
    )(stacked)

def propagate_model(padded_field, source_term):
    laplacian = (
        padded_field[:, 2:, 1:-1]
        + padded_field[:, :-2, 1:-1]
        + padded_field[:, 1:-1, 2:]
        + padded_field[:, 1:-1, :-2]
        - 4.0 * padded_field[:, 1:-1, 1:-1]
    )
    return padded_field[:, 1:-1, 1:-1] + diffusion * laplacian + heating * source_term


def propagate_members_last(padded_field, source_term):
    laplacian = (
        padded_field[1:-1, 2:]
        + padded_field[1:-1, :-2]
        + padded_field[2:, 1:-1]
        + padded_field[:-2, 1:-1]
        - 4.0 * padded_field[1:-1, 1:-1]
    )
    return padded_field[1:-1, 1:-1] + diffusion * laplacian + heating * source_term


def from_neighbour(block, axis, step):
    count = lax.axis_size(axis)
    if step > 0:
        pairs = [(i, i + 1) for i in range(count - 1)]
    else:
        pairs = [(i + 1, i) for i in range(count - 1)]
    return lax.ppermute(block, axis, pairs)


def forecast_in_pieces(warmth, heat):
    width, height = warmth.shape[0], warmth.shape[1]
    left = from_neighbour(jnp.concatenate([warmth[-2:], heat[-1:]], axis=0), "gy", 1)
    right = from_neighbour(jnp.concatenate([warmth[:2], heat[:1]], axis=0), "gy", -1)
    warmth_wide = jnp.concatenate([left[:2], warmth, right[:2]], axis=0)
    heat_wide = jnp.concatenate([left[2:], heat, right[2:]], axis=0)
    edge = jnp.zeros_like(heat_wide[:1, :1])
    top = from_neighbour(
        jnp.concatenate(
            [warmth_wide[:, -2:], jnp.concatenate([edge, heat_wide[:, -1:], edge], axis=0)],
            axis=1,
        ),
        "gx",
        1,
    )
    bottom = from_neighbour(
        jnp.concatenate(
            [warmth_wide[:, :2], jnp.concatenate([edge, heat_wide[:, :1], edge], axis=0)],
            axis=1,
        ),
        "gx",
        -1,
    )
    at_x, at_y = lax.axis_index("gx"), lax.axis_index("gy")
    col = lax.broadcasted_iota(jnp.int32, (width + 2, 1, 1), 0)
    off_grid = ((col == 0) & (at_y == 0)) | (
        (col == width + 1) & (at_y == lax.axis_size("gy") - 1)
    )
    first_inner = jnp.where(
        off_grid, 0.0, propagate_members_last(warmth_wide, heat_wide[:, 1:-1])
    )
    second_inner = propagate_members_last(first_inner, heat[:, 2:-2])
    first_top = propagate_members_last(
        jnp.concatenate([top[:, :2], warmth_wide[:, :2]], axis=1),
        jnp.concatenate([top[1:-1, 2:], heat_wide[:, :1]], axis=1),
    )
    first_bottom = propagate_members_last(
        jnp.concatenate([warmth_wide[:, -2:], bottom[:, :2]], axis=1),
        jnp.concatenate([heat_wide[:, -1:], bottom[1:-1, 2:]], axis=1),
    )
    row = lax.broadcasted_iota(jnp.int32, (1, 2, 1), 1)
    first_top = jnp.where(off_grid | ((row == 0) & (at_x == 0)), 0.0, first_top)
    first_bottom = jnp.where(
        off_grid | ((row == 1) & (at_x == lax.axis_size("gx") - 1)), 0.0, first_bottom
    )
    second_top = propagate_members_last(
        jnp.concatenate([first_top, first_inner[:, :2]], axis=1), heat[:, :2]
    )
    second_bottom = propagate_members_last(
        jnp.concatenate([first_inner[:, -2:], first_bottom], axis=1), heat[:, -2:]
    )
    return [(0, second_top), (2, second_inner), (height - 2, second_bottom)]


def shards(
    prior_gas_warmth,
    fire_power_output,
    measured_warmth,
    reading_noise_spread,
    reading_local_location,
):
    sample_number, block_height_number, block_width_number = prior_gas_warmth.shape
    warmth_t = jnp.transpose(prior_gas_warmth, (2, 1, 0))
    heat_t = jnp.transpose(fire_power_output, (2, 1, 0))
    pieces = forecast_in_pieces(warmth_t, heat_t)
    mean_heat_t = jnp.mean(heat_t, axis=2)
    heat_anomaly_t = heat_t - mean_heat_t[:, :, None]
    coefficient_line = 1.0 / (reading_noise_spread * math.sqrt(sample_number - 1))
    weight_line = coefficient_line * coefficient_line
    row_hot = (
        (reading_local_location // block_width_number)[:, None]
        == lax.broadcasted_iota(jnp.int32, (1, block_height_number), 1)
    ).astype(jnp.float32)
    col_hot = (
        (reading_local_location % block_width_number)[:, None]
        == lax.broadcasted_iota(jnp.int32, (1, block_width_number), 1)
    ).astype(jnp.float32)
    weighted_rows = jnp.concatenate(
        [row_hot * weight_line[:, None], row_hot * (weight_line * measured_warmth)[:, None]],
        axis=1,
    )
    cell_sums = lax.dot_general(
        col_hot, weighted_rows, (((0,), (0,)), ((), ())), precision=lax.Precision.HIGHEST
    )
    averages, deviations, gram_local, projected = [], [], 0.0, 0.0
    for start, piece in pieces:
        count = piece.shape[1]
        average = jnp.mean(piece, axis=2)
        deviation = piece - average[:, :, None]
        cell_weight = cell_sums[:, start : start + count]
        cell_residual = (
            cell_sums[:, block_height_number + start : block_height_number + start + count]
            - average * cell_weight
        )
        gram_local = gram_local + lax.dot_general(
            deviation * cell_weight[:, :, None],
            deviation,
            (((0, 1), (0, 1)), ((), ())),
            precision=lax.Precision.HIGHEST,
        )
        projected = projected + lax.dot_general(
            deviation,
            cell_residual,
            (((0, 1), (0, 1)), ((), ())),
            precision=lax.Precision.HIGHEST,
        )
        averages.append(average)
        deviations.append(deviation)
    average_t = jnp.concatenate(averages, axis=1)
    deviation_t = jnp.concatenate(deviations, axis=1)
    combination_transposed = combination_transposed_of(
        butterfly_sum(jnp.concatenate([gram_local, projected[None, :]], axis=0), ("gx", "gy"))
    )
    contract = (((2,), (1,)), ((), ()))
    updated_t = average_t[:, :, None] + lax.dot_general(
        deviation_t, combination_transposed, contract, precision=lax.Precision.HIGHEST
    )
    heat_out_t = mean_heat_t[:, :, None] + lax.dot_general(
        heat_anomaly_t, combination_transposed, contract, precision=lax.Precision.HIGHEST
    )
    return (jnp.transpose(updated_t, (2, 1, 0)), jnp.transpose(heat_out_t, (2, 1, 0)))


def solution(mesh):
    placed = (
        P(None, "gx", "gy"),
        P(None, "gx", "gy"),
        P(("gx", "gy")),
        P(("gx", "gy")),
        P(("gx", "gy")),
    )
    return jax.shard_map(
        shards,
        mesh=mesh,
        in_specs=placed,
        out_specs=(P(None, "gx", "gy"), P(None, "gx", "gy")),
        check_vma=False,
    )
```

```python
import math

import jax
import jax.numpy as jnp
from jax import lax
from jax.experimental import pallas as pl
from jax.experimental.pallas import tpu as pltpu
from jax.sharding import PartitionSpec as P

diffusion = 0.2
heating = 0.5


def xor_tree(received, base, strides):
    if not strides:
        return received[base]
    return xor_tree(received, base, strides[:-1]) + xor_tree(
        received, base ^ strides[-1], strides[:-1]
    )


def butterfly_sum(value, axes):
    for axis in axes:
        count = lax.axis_size(axis)
        if count & (count - 1):
            value = lax.psum(value, axis)
            continue
        bits = [1 << b for b in range(count.bit_length() - 1)]
        for first in range(0, len(bits), 2):
            strides = bits[first : first + 2]
            received = {0: value}
            for mask in range(1, 1 << len(strides)):
                offset = 0
                for position, stride in enumerate(strides):
                    if mask >> position & 1:
                        offset ^= stride
                pairs = [(i, i ^ offset) for i in range(count)]
                received[offset] = lax.ppermute(value, axis, pairs)
            value = xor_tree(received, 0, strides)
    return value


def combination_kernel(stacked_ref, combination_ref, work_ref, inverse_ref):
    size = stacked_ref.shape[1]
    square_row = lax.broadcasted_iota(jnp.int32, (size, size), 0)
    square_col = lax.broadcasted_iota(jnp.int32, (size, size), 1)
    unit = jnp.where(square_row == square_col, 1.0, 0.0).astype(jnp.float32)
    work_ref[...] = stacked_ref[:size, :] + unit
    inverse_ref[...] = unit
    lane = lax.broadcasted_iota(jnp.int32, (1, size), 1)

    def pick(vector, where_true, axis):
        return jnp.sum(jnp.where(where_true, vector, 0.0), axis=axis, keepdims=True)

    for first in range(0, size, 8):
        span = size - first
        sublane = lax.broadcasted_iota(jnp.int32, (span, 1), 0) + first
        band_col = lax.broadcasted_iota(jnp.int32, (span, size), 1)

        def step(pair, carry, first=first, sublane=sublane, band_col=band_col):
            k = 2 * pair
            row0 = work_ref[pl.ds(k, 1), :]
            row1 = work_ref[pl.ds(k + 1, 1), :]
            band = work_ref[first:, :]
            col0 = pick(band, band_col == k, 1)
            col1 = pick(band, band_col == k + 1, 1)
            scale0 = 1.0 / jnp.sqrt(pick(row0, lane == k, 1))
            coupling = pick(row0, lane == k + 1, 1) * scale0
            scale1 = 1.0 / jnp.sqrt(pick(row1, lane == k + 1, 1) - coupling * coupling)
            factor_row0 = jnp.where(lane >= k, row0 * scale0, 0.0)
            factor_row1 = jnp.where(lane >= k + 1, (row1 - coupling * factor_row0) * scale1, 0.0)
            factor_col0 = jnp.where(sublane >= k, col0 * scale0, 0.0)
            factor_col1 = jnp.where(
                sublane >= k + 1, (col1 - factor_col0 * coupling) * scale1, 0.0
            )
            work_ref[first:, :] = band - factor_col0 * factor_row0 - factor_col1 * factor_row1
            inverse_row0 = inverse_ref[pl.ds(k, 1), :] * scale0
            inverse_row1 = (inverse_ref[pl.ds(k + 1, 1), :] - coupling * inverse_row0) * scale1
            below0 = jnp.where(sublane > k + 1, factor_col0, 0.0)
            below1 = jnp.where(sublane > k + 1, factor_col1, 0.0)
            inverse_ref[first:, :] = (
                inverse_ref[first:, :] - below0 * inverse_row0 - below1 * inverse_row1
            )
            inverse_ref[pl.ds(k, 1), :] = inverse_row0
            inverse_ref[pl.ds(k + 1, 1), :] = inverse_row1
            return carry

        lax.fori_loop(first // 2, min(first + 8, size) // 2, step, 0)
    lower_inverse = inverse_ref[...]
    projected_row = stacked_ref[size : size + 1, :]
    whitened = jnp.sum(lower_inverse * projected_row, axis=1, keepdims=True)
    mean_weights = jnp.sum(lower_inverse * whitened, axis=0, keepdims=True)
    combination_ref[...] = lower_inverse + mean_weights


def combination_transposed_of(stacked):
    size = stacked.shape[1]
    return pl.pallas_call(
        combination_kernel,
        out_shape=jax.ShapeDtypeStruct((size, size), jnp.float32),
        in_specs=[pl.BlockSpec(memory_space=pltpu.VMEM)],
        out_specs=pl.BlockSpec(memory_space=pltpu.VMEM),
        scratch_shapes=[pltpu.VMEM((size, size), jnp.float32)] * 2,
    )(stacked)

def propagate_model(padded_field, source_term):
    laplacian = (
        padded_field[:, 2:, 1:-1]
        + padded_field[:, :-2, 1:-1]
        + padded_field[:, 1:-1, 2:]
        + padded_field[:, 1:-1, :-2]
        - 4.0 * padded_field[:, 1:-1, 1:-1]
    )
    return padded_field[:, 1:-1, 1:-1] + diffusion * laplacian + heating * source_term


def propagate_members_last(padded_field, source_term):
    laplacian = (
        padded_field[1:-1, 2:]
        + padded_field[1:-1, :-2]
        + padded_field[2:, 1:-1]
        + padded_field[:-2, 1:-1]
        - 4.0 * padded_field[1:-1, 1:-1]
    )
    return padded_field[1:-1, 1:-1] + diffusion * laplacian + heating * source_term


def from_neighbour(block, axis, step):
    count = lax.axis_size(axis)
    if step > 0:
        pairs = [(i, i + 1) for i in range(count - 1)]
    else:
        pairs = [(i + 1, i) for i in range(count - 1)]
    return lax.ppermute(block, axis, pairs)


def forecast_in_pieces(warmth, heat):
    width, height = warmth.shape[0], warmth.shape[1]
    left = from_neighbour(jnp.concatenate([warmth[-2:], heat[-1:]], axis=0), "gy", 1)
    right = from_neighbour(jnp.concatenate([warmth[:2], heat[:1]], axis=0), "gy", -1)
    warmth_wide = jnp.concatenate([left[:2], warmth, right[:2]], axis=0)
    heat_wide = jnp.concatenate([left[2:], heat, right[2:]], axis=0)
    edge = jnp.zeros_like(heat_wide[:1, :1])
    top = from_neighbour(
        jnp.concatenate(
            [warmth_wide[:, -2:], jnp.concatenate([edge, heat_wide[:, -1:], edge], axis=0)],
            axis=1,
        ),
        "gx",
        1,
    )
    bottom = from_neighbour(
        jnp.concatenate(
            [warmth_wide[:, :2], jnp.concatenate([edge, heat_wide[:, :1], edge], axis=0)],
            axis=1,
        ),
        "gx",
        -1,
    )
    at_x, at_y = lax.axis_index("gx"), lax.axis_index("gy")
    col = lax.broadcasted_iota(jnp.int32, (width + 2, 1, 1), 0)
    off_grid = ((col == 0) & (at_y == 0)) | (
        (col == width + 1) & (at_y == lax.axis_size("gy") - 1)
    )
    first_inner = jnp.where(
        off_grid, 0.0, propagate_members_last(warmth_wide, heat_wide[:, 1:-1])
    )
    second_inner = propagate_members_last(first_inner, heat[:, 2:-2])
    first_top = propagate_members_last(
        jnp.concatenate([top[:, :2], warmth_wide[:, :2]], axis=1),
        jnp.concatenate([top[1:-1, 2:], heat_wide[:, :1]], axis=1),
    )
    first_bottom = propagate_members_last(
        jnp.concatenate([warmth_wide[:, -2:], bottom[:, :2]], axis=1),
        jnp.concatenate([heat_wide[:, -1:], bottom[1:-1, 2:]], axis=1),
    )
    row = lax.broadcasted_iota(jnp.int32, (1, 2, 1), 1)
    first_top = jnp.where(off_grid | ((row == 0) & (at_x == 0)), 0.0, first_top)
    first_bottom = jnp.where(
        off_grid | ((row == 1) & (at_x == lax.axis_size("gx") - 1)), 0.0, first_bottom
    )
    second_top = propagate_members_last(
        jnp.concatenate([first_top, first_inner[:, :2]], axis=1), heat[:, :2]
    )
    second_bottom = propagate_members_last(
        jnp.concatenate([first_inner[:, -2:], first_bottom], axis=1), heat[:, -2:]
    )
    return [(0, second_top), (2, second_inner), (height - 2, second_bottom)]


def shards(
    prior_gas_warmth,
    fire_power_output,
    measured_warmth,
    reading_noise_spread,
    reading_local_location,
):
    sample_number, block_height_number, block_width_number = prior_gas_warmth.shape
    warmth_t = jnp.transpose(prior_gas_warmth, (2, 1, 0))
    heat_t = jnp.transpose(fire_power_output, (2, 1, 0))
    pieces = forecast_in_pieces(warmth_t, heat_t)
    mean_heat_t = jnp.mean(heat_t, axis=2)
    heat_anomaly_t = heat_t - mean_heat_t[:, :, None]
    coefficient_line = 1.0 / (reading_noise_spread * math.sqrt(sample_number - 1))
    weight_line = coefficient_line * coefficient_line
    row_hot = (
        (reading_local_location // block_width_number)[:, None]
        == lax.broadcasted_iota(jnp.int32, (1, block_height_number), 1)
    ).astype(jnp.float32)
    col_hot = (
        (reading_local_location % block_width_number)[:, None]
        == lax.broadcasted_iota(jnp.int32, (1, block_width_number), 1)
    ).astype(jnp.float32)
    weighted_rows = jnp.concatenate(
        [row_hot * weight_line[:, None], row_hot * (weight_line * measured_warmth)[:, None]],
        axis=1,
    )
    cell_sums = lax.dot_general(
        col_hot, weighted_rows, (((0,), (0,)), ((), ())), precision=lax.Precision.HIGHEST
    )
    averages, deviations, gram_local, projected = [], [], 0.0, 0.0
    for start, piece in pieces:
        count = piece.shape[1]
        average = jnp.mean(piece, axis=2)
        deviation = piece - average[:, :, None]
        cell_weight = cell_sums[:, start : start + count]
        cell_residual = (
            cell_sums[:, block_height_number + start : block_height_number + start + count]
            - average * cell_weight
        )
        gram_local = gram_local + lax.dot_general(
            deviation * cell_weight[:, :, None],
            deviation,
            (((0, 1), (0, 1)), ((), ())),
            precision=lax.Precision.HIGHEST,
        )
        projected = projected + lax.dot_general(
            deviation,
            cell_residual,
            (((0, 1), (0, 1)), ((), ())),
            precision=lax.Precision.HIGHEST,
        )
        averages.append(average)
        deviations.append(deviation)
    average_t = jnp.concatenate(averages, axis=1)
    deviation_t = jnp.concatenate(deviations, axis=1)
    combination_transposed = combination_transposed_of(
        butterfly_sum(jnp.concatenate([gram_local, projected[None, :]], axis=0), ("gx", "gy"))
    )
    contract = (((2,), (1,)), ((), ()))
    updated_t = average_t[:, :, None] + lax.dot_general(
        deviation_t, combination_transposed, contract, precision=lax.Precision.HIGHEST
    )
    heat_out_t = mean_heat_t[:, :, None] + lax.dot_general(
        heat_anomaly_t, combination_transposed, contract, precision=lax.Precision.HIGHEST
    )
    return (jnp.transpose(updated_t, (2, 1, 0)), jnp.transpose(heat_out_t, (2, 1, 0)))


def solution(mesh):
    placed = (
        P(None, "gx", "gy"),
        P(None, "gx", "gy"),
        P(("gx", "gy")),
        P(("gx", "gy")),
        P(("gx", "gy")),
    )
    return jax.shard_map(
        shards,
        mesh=mesh,
        in_specs=placed,
        out_specs=(P(None, "gx", "gy"), P(None, "gx", "gy")),
        check_vma=False,
    )
```

```python
import math

import jax
import jax.numpy as jnp
from jax import lax
from jax.experimental import pallas as pl
from jax.experimental.pallas import tpu as pltpu
from jax.sharding import PartitionSpec as P

diffusion = 0.2
heating = 0.5


def xor_tree(received, base, strides):
    if not strides:
        return received[base]
    return xor_tree(received, base, strides[:-1]) + xor_tree(
        received, base ^ strides[-1], strides[:-1]
    )


def butterfly_sum(value, axes):
    for axis in axes:
        count = lax.axis_size(axis)
        if count & (count - 1):
            value = lax.psum(value, axis)
            continue
        bits = [1 << b for b in range(count.bit_length() - 1)]
        for first in range(len(bits)):
            strides = bits[first : first + 1]
            received = {0: value}
            for mask in range(1, 1 << len(strides)):
                offset = 0
                for position, stride in enumerate(strides):
                    if mask >> position & 1:
                        offset ^= stride
                pairs = [(i, i ^ offset) for i in range(count)]
                received[offset] = lax.ppermute(value, axis, pairs)
            value = xor_tree(received, 0, strides)
    return value


def butterfly_terms(value, axes):
    *early, last = axes
    value = butterfly_sum(value, early)
    count = lax.axis_size(last)
    if count == 1 or count & (count - 1):
        return butterfly_sum(value, [last]), jnp.zeros_like(value)
    stride = count // 2
    value = butterfly_sum_bits(value, last, count, stride)
    pairs = [(i, i ^ stride) for i in range(count)]
    return value, lax.ppermute(value, last, pairs)


def butterfly_sum_bits(value, axis, count, limit):
    stride = 1
    while stride < limit:
        pairs = [(i, i ^ stride) for i in range(count)]
        value = value + lax.ppermute(value, axis, pairs)
        stride *= 2
    return value


def combination_kernel(own_ref, other_ref, combination_ref, work_ref, inverse_ref):
    size = own_ref.shape[1]
    square_row = lax.broadcasted_iota(jnp.int32, (size, size), 0)
    square_col = lax.broadcasted_iota(jnp.int32, (size, size), 1)
    unit = jnp.where(square_row == square_col, 1.0, 0.0).astype(jnp.float32)
    work_ref[...] = (own_ref[:size, :] + other_ref[:size, :]) + unit
    inverse_ref[...] = unit
    lane = lax.broadcasted_iota(jnp.int32, (1, size), 1)

    def pick(vector, where_true, axis):
        return jnp.sum(jnp.where(where_true, vector, 0.0), axis=axis, keepdims=True)

    for first in range(0, size, 8):
        span = size - first
        sublane = lax.broadcasted_iota(jnp.int32, (span, 1), 0) + first
        band_col = lax.broadcasted_iota(jnp.int32, (span, size), 1)

        def step(pair, carry, first=first, sublane=sublane, band_col=band_col):
            k = 2 * pair
            row0 = work_ref[pl.ds(k, 1), :]
            row1 = work_ref[pl.ds(k + 1, 1), :]
            band = work_ref[first:, :]
            col0 = pick(band, band_col == k, 1)
            col1 = pick(band, band_col == k + 1, 1)
            scale0 = 1.0 / jnp.sqrt(pick(row0, lane == k, 1))
            coupling = pick(row0, lane == k + 1, 1) * scale0
            scale1 = 1.0 / jnp.sqrt(pick(row1, lane == k + 1, 1) - coupling * coupling)
            factor_row0 = jnp.where(lane >= k, row0 * scale0, 0.0)
            factor_row1 = jnp.where(lane >= k + 1, (row1 - coupling * factor_row0) * scale1, 0.0)
            factor_col0 = jnp.where(sublane >= k, col0 * scale0, 0.0)
            factor_col1 = jnp.where(
                sublane >= k + 1, (col1 - factor_col0 * coupling) * scale1, 0.0
            )
            work_ref[first:, :] = band - factor_col0 * factor_row0 - factor_col1 * factor_row1
            inverse_row0 = inverse_ref[pl.ds(k, 1), :] * scale0
            inverse_row1 = (inverse_ref[pl.ds(k + 1, 1), :] - coupling * inverse_row0) * scale1
            below0 = jnp.where(sublane > k + 1, factor_col0, 0.0)
            below1 = jnp.where(sublane > k + 1, factor_col1, 0.0)
            inverse_ref[first:, :] = (
                inverse_ref[first:, :] - below0 * inverse_row0 - below1 * inverse_row1
            )
            inverse_ref[pl.ds(k, 1), :] = inverse_row0
            inverse_ref[pl.ds(k + 1, 1), :] = inverse_row1
            return carry

        lax.fori_loop(first // 2, min(first + 8, size) // 2, step, 0)
    lower_inverse = inverse_ref[...]
    projected_row = own_ref[size : size + 1, :] + other_ref[size : size + 1, :]
    whitened = jnp.sum(lower_inverse * projected_row, axis=1, keepdims=True)
    mean_weights = jnp.sum(lower_inverse * whitened, axis=0, keepdims=True)
    combination_ref[...] = lower_inverse + mean_weights


def combination_transposed_of(own, other):
    size = own.shape[1]
    return pl.pallas_call(
        combination_kernel,
        out_shape=jax.ShapeDtypeStruct((size, size), jnp.float32),
        in_specs=[pl.BlockSpec(memory_space=pltpu.VMEM)] * 2,
        out_specs=pl.BlockSpec(memory_space=pltpu.VMEM),
        scratch_shapes=[pltpu.VMEM((size, size), jnp.float32)] * 2,
    )(own, other)

def propagate_model(padded_field, source_term):
    laplacian = (
        padded_field[:, 2:, 1:-1]
        + padded_field[:, :-2, 1:-1]
        + padded_field[:, 1:-1, 2:]
        + padded_field[:, 1:-1, :-2]
        - 4.0 * padded_field[:, 1:-1, 1:-1]
    )
    return padded_field[:, 1:-1, 1:-1] + diffusion * laplacian + heating * source_term


def propagate_members_last(padded_field, source_term):
    laplacian = (
        padded_field[1:-1, 2:]
        + padded_field[1:-1, :-2]
        + padded_field[2:, 1:-1]
        + padded_field[:-2, 1:-1]
        - 4.0 * padded_field[1:-1, 1:-1]
    )
    return padded_field[1:-1, 1:-1] + diffusion * laplacian + heating * source_term


def from_neighbour(block, axis, step):
    count = lax.axis_size(axis)
    if step > 0:
        pairs = [(i, i + 1) for i in range(count - 1)]
    else:
        pairs = [(i + 1, i) for i in range(count - 1)]
    return lax.ppermute(block, axis, pairs)


def forecast_in_pieces(warmth, heat):
    width, height = warmth.shape[0], warmth.shape[1]
    left = from_neighbour(jnp.concatenate([warmth[-2:], heat[-1:]], axis=0), "gy", 1)
    right = from_neighbour(jnp.concatenate([warmth[:2], heat[:1]], axis=0), "gy", -1)
    warmth_wide = jnp.concatenate([left[:2], warmth, right[:2]], axis=0)
    heat_wide = jnp.concatenate([left[2:], heat, right[2:]], axis=0)
    edge = jnp.zeros_like(heat_wide[:1, :1])
    top = from_neighbour(
        jnp.concatenate(
            [warmth_wide[:, -2:], jnp.concatenate([edge, heat_wide[:, -1:], edge], axis=0)],
            axis=1,
        ),
        "gx",
        1,
    )
    bottom = from_neighbour(
        jnp.concatenate(
            [warmth_wide[:, :2], jnp.concatenate([edge, heat_wide[:, :1], edge], axis=0)],
            axis=1,
        ),
        "gx",
        -1,
    )
    at_x, at_y = lax.axis_index("gx"), lax.axis_index("gy")
    col = lax.broadcasted_iota(jnp.int32, (width + 2, 1, 1), 0)
    off_grid = ((col == 0) & (at_y == 0)) | (
        (col == width + 1) & (at_y == lax.axis_size("gy") - 1)
    )
    first_inner = jnp.where(
        off_grid, 0.0, propagate_members_last(warmth_wide, heat_wide[:, 1:-1])
    )
    second_inner = propagate_members_last(first_inner, heat[:, 2:-2])
    first_top = propagate_members_last(
        jnp.concatenate([top[:, :2], warmth_wide[:, :2]], axis=1),
        jnp.concatenate([top[1:-1, 2:], heat_wide[:, :1]], axis=1),
    )
    first_bottom = propagate_members_last(
        jnp.concatenate([warmth_wide[:, -2:], bottom[:, :2]], axis=1),
        jnp.concatenate([heat_wide[:, -1:], bottom[1:-1, 2:]], axis=1),
    )
    row = lax.broadcasted_iota(jnp.int32, (1, 2, 1), 1)
    first_top = jnp.where(off_grid | ((row == 0) & (at_x == 0)), 0.0, first_top)
    first_bottom = jnp.where(
        off_grid | ((row == 1) & (at_x == lax.axis_size("gx") - 1)), 0.0, first_bottom
    )
    second_top = propagate_members_last(
        jnp.concatenate([first_top, first_inner[:, :2]], axis=1), heat[:, :2]
    )
    second_bottom = propagate_members_last(
        jnp.concatenate([first_inner[:, -2:], first_bottom], axis=1), heat[:, -2:]
    )
    return [(0, second_top), (2, second_inner), (height - 2, second_bottom)]


def shards(
    prior_gas_warmth,
    fire_power_output,
    measured_warmth,
    reading_noise_spread,
    reading_local_location,
):
    sample_number, block_height_number, block_width_number = prior_gas_warmth.shape
    warmth_t = jnp.transpose(prior_gas_warmth, (2, 1, 0))
    heat_t = jnp.transpose(fire_power_output, (2, 1, 0))
    pieces = forecast_in_pieces(warmth_t, heat_t)
    mean_heat_t = jnp.mean(heat_t, axis=2)
    heat_anomaly_t = heat_t - mean_heat_t[:, :, None]
    coefficient_line = 1.0 / (reading_noise_spread * math.sqrt(sample_number - 1))
    weight_line = coefficient_line * coefficient_line
    row_hot = (
        (reading_local_location // block_width_number)[:, None]
        == lax.broadcasted_iota(jnp.int32, (1, block_height_number), 1)
    ).astype(jnp.float32)
    col_hot = (
        (reading_local_location % block_width_number)[:, None]
        == lax.broadcasted_iota(jnp.int32, (1, block_width_number), 1)
    ).astype(jnp.float32)
    weighted_rows = jnp.concatenate(
        [row_hot * weight_line[:, None], row_hot * (weight_line * measured_warmth)[:, None]],
        axis=1,
    )
    cell_sums = lax.dot_general(
        col_hot, weighted_rows, (((0,), (0,)), ((), ())), precision=lax.Precision.HIGHEST
    )
    averages, deviations, gram_local, projected = [], [], 0.0, 0.0
    for start, piece in pieces:
        count = piece.shape[1]
        average = jnp.mean(piece, axis=2)
        deviation = piece - average[:, :, None]
        cell_weight = cell_sums[:, start : start + count]
        cell_residual = (
            cell_sums[:, block_height_number + start : block_height_number + start + count]
            - average * cell_weight
        )
        gram_local = gram_local + lax.dot_general(
            deviation * cell_weight[:, :, None],
            deviation,
            (((0, 1), (0, 1)), ((), ())),
            precision=lax.Precision.HIGHEST,
        )
        projected = projected + lax.dot_general(
            deviation,
            cell_residual,
            (((0, 1), (0, 1)), ((), ())),
            precision=lax.Precision.HIGHEST,
        )
        averages.append(average)
        deviations.append(deviation)
    average_t = jnp.concatenate(averages, axis=1)
    deviation_t = jnp.concatenate(deviations, axis=1)
    combination_transposed = combination_transposed_of(
        *butterfly_terms(jnp.concatenate([gram_local, projected[None, :]], axis=0), ("gx", "gy"))
    )
    contract = (((2,), (1,)), ((), ()))
    updated_t = average_t[:, :, None] + lax.dot_general(
        deviation_t, combination_transposed, contract, precision=lax.Precision.HIGHEST
    )
    heat_out_t = mean_heat_t[:, :, None] + lax.dot_general(
        heat_anomaly_t, combination_transposed, contract, precision=lax.Precision.HIGHEST
    )
    return (jnp.transpose(updated_t, (2, 1, 0)), jnp.transpose(heat_out_t, (2, 1, 0)))


def solution(mesh):
    placed = (
        P(None, "gx", "gy"),
        P(None, "gx", "gy"),
        P(("gx", "gy")),
        P(("gx", "gy")),
        P(("gx", "gy")),
    )
    return jax.shard_map(
        shards,
        mesh=mesh,
        in_specs=placed,
        out_specs=(P(None, "gx", "gy"), P(None, "gx", "gy")),
        check_vma=False,
    )
```

```python
import math

import jax
import jax.numpy as jnp
from jax import lax
from jax.experimental import pallas as pl
from jax.experimental.pallas import tpu as pltpu
from jax.sharding import PartitionSpec as P

diffusion = 0.2
heating = 0.5


def xor_tree(received, base, strides):
    if not strides:
        return received[base]
    return xor_tree(received, base, strides[:-1]) + xor_tree(
        received, base ^ strides[-1], strides[:-1]
    )


def butterfly_sum(value, axes):
    for axis in axes:
        count = lax.axis_size(axis)
        if count & (count - 1):
            value = lax.psum(value, axis)
            continue
        bits = [1 << b for b in range(count.bit_length() - 1)]
        for first in range(len(bits)):
            strides = bits[first : first + 1]
            received = {0: value}
            for mask in range(1, 1 << len(strides)):
                offset = 0
                for position, stride in enumerate(strides):
                    if mask >> position & 1:
                        offset ^= stride
                pairs = [(i, i ^ offset) for i in range(count)]
                received[offset] = lax.ppermute(value, axis, pairs)
            value = xor_tree(received, 0, strides)
    return value


def combination_kernel(stacked_ref, combination_ref, work_ref, inverse_ref):
    size = stacked_ref.shape[1]
    square_row = lax.broadcasted_iota(jnp.int32, (size, size), 0)
    square_col = lax.broadcasted_iota(jnp.int32, (size, size), 1)
    unit = jnp.where(square_row == square_col, 1.0, 0.0).astype(jnp.float32)
    work_ref[...] = stacked_ref[:size, :] + unit
    inverse_ref[...] = unit
    lane = lax.broadcasted_iota(jnp.int32, (1, size), 1)

    def pick(vector, where_true, axis):
        return jnp.sum(jnp.where(where_true, vector, 0.0), axis=axis, keepdims=True)

    for first in range(0, size, 8):
        span = size - first
        sublane = lax.broadcasted_iota(jnp.int32, (span, 1), 0) + first
        band_col = lax.broadcasted_iota(jnp.int32, (span, size), 1)

        def step(pair, carry, first=first, sublane=sublane, band_col=band_col):
            k = 2 * pair
            row0 = work_ref[pl.ds(k, 1), :]
            row1 = work_ref[pl.ds(k + 1, 1), :]
            band = work_ref[first:, :]
            col0 = pick(band, band_col == k, 1)
            col1 = pick(band, band_col == k + 1, 1)
            scale0 = 1.0 / jnp.sqrt(pick(row0, lane == k, 1))
            coupling = pick(row0, lane == k + 1, 1) * scale0
            scale1 = 1.0 / jnp.sqrt(pick(row1, lane == k + 1, 1) - coupling * coupling)
            factor_row0 = jnp.where(lane >= k, row0 * scale0, 0.0)
            factor_row1 = jnp.where(lane >= k + 1, (row1 - coupling * factor_row0) * scale1, 0.0)
            factor_col0 = jnp.where(sublane >= k, col0 * scale0, 0.0)
            factor_col1 = jnp.where(
                sublane >= k + 1, (col1 - factor_col0 * coupling) * scale1, 0.0
            )
            work_ref[first:, :] = band - factor_col0 * factor_row0 - factor_col1 * factor_row1
            inverse_row0 = inverse_ref[pl.ds(k, 1), :] * scale0
            inverse_row1 = (inverse_ref[pl.ds(k + 1, 1), :] - coupling * inverse_row0) * scale1
            below0 = jnp.where(sublane > k + 1, factor_col0, 0.0)
            below1 = jnp.where(sublane > k + 1, factor_col1, 0.0)
            inverse_ref[first:, :] = (
                inverse_ref[first:, :] - below0 * inverse_row0 - below1 * inverse_row1
            )
            inverse_ref[pl.ds(k, 1), :] = inverse_row0
            inverse_ref[pl.ds(k + 1, 1), :] = inverse_row1
            return carry

        lax.fori_loop(first // 2, min(first + 8, size) // 2, step, 0)
    lower_inverse = inverse_ref[...]
    projected_row = stacked_ref[size : size + 1, :]
    whitened = jnp.sum(lower_inverse * projected_row, axis=1, keepdims=True)
    mean_weights = jnp.sum(lower_inverse * whitened, axis=0, keepdims=True)
    combination_ref[...] = lower_inverse + mean_weights


def combination_transposed_of(stacked):
    size = stacked.shape[1]
    return pl.pallas_call(
        combination_kernel,
        out_shape=jax.ShapeDtypeStruct((size, size), jnp.float32),
        in_specs=[pl.BlockSpec(memory_space=pltpu.VMEM)],
        out_specs=pl.BlockSpec(memory_space=pltpu.VMEM),
        scratch_shapes=[pltpu.VMEM((size, size), jnp.float32)] * 2,
    )(stacked)

def propagate_model(padded_field, source_term):
    laplacian = (
        padded_field[:, 2:, 1:-1]
        + padded_field[:, :-2, 1:-1]
        + padded_field[:, 1:-1, 2:]
        + padded_field[:, 1:-1, :-2]
        - 4.0 * padded_field[:, 1:-1, 1:-1]
    )
    return padded_field[:, 1:-1, 1:-1] + diffusion * laplacian + heating * source_term


def propagate_members_last(padded_field, source_term):
    laplacian = (
        padded_field[1:-1, 2:]
        + padded_field[1:-1, :-2]
        + padded_field[2:, 1:-1]
        + padded_field[:-2, 1:-1]
        - 4.0 * padded_field[1:-1, 1:-1]
    )
    return padded_field[1:-1, 1:-1] + diffusion * laplacian + heating * source_term


def from_neighbour(block, axis, step):
    count = lax.axis_size(axis)
    if step > 0:
        pairs = [(i, i + 1) for i in range(count - 1)]
    else:
        pairs = [(i + 1, i) for i in range(count - 1)]
    return lax.ppermute(block, axis, pairs)


def forecast_in_pieces(warmth, heat):
    width, height = warmth.shape[0], warmth.shape[1]
    left = from_neighbour(jnp.concatenate([warmth[-2:], heat[-1:]], axis=0), "gy", 1)
    right = from_neighbour(jnp.concatenate([warmth[:2], heat[:1]], axis=0), "gy", -1)
    warmth_wide = jnp.concatenate([left[:2], warmth, right[:2]], axis=0)
    heat_wide = jnp.concatenate([left[2:], heat, right[2:]], axis=0)
    edge = jnp.zeros_like(heat_wide[:1, :1])
    top = from_neighbour(
        jnp.concatenate(
            [warmth_wide[:, -2:], jnp.concatenate([edge, heat_wide[:, -1:], edge], axis=0)],
            axis=1,
        ),
        "gx",
        1,
    )
    bottom = from_neighbour(
        jnp.concatenate(
            [warmth_wide[:, :2], jnp.concatenate([edge, heat_wide[:, :1], edge], axis=0)],
            axis=1,
        ),
        "gx",
        -1,
    )
    at_x, at_y = lax.axis_index("gx"), lax.axis_index("gy")
    col = lax.broadcasted_iota(jnp.int32, (width + 2, 1, 1), 0)
    off_grid = ((col == 0) & (at_y == 0)) | (
        (col == width + 1) & (at_y == lax.axis_size("gy") - 1)
    )
    first_inner = jnp.where(
        off_grid, 0.0, propagate_members_last(warmth_wide, heat_wide[:, 1:-1])
    )
    second_inner = propagate_members_last(first_inner, heat[:, 2:-2])
    first_top = propagate_members_last(
        jnp.concatenate([top[:, :2], warmth_wide[:, :2]], axis=1),
        jnp.concatenate([top[1:-1, 2:], heat_wide[:, :1]], axis=1),
    )
    first_bottom = propagate_members_last(
        jnp.concatenate([warmth_wide[:, -2:], bottom[:, :2]], axis=1),
        jnp.concatenate([heat_wide[:, -1:], bottom[1:-1, 2:]], axis=1),
    )
    row = lax.broadcasted_iota(jnp.int32, (1, 2, 1), 1)
    first_top = jnp.where(off_grid | ((row == 0) & (at_x == 0)), 0.0, first_top)
    first_bottom = jnp.where(
        off_grid | ((row == 1) & (at_x == lax.axis_size("gx") - 1)), 0.0, first_bottom
    )
    second_top = propagate_members_last(
        jnp.concatenate([first_top, first_inner[:, :2]], axis=1), heat[:, :2]
    )
    second_bottom = propagate_members_last(
        jnp.concatenate([first_inner[:, -2:], first_bottom], axis=1), heat[:, -2:]
    )
    return [(0, second_top), (2, second_inner), (height - 2, second_bottom)]


def shards(
    prior_gas_warmth,
    fire_power_output,
    measured_warmth,
    reading_noise_spread,
    reading_local_location,
):
    sample_number, block_height_number, block_width_number = prior_gas_warmth.shape
    warmth_t = jnp.transpose(prior_gas_warmth, (2, 1, 0))
    heat_t = jnp.transpose(fire_power_output, (2, 1, 0))
    pieces = forecast_in_pieces(warmth_t, heat_t)
    mean_heat_t = jnp.mean(heat_t, axis=2)
    heat_anomaly_t = heat_t - mean_heat_t[:, :, None]
    coefficient_line = 1.0 / (reading_noise_spread * math.sqrt(sample_number - 1))
    weight_line = coefficient_line * coefficient_line
    row_hot = (
        (reading_local_location // block_width_number)[:, None]
        == lax.broadcasted_iota(jnp.int32, (1, block_height_number), 1)
    ).astype(jnp.float32)
    col_hot = (
        (reading_local_location % block_width_number)[:, None]
        == lax.broadcasted_iota(jnp.int32, (1, block_width_number), 1)
    ).astype(jnp.float32)
    weighted_rows = jnp.concatenate(
        [row_hot * weight_line[:, None], row_hot * (weight_line * measured_warmth)[:, None]],
        axis=1,
    )
    cell_sums = lax.dot_general(
        col_hot, weighted_rows, (((0,), (0,)), ((), ())), precision=lax.Precision.HIGHEST
    )
    averages, deviations, gram_local, projected = [], [], 0.0, 0.0
    for start, piece in pieces:
        count = piece.shape[1]
        average = jnp.mean(piece, axis=2)
        deviation = piece - average[:, :, None]
        cell_weight = cell_sums[:, start : start + count]
        cell_residual = (
            cell_sums[:, block_height_number + start : block_height_number + start + count]
            - average * cell_weight
        )
        gram_local = gram_local + lax.dot_general(
            deviation * cell_weight[:, :, None],
            deviation,
            (((0, 1), (0, 1)), ((), ())),
            precision=lax.Precision.HIGHEST,
        )
        projected = projected + lax.dot_general(
            deviation,
            cell_residual,
            (((0, 1), (0, 1)), ((), ())),
            precision=lax.Precision.HIGHEST,
        )
        averages.append(average)
        deviations.append(deviation)
    average_t = jnp.concatenate(averages, axis=1)
    deviation_t = lax.optimization_barrier(jnp.concatenate(deviations, axis=1))
    combination_transposed = combination_transposed_of(
        butterfly_sum(jnp.concatenate([gram_local, projected[None, :]], axis=0), ("gx", "gy"))
    )
    contract = (((2,), (1,)), ((), ()))
    updated_t = average_t[:, :, None] + lax.dot_general(
        deviation_t, combination_transposed, contract, precision=lax.Precision.HIGHEST
    )
    heat_out_t = mean_heat_t[:, :, None] + lax.dot_general(
        heat_anomaly_t, combination_transposed, contract, precision=lax.Precision.HIGHEST
    )
    return (jnp.transpose(updated_t, (2, 1, 0)), jnp.transpose(heat_out_t, (2, 1, 0)))


def solution(mesh):
    placed = (
        P(None, "gx", "gy"),
        P(None, "gx", "gy"),
        P(("gx", "gy")),
        P(("gx", "gy")),
        P(("gx", "gy")),
    )
    return jax.shard_map(
        shards,
        mesh=mesh,
        in_specs=placed,
        out_specs=(P(None, "gx", "gy"), P(None, "gx", "gy")),
        check_vma=False,
    )
```

```python
import math

import jax
import jax.numpy as jnp
from jax import lax
from jax.experimental import pallas as pl
from jax.experimental.pallas import tpu as pltpu
from jax.sharding import PartitionSpec as P

diffusion = 0.2
heating = 0.5


def xor_tree(received, base, strides):
    if not strides:
        return received[base]
    return xor_tree(received, base, strides[:-1]) + xor_tree(
        received, base ^ strides[-1], strides[:-1]
    )


def butterfly_sum(value, axes):
    for axis in axes:
        count = lax.axis_size(axis)
        if count & (count - 1):
            value = lax.psum(value, axis)
            continue
        bits = [1 << b for b in range(count.bit_length() - 1)]
        for first in range(len(bits)):
            strides = bits[first : first + 1]
            received = {0: value}
            for mask in range(1, 1 << len(strides)):
                offset = 0
                for position, stride in enumerate(strides):
                    if mask >> position & 1:
                        offset ^= stride
                pairs = [(i, i ^ offset) for i in range(count)]
                received[offset] = lax.ppermute(value, axis, pairs)
            value = xor_tree(received, 0, strides)
    return value


def combination_kernel(stacked_ref, combination_ref, work_ref, inverse_ref):
    size = stacked_ref.shape[1]
    square_row = lax.broadcasted_iota(jnp.int32, (size, size), 0)
    square_col = lax.broadcasted_iota(jnp.int32, (size, size), 1)
    unit = jnp.where(square_row == square_col, 1.0, 0.0).astype(jnp.float32)
    work_ref[...] = stacked_ref[:size, :] + unit
    inverse_ref[...] = unit
    lane = lax.broadcasted_iota(jnp.int32, (1, size), 1)

    def pick(vector, where_true, axis):
        return jnp.sum(jnp.where(where_true, vector, 0.0), axis=axis, keepdims=True)

    for first in range(0, size, 8):
        span = size - first
        sublane = lax.broadcasted_iota(jnp.int32, (span, 1), 0) + first
        band_col = lax.broadcasted_iota(jnp.int32, (span, size), 1)

        def step(pair, carry, first=first, sublane=sublane, band_col=band_col):
            k = 2 * pair
            row0 = work_ref[pl.ds(k, 1), :]
            row1 = work_ref[pl.ds(k + 1, 1), :]
            band = work_ref[first:, :]
            col0 = pick(band, band_col == k, 1)
            col1 = pick(band, band_col == k + 1, 1)
            scale0 = 1.0 / jnp.sqrt(pick(row0, lane == k, 1))
            coupling = pick(row0, lane == k + 1, 1) * scale0
            scale1 = 1.0 / jnp.sqrt(pick(row1, lane == k + 1, 1) - coupling * coupling)
            factor_row0 = jnp.where(lane >= k, row0 * scale0, 0.0)
            factor_row1 = jnp.where(lane >= k + 1, (row1 - coupling * factor_row0) * scale1, 0.0)
            factor_col0 = jnp.where(sublane >= k, col0 * scale0, 0.0)
            factor_col1 = jnp.where(
                sublane >= k + 1, (col1 - factor_col0 * coupling) * scale1, 0.0
            )
            work_ref[first:, :] = band - factor_col0 * factor_row0 - factor_col1 * factor_row1
            inverse_row0 = inverse_ref[pl.ds(k, 1), :] * scale0
            inverse_row1 = (inverse_ref[pl.ds(k + 1, 1), :] - coupling * inverse_row0) * scale1
            below0 = jnp.where(sublane > k + 1, factor_col0, 0.0)
            below1 = jnp.where(sublane > k + 1, factor_col1, 0.0)
            inverse_ref[first:, :] = (
                inverse_ref[first:, :] - below0 * inverse_row0 - below1 * inverse_row1
            )
            inverse_ref[pl.ds(k, 1), :] = inverse_row0
            inverse_ref[pl.ds(k + 1, 1), :] = inverse_row1
            return carry

        lax.fori_loop(first // 2, min(first + 8, size) // 2, step, 0)
    lower_inverse = inverse_ref[...]
    projected_row = stacked_ref[size : size + 1, :]
    whitened = jnp.sum(lower_inverse * projected_row, axis=1, keepdims=True)
    mean_weights = jnp.sum(lower_inverse * whitened, axis=0, keepdims=True)
    combination_ref[...] = lower_inverse + mean_weights


def combination_transposed_of(stacked):
    size = stacked.shape[1]
    return pl.pallas_call(
        combination_kernel,
        out_shape=jax.ShapeDtypeStruct((size, size), jnp.float32),
        in_specs=[pl.BlockSpec(memory_space=pltpu.VMEM)],
        out_specs=pl.BlockSpec(memory_space=pltpu.VMEM),
        scratch_shapes=[pltpu.VMEM((size, size), jnp.float32)] * 2,
    )(stacked)

def propagate_model(padded_field, source_term):
    laplacian = (
        padded_field[:, 2:, 1:-1]
        + padded_field[:, :-2, 1:-1]
        + padded_field[:, 1:-1, 2:]
        + padded_field[:, 1:-1, :-2]
        - 4.0 * padded_field[:, 1:-1, 1:-1]
    )
    return padded_field[:, 1:-1, 1:-1] + diffusion * laplacian + heating * source_term


def propagate_members_last(padded_field, source_term):
    laplacian = (
        padded_field[1:-1, 2:]
        + padded_field[1:-1, :-2]
        + padded_field[2:, 1:-1]
        + padded_field[:-2, 1:-1]
        - 4.0 * padded_field[1:-1, 1:-1]
    )
    return padded_field[1:-1, 1:-1] + diffusion * laplacian + heating * source_term


def from_neighbour(block, axis, step):
    count = lax.axis_size(axis)
    if step > 0:
        pairs = [(i, i + 1) for i in range(count - 1)]
    else:
        pairs = [(i + 1, i) for i in range(count - 1)]
    return lax.ppermute(block, axis, pairs)


def forecast_in_pieces(warmth, heat):
    width, height = warmth.shape[0], warmth.shape[1]
    left = from_neighbour(jnp.concatenate([warmth[-2:], heat[-1:]], axis=0), "gy", 1)
    right = from_neighbour(jnp.concatenate([warmth[:2], heat[:1]], axis=0), "gy", -1)
    warmth_wide = jnp.concatenate([left[:2], warmth, right[:2]], axis=0)
    heat_wide = jnp.concatenate([left[2:], heat, right[2:]], axis=0)
    edge = jnp.zeros_like(heat_wide[:1, :1])
    top = from_neighbour(
        jnp.concatenate(
            [warmth_wide[:, -2:], jnp.concatenate([edge, heat_wide[:, -1:], edge], axis=0)],
            axis=1,
        ),
        "gx",
        1,
    )
    bottom = from_neighbour(
        jnp.concatenate(
            [warmth_wide[:, :2], jnp.concatenate([edge, heat_wide[:, :1], edge], axis=0)],
            axis=1,
        ),
        "gx",
        -1,
    )
    at_x, at_y = lax.axis_index("gx"), lax.axis_index("gy")
    col = lax.broadcasted_iota(jnp.int32, (width + 2, 1, 1), 0)
    off_grid = ((col == 0) & (at_y == 0)) | (
        (col == width + 1) & (at_y == lax.axis_size("gy") - 1)
    )
    first_inner = jnp.where(
        off_grid, 0.0, propagate_members_last(warmth_wide, heat_wide[:, 1:-1])
    )
    second_inner = propagate_members_last(first_inner, heat[:, 2:-2])
    first_top = propagate_members_last(
        jnp.concatenate([top[:, :2], warmth_wide[:, :2]], axis=1),
        jnp.concatenate([top[1:-1, 2:], heat_wide[:, :1]], axis=1),
    )
    first_bottom = propagate_members_last(
        jnp.concatenate([warmth_wide[:, -2:], bottom[:, :2]], axis=1),
        jnp.concatenate([heat_wide[:, -1:], bottom[1:-1, 2:]], axis=1),
    )
    row = lax.broadcasted_iota(jnp.int32, (1, 2, 1), 1)
    first_top = jnp.where(off_grid | ((row == 0) & (at_x == 0)), 0.0, first_top)
    first_bottom = jnp.where(
        off_grid | ((row == 1) & (at_x == lax.axis_size("gx") - 1)), 0.0, first_bottom
    )
    second_top = propagate_members_last(
        jnp.concatenate([first_top, first_inner[:, :2]], axis=1), heat[:, :2]
    )
    second_bottom = propagate_members_last(
        jnp.concatenate([first_inner[:, -2:], first_bottom], axis=1), heat[:, -2:]
    )
    return [(0, second_top), (2, second_inner), (height - 2, second_bottom)]


def shards(
    prior_gas_warmth,
    fire_power_output,
    measured_warmth,
    reading_noise_spread,
    reading_local_location,
):
    sample_number, block_height_number, block_width_number = prior_gas_warmth.shape
    warmth_t = jnp.transpose(prior_gas_warmth, (2, 1, 0))
    heat_t = jnp.transpose(fire_power_output, (2, 1, 0))
    pieces = forecast_in_pieces(warmth_t, heat_t)
    mean_heat_t = jnp.mean(heat_t, axis=2)
    heat_anomaly_t = heat_t - mean_heat_t[:, :, None]
    coefficient_line = 1.0 / (reading_noise_spread * math.sqrt(sample_number - 1))
    weight_line = coefficient_line * coefficient_line
    row_hot = (
        (reading_local_location // block_width_number)[:, None]
        == lax.broadcasted_iota(jnp.int32, (1, block_height_number), 1)
    ).astype(jnp.float32)
    col_hot = (
        (reading_local_location % block_width_number)[:, None]
        == lax.broadcasted_iota(jnp.int32, (1, block_width_number), 1)
    ).astype(jnp.float32)
    weighted_rows = jnp.concatenate(
        [row_hot * weight_line[:, None], row_hot * (weight_line * measured_warmth)[:, None]],
        axis=1,
    )
    cell_sums = lax.dot_general(
        col_hot, weighted_rows, (((0,), (0,)), ((), ())), precision=lax.Precision.HIGHEST
    )
    averages, deviations, gram_local, projected = [], [], 0.0, 0.0
    for start, piece in pieces:
        count = piece.shape[1]
        average = jnp.mean(piece, axis=2)
        deviation = piece - average[:, :, None]
        cell_weight = cell_sums[:, start : start + count]
        cell_residual = (
            cell_sums[:, block_height_number + start : block_height_number + start + count]
            - average * cell_weight
        )
        gram_local = gram_local + lax.dot_general(
            deviation * cell_weight[:, :, None],
            deviation,
            (((0, 1), (0, 1)), ((), ())),
            precision=lax.Precision.HIGHEST,
        )
        projected = projected + lax.dot_general(
            deviation,
            cell_residual,
            (((0, 1), (0, 1)), ((), ())),
            precision=lax.Precision.HIGHEST,
        )
        averages.append(average)
        deviations.append(deviation)
    combination_transposed = combination_transposed_of(
        butterfly_sum(jnp.concatenate([gram_local, projected[None, :]], axis=0), ("gx", "gy"))
    )
    contract = (((2,), (1,)), ((), ()))
    updated_t = jnp.concatenate(
        [
            average[:, :, None]
            + lax.dot_general(
                deviation, combination_transposed, contract, precision=lax.Precision.HIGHEST
            )
            for average, deviation in zip(averages, deviations)
        ],
        axis=1,
    )
    heat_out_t = mean_heat_t[:, :, None] + lax.dot_general(
        heat_anomaly_t, combination_transposed, contract, precision=lax.Precision.HIGHEST
    )
    return (jnp.transpose(updated_t, (2, 1, 0)), jnp.transpose(heat_out_t, (2, 1, 0)))


def solution(mesh):
    placed = (
        P(None, "gx", "gy"),
        P(None, "gx", "gy"),
        P(("gx", "gy")),
        P(("gx", "gy")),
        P(("gx", "gy")),
    )
    return jax.shard_map(
        shards,
        mesh=mesh,
        in_specs=placed,
        out_specs=(P(None, "gx", "gy"), P(None, "gx", "gy")),
        check_vma=False,
    )
```

```python
import math

import jax
import jax.numpy as jnp
from jax import lax
from jax.experimental import pallas as pl
from jax.experimental.pallas import tpu as pltpu
from jax.sharding import PartitionSpec as P

diffusion = 0.2
heating = 0.5


def xor_tree(received, base, strides):
    if not strides:
        return received[base]
    return xor_tree(received, base, strides[:-1]) + xor_tree(
        received, base ^ strides[-1], strides[:-1]
    )


def butterfly_sum(value, axes):
    for axis in axes:
        count = lax.axis_size(axis)
        if count & (count - 1):
            value = lax.psum(value, axis)
            continue
        bits = [1 << b for b in range(count.bit_length() - 1)]
        for first in range(len(bits)):
            strides = bits[first : first + 1]
            received = {0: value}
            for mask in range(1, 1 << len(strides)):
                offset = 0
                for position, stride in enumerate(strides):
                    if mask >> position & 1:
                        offset ^= stride
                pairs = [(i, i ^ offset) for i in range(count)]
                received[offset] = lax.ppermute(value, axis, pairs)
            value = xor_tree(received, 0, strides)
    return value


def combination_kernel(stacked_ref, combination_ref, work_ref, inverse_ref):
    size = stacked_ref.shape[1]
    square_row = lax.broadcasted_iota(jnp.int32, (size, size), 0)
    square_col = lax.broadcasted_iota(jnp.int32, (size, size), 1)
    unit = jnp.where(square_row == square_col, 1.0, 0.0).astype(jnp.float32)
    work_ref[...] = stacked_ref[:size, :] + unit
    inverse_ref[...] = unit
    lane = lax.broadcasted_iota(jnp.int32, (1, size), 1)

    def pick(vector, where_true, axis):
        return jnp.sum(jnp.where(where_true, vector, 0.0), axis=axis, keepdims=True)

    for first in range(0, size, 8):
        span = size - first
        sublane = lax.broadcasted_iota(jnp.int32, (span, 1), 0) + first
        band_col = lax.broadcasted_iota(jnp.int32, (span, size), 1)

        def step(pair, carry, first=first, sublane=sublane, band_col=band_col):
            k = 2 * pair
            row0 = work_ref[pl.ds(k, 1), :]
            row1 = work_ref[pl.ds(k + 1, 1), :]
            band = work_ref[first:, :]
            col0 = pick(band, band_col == k, 1)
            col1 = pick(band, band_col == k + 1, 1)
            scale0 = 1.0 / jnp.sqrt(pick(row0, lane == k, 1))
            coupling = pick(row0, lane == k + 1, 1) * scale0
            scale1 = 1.0 / jnp.sqrt(pick(row1, lane == k + 1, 1) - coupling * coupling)
            factor_row0 = jnp.where(lane >= k, row0 * scale0, 0.0)
            factor_row1 = jnp.where(lane >= k + 1, (row1 - coupling * factor_row0) * scale1, 0.0)
            factor_col0 = jnp.where(sublane >= k, col0 * scale0, 0.0)
            factor_col1 = jnp.where(
                sublane >= k + 1, (col1 - factor_col0 * coupling) * scale1, 0.0
            )
            work_ref[first:, :] = band - factor_col0 * factor_row0 - factor_col1 * factor_row1
            inverse_row0 = inverse_ref[pl.ds(k, 1), :] * scale0
            inverse_row1 = (inverse_ref[pl.ds(k + 1, 1), :] - coupling * inverse_row0) * scale1
            inverse_ref[first:, :] = (
                inverse_ref[first:, :] - factor_col0 * inverse_row0 - factor_col1 * inverse_row1
            )
            inverse_ref[pl.ds(k, 1), :] = inverse_row0
            inverse_ref[pl.ds(k + 1, 1), :] = inverse_row1
            return carry

        lax.fori_loop(first // 2, min(first + 8, size) // 2, step, 0)
    lower_inverse = inverse_ref[...]
    projected_row = stacked_ref[size : size + 1, :]
    whitened = jnp.sum(lower_inverse * projected_row, axis=1, keepdims=True)
    mean_weights = jnp.sum(lower_inverse * whitened, axis=0, keepdims=True)
    combination_ref[...] = lower_inverse + mean_weights


def combination_transposed_of(stacked):
    size = stacked.shape[1]
    return pl.pallas_call(
        combination_kernel,
        out_shape=jax.ShapeDtypeStruct((size, size), jnp.float32),
        in_specs=[pl.BlockSpec(memory_space=pltpu.VMEM)],
        out_specs=pl.BlockSpec(memory_space=pltpu.VMEM),
        scratch_shapes=[pltpu.VMEM((size, size), jnp.float32)] * 2,
    )(stacked)

def propagate_model(padded_field, source_term):
    laplacian = (
        padded_field[:, 2:, 1:-1]
        + padded_field[:, :-2, 1:-1]
        + padded_field[:, 1:-1, 2:]
        + padded_field[:, 1:-1, :-2]
        - 4.0 * padded_field[:, 1:-1, 1:-1]
    )
    return padded_field[:, 1:-1, 1:-1] + diffusion * laplacian + heating * source_term


def propagate_members_last(padded_field, source_term):
    laplacian = (
        padded_field[1:-1, 2:]
        + padded_field[1:-1, :-2]
        + padded_field[2:, 1:-1]
        + padded_field[:-2, 1:-1]
        - 4.0 * padded_field[1:-1, 1:-1]
    )
    return padded_field[1:-1, 1:-1] + diffusion * laplacian + heating * source_term


def from_neighbour(block, axis, step):
    count = lax.axis_size(axis)
    if step > 0:
        pairs = [(i, i + 1) for i in range(count - 1)]
    else:
        pairs = [(i + 1, i) for i in range(count - 1)]
    return lax.ppermute(block, axis, pairs)


def forecast_in_pieces(warmth, heat):
    width, height = warmth.shape[0], warmth.shape[1]
    left = from_neighbour(jnp.concatenate([warmth[-2:], heat[-1:]], axis=0), "gy", 1)
    right = from_neighbour(jnp.concatenate([warmth[:2], heat[:1]], axis=0), "gy", -1)
    warmth_wide = jnp.concatenate([left[:2], warmth, right[:2]], axis=0)
    heat_wide = jnp.concatenate([left[2:], heat, right[2:]], axis=0)
    edge = jnp.zeros_like(heat_wide[:1, :1])
    top = from_neighbour(
        jnp.concatenate(
            [warmth_wide[:, -2:], jnp.concatenate([edge, heat_wide[:, -1:], edge], axis=0)],
            axis=1,
        ),
        "gx",
        1,
    )
    bottom = from_neighbour(
        jnp.concatenate(
            [warmth_wide[:, :2], jnp.concatenate([edge, heat_wide[:, :1], edge], axis=0)],
            axis=1,
        ),
        "gx",
        -1,
    )
    at_x, at_y = lax.axis_index("gx"), lax.axis_index("gy")
    col = lax.broadcasted_iota(jnp.int32, (width + 2, 1, 1), 0)
    off_grid = ((col == 0) & (at_y == 0)) | (
        (col == width + 1) & (at_y == lax.axis_size("gy") - 1)
    )
    first_inner = jnp.where(
        off_grid, 0.0, propagate_members_last(warmth_wide, heat_wide[:, 1:-1])
    )
    second_inner = propagate_members_last(first_inner, heat[:, 2:-2])
    first_top = propagate_members_last(
        jnp.concatenate([top[:, :2], warmth_wide[:, :2]], axis=1),
        jnp.concatenate([top[1:-1, 2:], heat_wide[:, :1]], axis=1),
    )
    first_bottom = propagate_members_last(
        jnp.concatenate([warmth_wide[:, -2:], bottom[:, :2]], axis=1),
        jnp.concatenate([heat_wide[:, -1:], bottom[1:-1, 2:]], axis=1),
    )
    row = lax.broadcasted_iota(jnp.int32, (1, 2, 1), 1)
    first_top = jnp.where(off_grid | ((row == 0) & (at_x == 0)), 0.0, first_top)
    first_bottom = jnp.where(
        off_grid | ((row == 1) & (at_x == lax.axis_size("gx") - 1)), 0.0, first_bottom
    )
    second_top = propagate_members_last(
        jnp.concatenate([first_top, first_inner[:, :2]], axis=1), heat[:, :2]
    )
    second_bottom = propagate_members_last(
        jnp.concatenate([first_inner[:, -2:], first_bottom], axis=1), heat[:, -2:]
    )
    return [(0, second_top), (2, second_inner), (height - 2, second_bottom)]


def shards(
    prior_gas_warmth,
    fire_power_output,
    measured_warmth,
    reading_noise_spread,
    reading_local_location,
):
    sample_number, block_height_number, block_width_number = prior_gas_warmth.shape
    warmth_t = jnp.transpose(prior_gas_warmth, (2, 1, 0))
    heat_t = jnp.transpose(fire_power_output, (2, 1, 0))
    pieces = forecast_in_pieces(warmth_t, heat_t)
    mean_heat_t = jnp.mean(heat_t, axis=2)
    heat_anomaly_t = heat_t - mean_heat_t[:, :, None]
    coefficient_line = 1.0 / (reading_noise_spread * math.sqrt(sample_number - 1))
    weight_line = coefficient_line * coefficient_line
    row_hot = (
        (reading_local_location // block_width_number)[:, None]
        == lax.broadcasted_iota(jnp.int32, (1, block_height_number), 1)
    ).astype(jnp.float32)
    col_hot = (
        (reading_local_location % block_width_number)[:, None]
        == lax.broadcasted_iota(jnp.int32, (1, block_width_number), 1)
    ).astype(jnp.float32)
    weighted_rows = jnp.concatenate(
        [row_hot * weight_line[:, None], row_hot * (weight_line * measured_warmth)[:, None]],
        axis=1,
    )
    cell_sums = lax.dot_general(
        col_hot, weighted_rows, (((0,), (0,)), ((), ())), precision=lax.Precision.HIGHEST
    )
    averages, deviations, gram_local, projected = [], [], 0.0, 0.0
    for start, piece in pieces:
        count = piece.shape[1]
        average = jnp.mean(piece, axis=2)
        deviation = piece - average[:, :, None]
        cell_weight = cell_sums[:, start : start + count]
        cell_residual = (
            cell_sums[:, block_height_number + start : block_height_number + start + count]
            - average * cell_weight
        )
        gram_local = gram_local + lax.dot_general(
            deviation * cell_weight[:, :, None],
            deviation,
            (((0, 1), (0, 1)), ((), ())),
            precision=lax.Precision.HIGHEST,
        )
        projected = projected + lax.dot_general(
            deviation,
            cell_residual,
            (((0, 1), (0, 1)), ((), ())),
            precision=lax.Precision.HIGHEST,
        )
        averages.append(average)
        deviations.append(deviation)
    average_t = jnp.concatenate(averages, axis=1)
    deviation_t = jnp.concatenate(deviations, axis=1)
    combination_transposed = combination_transposed_of(
        butterfly_sum(jnp.concatenate([gram_local, projected[None, :]], axis=0), ("gx", "gy"))
    )
    contract = (((2,), (1,)), ((), ()))
    updated_t = average_t[:, :, None] + lax.dot_general(
        deviation_t, combination_transposed, contract, precision=lax.Precision.HIGHEST
    )
    heat_out_t = mean_heat_t[:, :, None] + lax.dot_general(
        heat_anomaly_t, combination_transposed, contract, precision=lax.Precision.HIGHEST
    )
    return (jnp.transpose(updated_t, (2, 1, 0)), jnp.transpose(heat_out_t, (2, 1, 0)))


def solution(mesh):
    placed = (
        P(None, "gx", "gy"),
        P(None, "gx", "gy"),
        P(("gx", "gy")),
        P(("gx", "gy")),
        P(("gx", "gy")),
    )
    return jax.shard_map(
        shards,
        mesh=mesh,
        in_specs=placed,
        out_specs=(P(None, "gx", "gy"), P(None, "gx", "gy")),
        check_vma=False,
    )
```

```python
import math

import jax
import jax.numpy as jnp
from jax import lax
from jax.experimental import pallas as pl
from jax.experimental.pallas import tpu as pltpu
from jax.sharding import PartitionSpec as P

diffusion = 0.2
heating = 0.5


def xor_tree(received, base, strides):
    if not strides:
        return received[base]
    return xor_tree(received, base, strides[:-1]) + xor_tree(
        received, base ^ strides[-1], strides[:-1]
    )


def butterfly_sum(value, axes):
    for axis in axes:
        count = lax.axis_size(axis)
        if count & (count - 1):
            value = lax.psum(value, axis)
            continue
        bits = [1 << b for b in range(count.bit_length() - 1)]
        for first in range(len(bits)):
            strides = bits[first : first + 1]
            received = {0: value}
            for mask in range(1, 1 << len(strides)):
                offset = 0
                for position, stride in enumerate(strides):
                    if mask >> position & 1:
                        offset ^= stride
                pairs = [(i, i ^ offset) for i in range(count)]
                received[offset] = lax.ppermute(value, axis, pairs)
            value = xor_tree(received, 0, strides)
    return value


def combination_kernel(stacked_ref, combination_ref, work_ref, inverse_ref):
    size = stacked_ref.shape[1]
    square_row = lax.broadcasted_iota(jnp.int32, (size, size), 0)
    square_col = lax.broadcasted_iota(jnp.int32, (size, size), 1)
    unit = jnp.where(square_row == square_col, 1.0, 0.0).astype(jnp.float32)
    work_ref[...] = stacked_ref[:size, :] + unit
    inverse_ref[...] = unit
    lane = lax.broadcasted_iota(jnp.int32, (1, size), 1)

    def pick(vector, where_true, axis):
        return jnp.sum(jnp.where(where_true, vector, 0.0), axis=axis, keepdims=True)

    for first in range(0, size, 8):
        span = size - first
        sublane = lax.broadcasted_iota(jnp.int32, (span, 1), 0) + first
        band_col = lax.broadcasted_iota(jnp.int32, (span, size), 1)

        def step(pair, carry, first=first, sublane=sublane, band_col=band_col):
            k = 2 * pair
            row0 = work_ref[pl.ds(k, 1), :]
            row1 = work_ref[pl.ds(k + 1, 1), :]
            band = work_ref[first:, :]
            col0 = pick(band, band_col == k, 1)
            col1 = pick(band, band_col == k + 1, 1)
            scale0 = 1.0 / jnp.sqrt(pick(row0, lane == k, 1))
            coupling = pick(row0, lane == k + 1, 1) * scale0
            scale1 = 1.0 / jnp.sqrt(pick(row1, lane == k + 1, 1) - coupling * coupling)
            factor_row0 = jnp.where(lane >= k, row0 * scale0, 0.0)
            factor_row1 = jnp.where(lane >= k + 1, (row1 - coupling * factor_row0) * scale1, 0.0)
            factor_col0 = jnp.where(sublane >= k, col0 * scale0, 0.0)
            factor_col1 = jnp.where(
                sublane >= k + 1, (col1 - factor_col0 * coupling) * scale1, 0.0
            )
            work_ref[first:, :] = band - factor_col0 * factor_row0 - factor_col1 * factor_row1
            inverse_row0 = inverse_ref[pl.ds(k, 1), :] * scale0
            inverse_row1 = (inverse_ref[pl.ds(k + 1, 1), :] - coupling * inverse_row0) * scale1
            below0 = jnp.where(sublane > k + 1, factor_col0, 0.0)
            below1 = jnp.where(sublane > k + 1, factor_col1, 0.0)
            inverse_ref[first:, :] = (
                inverse_ref[first:, :] - below0 * inverse_row0 - below1 * inverse_row1
            )
            inverse_ref[pl.ds(k, 1), :] = inverse_row0
            inverse_ref[pl.ds(k + 1, 1), :] = inverse_row1
            return carry

        lax.fori_loop(first // 2, min(first + 8, size) // 2, step, 0, unroll=True)
    lower_inverse = inverse_ref[...]
    projected_row = stacked_ref[size : size + 1, :]
    whitened = jnp.sum(lower_inverse * projected_row, axis=1, keepdims=True)
    mean_weights = jnp.sum(lower_inverse * whitened, axis=0, keepdims=True)
    combination_ref[...] = lower_inverse + mean_weights


def combination_transposed_of(stacked):
    size = stacked.shape[1]
    return pl.pallas_call(
        combination_kernel,
        out_shape=jax.ShapeDtypeStruct((size, size), jnp.float32),
        in_specs=[pl.BlockSpec(memory_space=pltpu.VMEM)],
        out_specs=pl.BlockSpec(memory_space=pltpu.VMEM),
        scratch_shapes=[pltpu.VMEM((size, size), jnp.float32)] * 2,
    )(stacked)

def propagate_model(padded_field, source_term):
    laplacian = (
        padded_field[:, 2:, 1:-1]
        + padded_field[:, :-2, 1:-1]
        + padded_field[:, 1:-1, 2:]
        + padded_field[:, 1:-1, :-2]
        - 4.0 * padded_field[:, 1:-1, 1:-1]
    )
    return padded_field[:, 1:-1, 1:-1] + diffusion * laplacian + heating * source_term


def propagate_members_last(padded_field, source_term):
    laplacian = (
        padded_field[1:-1, 2:]
        + padded_field[1:-1, :-2]
        + padded_field[2:, 1:-1]
        + padded_field[:-2, 1:-1]
        - 4.0 * padded_field[1:-1, 1:-1]
    )
    return padded_field[1:-1, 1:-1] + diffusion * laplacian + heating * source_term


def from_neighbour(block, axis, step):
    count = lax.axis_size(axis)
    if step > 0:
        pairs = [(i, i + 1) for i in range(count - 1)]
    else:
        pairs = [(i + 1, i) for i in range(count - 1)]
    return lax.ppermute(block, axis, pairs)


def forecast_in_pieces(warmth, heat):
    width, height = warmth.shape[0], warmth.shape[1]
    left = from_neighbour(jnp.concatenate([warmth[-2:], heat[-1:]], axis=0), "gy", 1)
    right = from_neighbour(jnp.concatenate([warmth[:2], heat[:1]], axis=0), "gy", -1)
    warmth_wide = jnp.concatenate([left[:2], warmth, right[:2]], axis=0)
    heat_wide = jnp.concatenate([left[2:], heat, right[2:]], axis=0)
    edge = jnp.zeros_like(heat_wide[:1, :1])
    top = from_neighbour(
        jnp.concatenate(
            [warmth_wide[:, -2:], jnp.concatenate([edge, heat_wide[:, -1:], edge], axis=0)],
            axis=1,
        ),
        "gx",
        1,
    )
    bottom = from_neighbour(
        jnp.concatenate(
            [warmth_wide[:, :2], jnp.concatenate([edge, heat_wide[:, :1], edge], axis=0)],
            axis=1,
        ),
        "gx",
        -1,
    )
    at_x, at_y = lax.axis_index("gx"), lax.axis_index("gy")
    col = lax.broadcasted_iota(jnp.int32, (width + 2, 1, 1), 0)
    off_grid = ((col == 0) & (at_y == 0)) | (
        (col == width + 1) & (at_y == lax.axis_size("gy") - 1)
    )
    first_inner = jnp.where(
        off_grid, 0.0, propagate_members_last(warmth_wide, heat_wide[:, 1:-1])
    )
    second_inner = propagate_members_last(first_inner, heat[:, 2:-2])
    first_top = propagate_members_last(
        jnp.concatenate([top[:, :2], warmth_wide[:, :2]], axis=1),
        jnp.concatenate([top[1:-1, 2:], heat_wide[:, :1]], axis=1),
    )
    first_bottom = propagate_members_last(
        jnp.concatenate([warmth_wide[:, -2:], bottom[:, :2]], axis=1),
        jnp.concatenate([heat_wide[:, -1:], bottom[1:-1, 2:]], axis=1),
    )
    row = lax.broadcasted_iota(jnp.int32, (1, 2, 1), 1)
    first_top = jnp.where(off_grid | ((row == 0) & (at_x == 0)), 0.0, first_top)
    first_bottom = jnp.where(
        off_grid | ((row == 1) & (at_x == lax.axis_size("gx") - 1)), 0.0, first_bottom
    )
    second_top = propagate_members_last(
        jnp.concatenate([first_top, first_inner[:, :2]], axis=1), heat[:, :2]
    )
    second_bottom = propagate_members_last(
        jnp.concatenate([first_inner[:, -2:], first_bottom], axis=1), heat[:, -2:]
    )
    return [(0, second_top), (2, second_inner), (height - 2, second_bottom)]


def shards(
    prior_gas_warmth,
    fire_power_output,
    measured_warmth,
    reading_noise_spread,
    reading_local_location,
):
    sample_number, block_height_number, block_width_number = prior_gas_warmth.shape
    warmth_t = jnp.transpose(prior_gas_warmth, (2, 1, 0))
    heat_t = jnp.transpose(fire_power_output, (2, 1, 0))
    pieces = forecast_in_pieces(warmth_t, heat_t)
    mean_heat_t = jnp.mean(heat_t, axis=2)
    heat_anomaly_t = heat_t - mean_heat_t[:, :, None]
    coefficient_line = 1.0 / (reading_noise_spread * math.sqrt(sample_number - 1))
    weight_line = coefficient_line * coefficient_line
    row_hot = (
        (reading_local_location // block_width_number)[:, None]
        == lax.broadcasted_iota(jnp.int32, (1, block_height_number), 1)
    ).astype(jnp.float32)
    col_hot = (
        (reading_local_location % block_width_number)[:, None]
        == lax.broadcasted_iota(jnp.int32, (1, block_width_number), 1)
    ).astype(jnp.float32)
    weighted_rows = jnp.concatenate(
        [row_hot * weight_line[:, None], row_hot * (weight_line * measured_warmth)[:, None]],
        axis=1,
    )
    cell_sums = lax.dot_general(
        col_hot, weighted_rows, (((0,), (0,)), ((), ())), precision=lax.Precision.HIGHEST
    )
    averages, deviations, gram_local, projected = [], [], 0.0, 0.0
    for start, piece in pieces:
        count = piece.shape[1]
        average = jnp.mean(piece, axis=2)
        deviation = piece - average[:, :, None]
        cell_weight = cell_sums[:, start : start + count]
        cell_residual = (
            cell_sums[:, block_height_number + start : block_height_number + start + count]
            - average * cell_weight
        )
        gram_local = gram_local + lax.dot_general(
            deviation * cell_weight[:, :, None],
            deviation,
            (((0, 1), (0, 1)), ((), ())),
            precision=lax.Precision.HIGHEST,
        )
        projected = projected + lax.dot_general(
            deviation,
            cell_residual,
            (((0, 1), (0, 1)), ((), ())),
            precision=lax.Precision.HIGHEST,
        )
        averages.append(average)
        deviations.append(deviation)
    average_t = jnp.concatenate(averages, axis=1)
    deviation_t = jnp.concatenate(deviations, axis=1)
    combination_transposed = combination_transposed_of(
        butterfly_sum(jnp.concatenate([gram_local, projected[None, :]], axis=0), ("gx", "gy"))
    )
    contract = (((2,), (1,)), ((), ()))
    updated_t = average_t[:, :, None] + lax.dot_general(
        deviation_t, combination_transposed, contract, precision=lax.Precision.HIGHEST
    )
    heat_out_t = mean_heat_t[:, :, None] + lax.dot_general(
        heat_anomaly_t, combination_transposed, contract, precision=lax.Precision.HIGHEST
    )
    return (jnp.transpose(updated_t, (2, 1, 0)), jnp.transpose(heat_out_t, (2, 1, 0)))


def solution(mesh):
    placed = (
        P(None, "gx", "gy"),
        P(None, "gx", "gy"),
        P(("gx", "gy")),
        P(("gx", "gy")),
        P(("gx", "gy")),
    )
    return jax.shard_map(
        shards,
        mesh=mesh,
        in_specs=placed,
        out_specs=(P(None, "gx", "gy"), P(None, "gx", "gy")),
        check_vma=False,
    )
```
